32 devices in a mesh: row: 2 (over core), col: 16 (over z, y, x).
Axes of the slice: x: 2, y: 2, z: 4, core: 2. Of those that a mesh axis runs over, the one named last changes fastest.
Arguments:
- features: bfloat16 [8192, 128], P(('row', 'col')), may hold values from -6 to 6
- tile_vals: bfloat16 [2, 16, 128, 128, 128], P('row', 'col'), may hold values from -0.15625 to 0.15625
- tile_rows: int32 [2, 16, 128], P('row', 'col'), may hold values from 0 to 31, as said below
- tile_cols: int32 [2, 16, 128], P('row', 'col'), may hold values from 0 to 3
- tile_count: int32 [2, 16], P('row', 'col'), may hold values from 16 to 128, as said below
- w_fwd: bfloat16 [128, 256], replicated, may hold values from -0.5 to 0.5
- w_bwd: bfloat16 [128, 256], replicated, may hold values from -0.5 to 0.5
Outputs:
- updated: bfloat16 [8192, 256], P(('row', 'col'))
The draws below stay inside these ranges and needn't reach their ends.
Inputs may be any that keep to these rules, and one draw needn't show every extreme that they name: Within one grid cell the pairs (tile_rows, tile_cols) of all slots are distinct. `tile_count`: some grid cell has all 128 slots live.
All inputs are finite; a program needn't handle non-finite values.
Results may differ from the reference program's by a relative error of at most 0.001.
Values may be sent and summed in bfloat16 or wider, within the bound.
No kernel may reach another device: no remote copies, remote signals or barrier semaphores. Data moves between devices by JAX's collectives and lax.ppermute only.
A program may use at most 128 MiB of HBM per device.

```python
import jax
import jax.numpy as jnp
from jax import lax

FEAT = 128
HID = 256
TILE = 128
NBC = 2
TILES = 128
GRID_R = 2
GRID_C = 16
NODES = 8192


def index_pairs(key):
    base = jax.random.fold_in(key, 11)
    keys = jax.random.split(base, GRID_R * GRID_C)
    total = NBC * GRID_C * NBC * GRID_R

    def single(one_key):
        return jax.random.permutation(one_key, total)[:TILES]
    picks = jax.vmap(single)(keys)
    return picks.reshape(GRID_R, GRID_C, TILES)


def draw_tile_rows(key, part):
    return (index_pairs(key) // (NBC * GRID_R)).astype(jnp.int32)


def draw_tile_cols(key, part):
    return (index_pairs(key) % (NBC * GRID_R)).astype(jnp.int32)


def draw_tile_count(key, part):
    raw = jax.random.randint(jax.random.fold_in(key, 23), (GRID_R * GRID_C,), 0, TILES)
    skewed = raw * raw // TILES * raw // TILES
    counts = jnp.maximum(TILES // 8, skewed)
    fullest = jax.random.randint(jax.random.fold_in(key, 29), (), 0, GRID_R * GRID_C)
    position = jnp.arange(GRID_R * GRID_C, dtype=jnp.int32)
    counts = jnp.where(position == fullest, TILES, counts)
    return counts.reshape(GRID_R, GRID_C).astype(jnp.int32)


def steps_of(key, shape, pieces, low, largest):
    def one(dim, parts):
        heights = jax.random.uniform(jax.random.fold_in(jax.random.fold_in(key, 6), dim), (parts,), jnp.float32, low / len(pieces), largest / len(pieces))
        return jnp.repeat(jnp.exp(heights), shape[dim] // parts).reshape((-1,) + (1,) * (len(shape) - dim - 1))

    gain = one(*pieces[0])
    for cut in pieces[1:]:
        gain = gain * one(*cut)
    return gain


def bell_draw(key, shape, width, limit, pieces=(), held_as=jnp.bfloat16):
    loudness = steps_of(key, shape, pieces, -0.22, 0.18) if pieces else 1.0
    drawn = jax.random.normal(key, shape, jnp.float32) * width * loudness
    return jnp.minimum(jnp.maximum(drawn, -limit), limit).astype(held_as)


def setup_inputs(seed: int = 0) -> dict:
    arg_keys = jax.random.split(jax.random.key(seed), 8)
    return {
        "features": bell_draw(arg_keys[0], (NODES, FEAT), 1.0, 6.0, ((0, 32),)),
        "tile_vals": bell_draw(arg_keys[1], (GRID_R, GRID_C, TILES, TILE, TILE), ((TILES * TILE // NBC) ** -0.5), 0.15625, ((0, 2), (1, 16))),
        "tile_rows": draw_tile_rows(jax.random.fold_in(arg_keys[7], 71), 0),
        "tile_cols": draw_tile_cols(jax.random.fold_in(arg_keys[7], 71), 0),
        "tile_count": draw_tile_count(jax.random.fold_in(arg_keys[7], 71), 0),
        "w_fwd": bell_draw(arg_keys[5], (FEAT, HID), FEAT ** -0.5, 0.5),
        "w_bwd": bell_draw(arg_keys[6], (FEAT, HID), FEAT ** -0.5, 0.5),
    }


def reference(features, tile_vals, tile_rows, tile_cols, tile_count, w_fwd, w_bwd):
    blocks = features.reshape(-1, TILE, FEAT)
    total_blocks = blocks.shape[0]
    slots = jnp.arange(TILES, dtype=jnp.int32)

    def cell(carry, index):
        along, against = carry
        rowid = index // GRID_C
        colid = index % GRID_C
        values = tile_vals[rowid, colid]
        rowblk = tile_rows[rowid, colid]
        colblk = tile_cols[rowid, colid]
        live = slots < tile_count[rowid, colid]
        values = jnp.where(live[:, None, None], values, jnp.zeros_like(values)).astype(jnp.float32)
        global_row = (rowid * GRID_C * NBC + rowblk).astype(jnp.int32)
        global_col = (((colblk // NBC) * GRID_C + colid) * NBC + colblk % NBC).astype(jnp.int32)
        source_col = blocks[global_col].astype(jnp.float32)
        source_row = blocks[global_row].astype(jnp.float32)
        fwd_terms = jnp.einsum("kab,kbf->kaf", values, source_col)
        bwd_terms = jnp.einsum("kba,kbf->kaf", values, source_row)
        along = along.at[global_row].add(fwd_terms)
        against = against.at[global_col].add(bwd_terms)
        return (along, against), None

    start = jnp.zeros((total_blocks, TILE, FEAT), jnp.float32)
    (along, against), _ = lax.scan(cell, (start, start), jnp.arange(GRID_R * GRID_C, dtype=jnp.int32))
    along = along.reshape(-1, FEAT)
    against = against.reshape(-1, FEAT)
    result = jnp.dot(along, w_fwd.astype(jnp.float32), precision=lax.Precision.HIGHEST)
    result = result + jnp.dot(against, w_bwd.astype(jnp.float32), precision=lax.Precision.HIGHEST)
    return result.astype(jnp.bfloat16)
```

```python
import jax
import jax.numpy as jnp
from jax import lax
from jax.sharding import PartitionSpec as P


def _nbits(n):
    bits = n.bit_length() - 1
    return bits if (1 << bits) == n else None


def _swap(x, axis, size, bit):
    perm = [(i, i ^ (1 << bit)) for i in range(size)]
    return lax.ppermute(x, axis, perm)


def gather_axis(x, axis):
    size = lax.axis_size(axis)
    nb = _nbits(size)
    if nb is None:
        return lax.all_gather(x, axis, axis=0, tiled=True)
    me = lax.axis_index(axis)
    have = x[None]
    order = list(range(nb - 1, -1, -1))
    for bit in order:
        got = _swap(have, axis, size, bit)
        mine = (me >> bit) & 1
        lo = jnp.where(mine == 0, have, got)
        hi = jnp.where(mine == 0, got, have)
        have = jnp.stack([lo, hi], axis=0).reshape((-1,) + have.shape[1:])
    shape = (2,) * nb + x.shape
    have = have.reshape(shape)
    processed = order[::-1]
    perm = [processed.index(b) for b in range(nb - 1, -1, -1)]
    have = jnp.transpose(have, perm + list(range(nb, nb + x.ndim)))
    return have.reshape((size * x.shape[0],) + x.shape[1:])


def scatter_sum_axis(x, axis):
    size = lax.axis_size(axis)
    nb = _nbits(size)
    if nb is None:
        return lax.psum_scatter(x, axis, scatter_dimension=0, tiled=True)
    me = lax.axis_index(axis)
    rest = x.shape[1:]
    data = x.reshape((2,) * nb + (x.shape[0] // size,) + rest)
    axes_bits = list(range(nb - 1, -1, -1))
    for bit in range(nb):
        a = axes_bits.index(bit)
        mine = (me >> bit) & 1
        keep = lax.dynamic_index_in_dim(data, mine, axis=a, keepdims=False)
        other = lax.dynamic_index_in_dim(data, 1 - mine, axis=a, keepdims=False)
        data = keep + _swap(other, axis, size, bit)
        axes_bits.pop(a)
    return data


def local(features, tile_vals, tile_rows, tile_cols, tile_count, w_fwd, w_bwd):
    row_size = lax.axis_size("row")
    col_size = lax.axis_size("col")
    values = tile_vals[0, 0]
    rowblk = tile_rows[0, 0]
    colblk = tile_cols[0, 0]
    slots = values.shape[0]
    side = values.shape[1]
    nodes_here = features.shape[0]
    nbc = nodes_here // side
    width = features.shape[1]
    nrow_blocks = col_size * nbc
    ncol_blocks = row_size * nbc
    cells = nrow_blocks * ncol_blocks

    slot_ids = jnp.arange(slots, dtype=jnp.int32)
    live = slot_ids < tile_count[0, 0]
    pos = jnp.where(live, rowblk * ncol_blocks + colblk, cells)
    inv = jnp.full((cells,), slots, jnp.int32).at[pos].set(slot_ids, mode="drop")
    present = inv < slots
    dense = values[jnp.minimum(inv, slots - 1)]
    dense = jnp.where(present[:, None, None], dense, jnp.zeros_like(dense))
    dense = dense.reshape(nrow_blocks, ncol_blocks, side, side)

    group = gather_axis(features, "row").reshape(ncol_blocks, side, width)
    stripe = gather_axis(features, "col").reshape(nrow_blocks, side, width)

    fwd_parts = jnp.einsum("bjak,jkf->baf", dense, group, preferred_element_type=jnp.float32)
    along = scatter_sum_axis(fwd_parts.reshape(-1, width), "col")
    bwd_parts = jnp.einsum("bjak,baf->jkf", dense, stripe, preferred_element_type=jnp.float32)
    against = scatter_sum_axis(bwd_parts.reshape(-1, width), "row")

    along = along.reshape(-1, width)
    against = against.reshape(-1, width)
    result = jnp.dot(along, w_fwd.astype(jnp.float32), precision=lax.Precision.HIGHEST)
    result = result + jnp.dot(against, w_bwd.astype(jnp.float32), precision=lax.Precision.HIGHEST)
    return result.astype(jnp.bfloat16)


def solution(mesh):
    in_specs = (
        P(("row", "col"), None),
        P("row", "col", None, None, None),
        P("row", "col", None),
        P("row", "col", None),
        P("row", "col"),
        P(),
        P(),
    )
    out_specs = P(("row", "col"), None)
    return jax.shard_map(local, mesh=mesh, in_specs=in_specs, out_specs=out_specs, check_vma=False)
```

```python
import jax
import jax.numpy as jnp
from jax import lax
from jax.experimental import pallas as pl
from jax.experimental.pallas import tpu as pltpu
from jax.sharding import PartitionSpec as P


def _nbits(n):
    bits = n.bit_length() - 1
    return bits if (1 << bits) == n else None


def _orders(nb):
    if nb == 4:
        return ((0, 1, 2, 3), (2, 0, 1, 3)), ((3, 0, 1, 2), (3, 2, 0, 1))
    rs = tuple(range(nb))
    return (rs, rs), (rs[::-1], rs[::-1])


def _pick(parity, pair, t):
    return jnp.where(parity == 0, pair[0][t], pair[1][t])


def _swap_col(x, row_size, col_size, bits):
    perm = []
    for r in range(row_size):
        b = bits[r % 2]
        for c in range(col_size):
            perm.append((r * col_size + c, r * col_size + (c ^ (1 << b))))
    return lax.ppermute(x, ("row", "col"), perm)


def _swap(x, axis, size, bit):
    perm = [(i, i ^ (1 << bit)) for i in range(size)]
    return lax.ppermute(x, axis, perm)


def gather_row(x):
    size = lax.axis_size("row")
    nb = _nbits(size)
    if nb is None:
        return lax.all_gather(x, "row", axis=0, tiled=True)
    me = lax.axis_index("row")
    have = x[None]
    order = list(range(nb - 1, -1, -1))
    for bit in order:
        got = _swap(have, "row", size, bit)
        mine = (me >> bit) & 1
        lo = jnp.where(mine == 0, have, got)
        hi = jnp.where(mine == 0, got, have)
        have = jnp.stack([lo, hi], axis=0).reshape((-1,) + have.shape[1:])
    have = have.reshape((2,) * nb + x.shape)
    processed = order[::-1]
    perm = [processed.index(b) for b in range(nb - 1, -1, -1)]
    have = jnp.transpose(have, perm + list(range(nb, nb + x.ndim)))
    return have.reshape((size * x.shape[0],) + x.shape[1:])


def scatter_sum_row(x):
    size = lax.axis_size("row")
    nb = _nbits(size)
    if nb is None:
        return lax.psum_scatter(x, "row", scatter_dimension=0, tiled=True)
    me = lax.axis_index("row")
    data = x.reshape((2,) * nb + (x.shape[0] // size,) + x.shape[1:])
    axes_bits = list(range(nb - 1, -1, -1))
    for bit in range(nb):
        a = axes_bits.index(bit)
        mine = (me >> bit) & 1
        keep = lax.dynamic_index_in_dim(data, mine, axis=a, keepdims=False)
        other = lax.dynamic_index_in_dim(data, 1 - mine, axis=a, keepdims=False)
        data = keep + _swap(other, "row", size, bit)
        axes_bits.pop(a)
    return data


def gather_col(x, order):
    row_size = lax.axis_size("row")
    col_size = lax.axis_size("col")
    nb = len(order[0])
    me = lax.axis_index("col")
    parity = lax.axis_index("row") % 2
    have = x[None]
    for t in range(nb):
        got = _swap_col(have, row_size, col_size, (order[0][t], order[1][t]))
        mine = (me >> _pick(parity, order, t)) & 1
        lo = jnp.where(mine == 0, have, got)
        hi = jnp.where(mine == 0, got, have)
        have = jnp.stack([lo, hi], axis=0).reshape((-1,) + have.shape[1:])
    return have


def scatter_sum_col(data, order):
    row_size = lax.axis_size("row")
    col_size = lax.axis_size("col")
    nb = len(order[0])
    me = lax.axis_index("col")
    parity = lax.axis_index("row") % 2
    for t in range(nb):
        mine = (me >> _pick(parity, order, t)) & 1
        keep = lax.dynamic_index_in_dim(data, mine, axis=0, keepdims=False)
        other = lax.dynamic_index_in_dim(data, 1 - mine, axis=0, keepdims=False)
        data = keep + _swap_col(other, row_size, col_size, (order[0][t], order[1][t]))
    return data


def _chunk(slots):
    return 16 if slots % 16 == 0 else slots


def along_call(rows, cols, cnt, values, group, nrb):
    slots, side, _ = values.shape
    width = group.shape[-1]
    k = _chunk(slots)

    def kernel(rows_ref, cols_ref, cnt_ref, vals_ref, grp_ref, out_ref):
        i = pl.program_id(0)
        n = cnt_ref[0]

        @pl.when(i == 0)
        def _():
            out_ref[...] = jnp.zeros(out_ref.shape, out_ref.dtype)

        def body(t, carry):
            s = i * k + t

            @pl.when(s < n)
            def _():
                r = rows_ref[s]
                c = cols_ref[s]
                out_ref[r] += jnp.dot(vals_ref[t], grp_ref[c], preferred_element_type=jnp.float32)

            return carry

        @pl.when(i * k < n)
        def _():
            lax.fori_loop(0, k, body, 0)

    def vals_map(i, rows_ref, cols_ref, cnt_ref):
        last = jnp.maximum(cnt_ref[0] - 1, 0) // k
        return (jnp.minimum(i, last), 0, 0)

    spec = pltpu.PrefetchScalarGridSpec(
        num_scalar_prefetch=3,
        grid=(slots // k,),
        in_specs=[
            pl.BlockSpec((k, side, side), vals_map),
            pl.BlockSpec(group.shape, lambda i, *_: (0, 0, 0)),
        ],
        out_specs=pl.BlockSpec((nrb, side, width), lambda i, *_: (0, 0, 0)),
    )
    return pl.pallas_call(
        kernel,
        grid_spec=spec,
        out_shape=jax.ShapeDtypeStruct((nrb, side, width), jnp.float32),
    )(rows, cols, cnt, values, group)


def against_call(rows, cols, cnt, values, stripe_t, ncb):
    slots, side, _ = values.shape
    width = stripe_t.shape[1]
    k = _chunk(slots)

    def kernel(rows_ref, cols_ref, cnt_ref, vals_ref, st_ref, out_ref):
        i = pl.program_id(0)
        n = cnt_ref[0]

        @pl.when(i == 0)
        def _():
            out_ref[...] = jnp.zeros(out_ref.shape, out_ref.dtype)

        def body(t, carry):
            s = i * k + t

            @pl.when(s < n)
            def _():
                r = rows_ref[s]
                c = cols_ref[s]
                out_ref[c] += jnp.dot(st_ref[r], vals_ref[t], preferred_element_type=jnp.float32)

            return carry

        @pl.when(i * k < n)
        def _():
            lax.fori_loop(0, k, body, 0)

    def vals_map(i, rows_ref, cols_ref, cnt_ref):
        last = jnp.maximum(cnt_ref[0] - 1, 0) // k
        return (jnp.minimum(i, last), 0, 0)

    spec = pltpu.PrefetchScalarGridSpec(
        num_scalar_prefetch=3,
        grid=(slots // k,),
        in_specs=[
            pl.BlockSpec((k, side, side), vals_map),
            pl.BlockSpec(stripe_t.shape, lambda i, *_: (0, 0, 0)),
        ],
        out_specs=pl.BlockSpec((ncb, width, side), lambda i, *_: (0, 0, 0)),
    )
    return pl.pallas_call(
        kernel,
        grid_spec=spec,
        out_shape=jax.ShapeDtypeStruct((ncb, width, side), jnp.float32),
    )(rows, cols, cnt, values, stripe_t)


def local(features, tile_vals, tile_rows, tile_cols, tile_count, w_fwd, w_bwd):
    row_size = lax.axis_size("row")
    col_size = lax.axis_size("col")
    values = tile_vals[0, 0]
    slots = values.shape[0]
    side = values.shape[1]
    nodes_here = features.shape[0]
    nbc = nodes_here // side
    width = features.shape[1]
    nrb = col_size * nbc
    ncb = row_size * nbc
    parity = lax.axis_index("row") % 2

    rowblk = jnp.clip(tile_rows[0, 0], 0, nrb - 1)
    colblk = jnp.clip(tile_cols[0, 0], 0, ncb - 1)
    cnt = jnp.clip(tile_count[0, 0], 0, slots).reshape(1).astype(jnp.int32)

    nb = _nbits(col_size)
    if nb is not None:
        rs_order, ag_order = _orders(nb)
        dest = rowblk // nbc
        sub = rowblk % nbc
        rs_pos = jnp.zeros_like(dest)
        ag_pos = jnp.zeros_like(dest)
        for t in range(nb):
            rs_pos = rs_pos + (((dest >> _pick(parity, rs_order, t)) & 1) << (nb - 1 - t))
            ag_pos = ag_pos + (((dest >> _pick(parity, ag_order, t)) & 1) << t)
        rows_fwd = rs_pos * nbc + sub
        rows_bwd = ag_pos * nbc + sub
    else:
        rows_fwd = rowblk
        rows_bwd = rowblk

    group = gather_row(features).reshape(ncb, side, width)
    fwd_parts = along_call(rows_fwd, colblk, cnt, values, group, nrb)

    mine_t = jnp.transpose(features.reshape(nbc, side, width), (0, 2, 1))
    if nb is not None:
        stripe_t = gather_col(mine_t, ag_order).reshape(nrb, width, side)
        along = scatter_sum_col(fwd_parts.reshape((2,) * nb + (nbc, side, width)), rs_order)
    else:
        stripe_t = lax.all_gather(mine_t, "col", axis=0, tiled=True)
        along = lax.psum_scatter(fwd_parts, "col", scatter_dimension=0, tiled=True)

    bwd_t = against_call(rows_bwd, colblk, cnt, values, stripe_t, ncb)
    against_t = scatter_sum_row(bwd_t)
    against = jnp.transpose(against_t, (0, 2, 1))

    along = along.reshape(-1, width)
    against = against.reshape(-1, width)
    result = jnp.dot(along, w_fwd.astype(jnp.float32), precision=lax.Precision.HIGHEST)
    result = result + jnp.dot(against, w_bwd.astype(jnp.float32), precision=lax.Precision.HIGHEST)
    return result.astype(jnp.bfloat16)


def solution(mesh):
    in_specs = (
        P(("row", "col"), None),
        P("row", "col", None, None, None),
        P("row", "col", None),
        P("row", "col", None),
        P("row", "col"),
        P(),
        P(),
    )
    out_specs = P(("row", "col"), None)
    return jax.shard_map(local, mesh=mesh, in_specs=in_specs, out_specs=out_specs, check_vma=False)
```

```python
import jax
import jax.numpy as jnp
from jax import lax
from jax.experimental import pallas as pl
from jax.experimental.pallas import tpu as pltpu
from jax.sharding import PartitionSpec as P


def _nbits(n):
    bits = n.bit_length() - 1
    return bits if (1 << bits) == n else None


def _orders(nb):
    if nb == 4:
        return ((0, 1, 2, 3), (2, 0, 1, 3)), ((3, 0, 1, 2), (3, 2, 0, 1))
    rs = tuple(range(nb))
    return (rs, rs), (rs[::-1], rs[::-1])


def _pick(parity, pair, t):
    return jnp.where(parity == 0, pair[0][t], pair[1][t])


def _swap_col(x, row_size, col_size, bits):
    perm = []
    for r in range(row_size):
        b = bits[r % 2]
        for c in range(col_size):
            perm.append((r * col_size + c, r * col_size + (c ^ (1 << b))))
    return lax.ppermute(x, ("row", "col"), perm)


def _swap(x, axis, size, bit):
    perm = [(i, i ^ (1 << bit)) for i in range(size)]
    return lax.ppermute(x, axis, perm)


def gather_row(x):
    size = lax.axis_size("row")
    nb = _nbits(size)
    if nb is None:
        return lax.all_gather(x, "row", axis=0, tiled=True)
    me = lax.axis_index("row")
    have = x[None]
    order = list(range(nb - 1, -1, -1))
    for bit in order:
        got = _swap(have, "row", size, bit)
        mine = (me >> bit) & 1
        lo = jnp.where(mine == 0, have, got)
        hi = jnp.where(mine == 0, got, have)
        have = jnp.stack([lo, hi], axis=0).reshape((-1,) + have.shape[1:])
    have = have.reshape((2,) * nb + x.shape)
    processed = order[::-1]
    perm = [processed.index(b) for b in range(nb - 1, -1, -1)]
    have = jnp.transpose(have, perm + list(range(nb, nb + x.ndim)))
    return have.reshape((size * x.shape[0],) + x.shape[1:])


def scatter_sum_row(x):
    size = lax.axis_size("row")
    nb = _nbits(size)
    if nb is None:
        return lax.psum_scatter(x, "row", scatter_dimension=0, tiled=True)
    me = lax.axis_index("row")
    data = x.reshape((2,) * nb + (x.shape[0] // size,) + x.shape[1:])
    axes_bits = list(range(nb - 1, -1, -1))
    for bit in range(nb):
        a = axes_bits.index(bit)
        mine = (me >> bit) & 1
        keep = lax.dynamic_index_in_dim(data, mine, axis=a, keepdims=False)
        other = lax.dynamic_index_in_dim(data, 1 - mine, axis=a, keepdims=False)
        data = keep + _swap(other, "row", size, bit)
        axes_bits.pop(a)
    return data


def gather_col(x, order):
    row_size = lax.axis_size("row")
    col_size = lax.axis_size("col")
    nb = len(order[0])
    me = lax.axis_index("col")
    parity = lax.axis_index("row") % 2
    have = x[None]
    for t in range(nb):
        got = _swap_col(have, row_size, col_size, (order[0][t], order[1][t]))
        mine = (me >> _pick(parity, order, t)) & 1
        lo = jnp.where(mine == 0, have, got)
        hi = jnp.where(mine == 0, got, have)
        have = jnp.stack([lo, hi], axis=0).reshape((-1,) + have.shape[1:])
    return have


def scatter_sum_col(data, order):
    row_size = lax.axis_size("row")
    col_size = lax.axis_size("col")
    nb = len(order[0])
    me = lax.axis_index("col")
    parity = lax.axis_index("row") % 2
    for t in range(nb):
        mine = (me >> _pick(parity, order, t)) & 1
        keep = lax.dynamic_index_in_dim(data, mine, axis=0, keepdims=False)
        other = lax.dynamic_index_in_dim(data, 1 - mine, axis=0, keepdims=False)
        data = keep + _swap_col(other, row_size, col_size, (order[0][t], order[1][t]))
    return data


def _chunk(slots):
    return 32 if slots % 32 == 0 else slots


def along_call(rows, cols, cnt, values, group, nrb):
    slots, side, _ = values.shape
    width = group.shape[-1]
    k = _chunk(slots)

    def kernel(rows_ref, cols_ref, cnt_ref, vals_ref, grp_ref, out_ref):
        i = pl.program_id(0)
        n = cnt_ref[0]

        @pl.when(i == 0)
        def _():
            out_ref[...] = jnp.zeros(out_ref.shape, out_ref.dtype)

        @pl.when(i * k < n)
        def _():
            for t in range(k):
                s = i * k + t
                tile = jnp.where(s < n, vals_ref[t], jnp.zeros((side, side), vals_ref.dtype))
                r = rows_ref[s]
                c = cols_ref[s]
                out_ref[r] += jnp.dot(tile, grp_ref[c], preferred_element_type=jnp.float32)

    def vals_map(i, rows_ref, cols_ref, cnt_ref):
        last = jnp.maximum(cnt_ref[0] - 1, 0) // k
        return (jnp.minimum(i, last), 0, 0)

    spec = pltpu.PrefetchScalarGridSpec(
        num_scalar_prefetch=3,
        grid=(slots // k,),
        in_specs=[
            pl.BlockSpec((k, side, side), vals_map),
            pl.BlockSpec(group.shape, lambda i, *_: (0, 0, 0)),
        ],
        out_specs=pl.BlockSpec((nrb, side, width), lambda i, *_: (0, 0, 0)),
    )
    return pl.pallas_call(
        kernel,
        grid_spec=spec,
        out_shape=jax.ShapeDtypeStruct((nrb, side, width), jnp.float32),
    )(rows, cols, cnt, values, group)


def against_call(rows, cols, cnt, values, stripe_t, ncb):
    slots, side, _ = values.shape
    width = stripe_t.shape[1]
    k = _chunk(slots)

    def kernel(rows_ref, cols_ref, cnt_ref, vals_ref, st_ref, out_ref):
        i = pl.program_id(0)
        n = cnt_ref[0]

        @pl.when(i == 0)
        def _():
            out_ref[...] = jnp.zeros(out_ref.shape, out_ref.dtype)

        @pl.when(i * k < n)
        def _():
            for t in range(k):
                s = i * k + t
                tile = jnp.where(s < n, vals_ref[t], jnp.zeros((side, side), vals_ref.dtype))
                r = rows_ref[s]
                c = cols_ref[s]
                out_ref[c] += jnp.dot(st_ref[r], tile, preferred_element_type=jnp.float32)

    def vals_map(i, rows_ref, cols_ref, cnt_ref):
        last = jnp.maximum(cnt_ref[0] - 1, 0) // k
        return (jnp.minimum(i, last), 0, 0)

    spec = pltpu.PrefetchScalarGridSpec(
        num_scalar_prefetch=3,
        grid=(slots // k,),
        in_specs=[
            pl.BlockSpec((k, side, side), vals_map),
            pl.BlockSpec(stripe_t.shape, lambda i, *_: (0, 0, 0)),
        ],
        out_specs=pl.BlockSpec((ncb, width, side), lambda i, *_: (0, 0, 0)),
    )
    return pl.pallas_call(
        kernel,
        grid_spec=spec,
        out_shape=jax.ShapeDtypeStruct((ncb, width, side), jnp.float32),
    )(rows, cols, cnt, values, stripe_t)


def local(features, tile_vals, tile_rows, tile_cols, tile_count, w_fwd, w_bwd):
    row_size = lax.axis_size("row")
    col_size = lax.axis_size("col")
    values = tile_vals[0, 0]
    slots = values.shape[0]
    side = values.shape[1]
    nodes_here = features.shape[0]
    nbc = nodes_here // side
    width = features.shape[1]
    nrb = col_size * nbc
    ncb = row_size * nbc
    parity = lax.axis_index("row") % 2

    rowblk = jnp.clip(tile_rows[0, 0], 0, nrb - 1)
    colblk = jnp.clip(tile_cols[0, 0], 0, ncb - 1)
    cnt = jnp.clip(tile_count[0, 0], 0, slots).reshape(1).astype(jnp.int32)

    nb = _nbits(col_size)
    if nb is not None:
        rs_order, ag_order = _orders(nb)
        dest = rowblk // nbc
        sub = rowblk % nbc
        rs_pos = jnp.zeros_like(dest)
        ag_pos = jnp.zeros_like(dest)
        for t in range(nb):
            rs_pos = rs_pos + (((dest >> _pick(parity, rs_order, t)) & 1) << (nb - 1 - t))
            ag_pos = ag_pos + (((dest >> _pick(parity, ag_order, t)) & 1) << t)
        rows_fwd = rs_pos * nbc + sub
        rows_bwd = ag_pos * nbc + sub
    else:
        rows_fwd = rowblk
        rows_bwd = rowblk

    group = gather_row(features).reshape(ncb, side, width)
    fwd_parts = along_call(rows_fwd, colblk, cnt, values, group, nrb)

    mine_t = jnp.transpose(features.reshape(nbc, side, width), (0, 2, 1))
    if nb is not None:
        stripe_t = gather_col(mine_t, ag_order).reshape(nrb, width, side)
        along = scatter_sum_col(fwd_parts.reshape((2,) * nb + (nbc, side, width)), rs_order)
    else:
        stripe_t = lax.all_gather(mine_t, "col", axis=0, tiled=True)
        along = lax.psum_scatter(fwd_parts, "col", scatter_dimension=0, tiled=True)

    bwd_t = against_call(rows_bwd, colblk, cnt, values, stripe_t, ncb)
    against_t = scatter_sum_row(bwd_t)
    against = jnp.transpose(against_t, (0, 2, 1))

    along = along.reshape(-1, width)
    against = against.reshape(-1, width)
    result = jnp.dot(along, w_fwd.astype(jnp.float32), precision=lax.Precision.HIGHEST)
    result = result + jnp.dot(against, w_bwd.astype(jnp.float32), precision=lax.Precision.HIGHEST)
    return result.astype(jnp.bfloat16)


def solution(mesh):
    in_specs = (
        P(("row", "col"), None),
        P("row", "col", None, None, None),
        P("row", "col", None),
        P("row", "col", None),
        P("row", "col"),
        P(),
        P(),
    )
    out_specs = P(("row", "col"), None)
    return jax.shard_map(local, mesh=mesh, in_specs=in_specs, out_specs=out_specs, check_vma=False)
```

```python
import jax
import jax.numpy as jnp
from jax import lax
from jax.experimental import pallas as pl
from jax.experimental.pallas import tpu as pltpu
from jax.sharding import PartitionSpec as P


def _nbits(n):
    bits = n.bit_length() - 1
    return bits if (1 << bits) == n else None


def _orders(nb):
    if nb == 4:
        return ((0, 1, 2, 3), (2, 0, 1, 3)), ((3, 0, 1, 2), (3, 2, 0, 1))
    rs = tuple(range(nb))
    return (rs, rs), (rs[::-1], rs[::-1])


def _pick(parity, pair, t):
    return jnp.where(parity == 0, pair[0][t], pair[1][t])


def _swap_col(x, row_size, col_size, bits):
    perm = []
    for r in range(row_size):
        b = bits[r % 2]
        for c in range(col_size):
            perm.append((r * col_size + c, r * col_size + (c ^ (1 << b))))
    return lax.ppermute(x, ("row", "col"), perm)


def _swap_row(x, row_size, bit):
    perm = [(i, i ^ (1 << bit)) for i in range(row_size)]
    return lax.ppermute(x, "row", perm)


def gather_blocks(x, steps, xchg):
    have = x[None]
    for t in range(steps):
        have = jnp.concatenate([have, xchg(have, t)], axis=0)
    return have


def scatter_blocks(data, steps, xchg):
    for t in range(steps):
        data = data[1] + xchg(data[0], t)
    return data


def gather_pos(g, me, bits):
    pos = jnp.zeros_like(g)
    for t, b in enumerate(bits):
        pos = pos + ((((g ^ me) >> b) & 1) << t)
    return pos


def scatter_pos(g, me, bits):
    nb = len(bits)
    pos = jnp.zeros_like(g)
    for t, b in enumerate(bits):
        pos = pos + ((1 - (((g ^ me) >> b) & 1)) << (nb - 1 - t))
    return pos


def _chunk(slots):
    return 32 if slots % 32 == 0 else slots


def along_call(idx, cnt, values, group, nrb):
    slots, side, _ = values.shape
    width = group.shape[-1]
    k = _chunk(slots)

    def kernel(idx_ref, cnt_ref, vals_ref, grp_ref, out_ref):
        i = pl.program_id(0)
        n = cnt_ref[0]

        @pl.when(i == 0)
        def _():
            out_ref[...] = jnp.zeros(out_ref.shape, out_ref.dtype)

        @pl.when(i * k < n)
        def _():
            for t in range(k):
                s = i * k + t
                tile = jnp.where(s < n, vals_ref[t], jnp.zeros((side, side), vals_ref.dtype))
                r = idx_ref[s]
                c = idx_ref[slots + s]
                out_ref[r] += jnp.dot(tile, grp_ref[c], preferred_element_type=jnp.float32)

    def vals_map(i, idx_ref, cnt_ref):
        last = jnp.maximum(cnt_ref[0] - 1, 0) // k
        return (jnp.minimum(i, last), 0, 0)

    spec = pltpu.PrefetchScalarGridSpec(
        num_scalar_prefetch=2,
        grid=(slots // k,),
        in_specs=[
            pl.BlockSpec((k, side, side), vals_map),
            pl.BlockSpec(group.shape, lambda i, *_: (0, 0, 0)),
        ],
        out_specs=pl.BlockSpec((nrb, side, width), lambda i, *_: (0, 0, 0)),
    )
    return pl.pallas_call(
        kernel,
        grid_spec=spec,
        out_shape=jax.ShapeDtypeStruct((nrb, side, width), jnp.float32),
    )(idx, cnt, values, group)


def against_call(idx, cnt, values, stripe_t, ncb):
    slots, side, _ = values.shape
    width = stripe_t.shape[1]
    k = _chunk(slots)

    def kernel(idx_ref, cnt_ref, vals_ref, st_ref, out_ref):
        i = pl.program_id(0)
        n = cnt_ref[0]

        @pl.when(i == 0)
        def _():
            out_ref[...] = jnp.zeros(out_ref.shape, out_ref.dtype)

        @pl.when(i * k < n)
        def _():
            for t in range(k):
                s = i * k + t
                tile = jnp.where(s < n, vals_ref[t], jnp.zeros((side, side), vals_ref.dtype))
                r = idx_ref[2 * slots + s]
                c = idx_ref[3 * slots + s]
                out_ref[c] += jnp.dot(st_ref[r], tile, preferred_element_type=jnp.float32)

    def vals_map(i, idx_ref, cnt_ref):
        last = jnp.maximum(cnt_ref[0] - 1, 0) // k
        return (jnp.minimum(i, last), 0, 0)

    spec = pltpu.PrefetchScalarGridSpec(
        num_scalar_prefetch=2,
        grid=(slots // k,),
        in_specs=[
            pl.BlockSpec((k, side, side), vals_map),
            pl.BlockSpec(stripe_t.shape, lambda i, *_: (0, 0, 0)),
        ],
        out_specs=pl.BlockSpec((ncb, width, side), lambda i, *_: (0, 0, 0)),
    )
    return pl.pallas_call(
        kernel,
        grid_spec=spec,
        out_shape=jax.ShapeDtypeStruct((ncb, width, side), jnp.float32),
    )(idx, cnt, values, stripe_t)


def local(features, tile_vals, tile_rows, tile_cols, tile_count, w_fwd, w_bwd):
    row_size = lax.axis_size("row")
    col_size = lax.axis_size("col")
    values = tile_vals[0, 0]
    slots = values.shape[0]
    side = values.shape[1]
    nodes_here = features.shape[0]
    nbc = nodes_here // side
    width = features.shape[1]
    nrb = col_size * nbc
    ncb = row_size * nbc
    me_r = lax.axis_index("row")
    me_c = lax.axis_index("col")
    parity = me_r % 2

    rowblk = jnp.clip(tile_rows[0, 0], 0, nrb - 1)
    colblk = jnp.clip(tile_cols[0, 0], 0, ncb - 1)
    cnt = jnp.clip(tile_count[0, 0], 0, slots).reshape(1).astype(jnp.int32)

    nb_c = _nbits(col_size)
    nb_r = _nbits(row_size)
    assert nb_c is not None and nb_r is not None
    rs_order, ag_order = _orders(nb_c)
    row_bits = tuple(range(nb_r))

    dest = rowblk // nbc
    sub = rowblk % nbc
    src = colblk // nbc
    csub = colblk % nbc
    rs_bits = [_pick(parity, rs_order, t) for t in range(nb_c)]
    ag_bits = [_pick(parity, ag_order, t) for t in range(nb_c)]
    rows_fwd = scatter_pos(dest, me_c, rs_bits) * nbc + sub
    rows_bwd = gather_pos(dest, me_c, ag_bits) * nbc + sub
    cols_fwd = gather_pos(src, me_r, row_bits) * nbc + csub
    cols_bwd = scatter_pos(src, me_r, row_bits) * nbc + csub
    idx = jnp.stack([rows_fwd, cols_fwd, rows_bwd, cols_bwd]).reshape(-1)

    def col_x(order):
        return lambda x, t: _swap_col(x, row_size, col_size, (order[0][t], order[1][t]))

    def row_x(x, t):
        return _swap_row(x, row_size, row_bits[t])

    group = gather_blocks(features, nb_r, row_x).reshape(ncb, side, width)
    fwd_parts = along_call(idx, cnt, values, group, nrb)

    mine_t = jnp.transpose(features.reshape(nbc, side, width), (0, 2, 1))
    stripe_t = gather_blocks(mine_t, nb_c, col_x(ag_order)).reshape(nrb, width, side)
    along = scatter_blocks(fwd_parts.reshape((2,) * nb_c + (nbc, side, width)), nb_c, col_x(rs_order))

    bwd_t = against_call(idx, cnt, values, stripe_t, ncb)
    against_t = scatter_blocks(bwd_t.reshape((2,) * nb_r + (nbc, width, side)), nb_r, row_x)
    against = jnp.transpose(against_t, (0, 2, 1))

    along = along.reshape(-1, width)
    against = against.reshape(-1, width)
    result = jnp.dot(along, w_fwd.astype(jnp.float32), precision=lax.Precision.HIGHEST)
    result = result + jnp.dot(against, w_bwd.astype(jnp.float32), precision=lax.Precision.HIGHEST)
    return result.astype(jnp.bfloat16)


def solution(mesh):
    in_specs = (
        P(("row", "col"), None),
        P("row", "col", None, None, None),
        P("row", "col", None),
        P("row", "col", None),
        P("row", "col"),
        P(),
        P(),
    )
    out_specs = P(("row", "col"), None)
    return jax.shard_map(local, mesh=mesh, in_specs=in_specs, out_specs=out_specs, check_vma=False)
```

```python
import jax
import jax.numpy as jnp
from jax import lax
from jax.experimental import pallas as pl
from jax.experimental.pallas import tpu as pltpu
from jax.sharding import PartitionSpec as P


def _nbits(n):
    bits = n.bit_length() - 1
    return bits if (1 << bits) == n else None


def _orders(nb):
    if nb == 4:
        return ((0, 1, 2, 3), (2, 0, 1, 3)), ((3, 0, 1, 2), (3, 2, 0, 1))
    rs = tuple(range(nb))
    return (rs, rs), (rs[::-1], rs[::-1])


def _pick(parity, pair, t):
    return jnp.where(parity == 0, pair[0][t], pair[1][t])


def _swap_col(x, row_size, col_size, bits):
    perm = []
    for r in range(row_size):
        b = bits[r % 2]
        for c in range(col_size):
            perm.append((r * col_size + c, r * col_size + (c ^ (1 << b))))
    return lax.ppermute(x, ("row", "col"), perm)


def _swap_row(x, row_size, bit):
    perm = [(i, i ^ (1 << bit)) for i in range(row_size)]
    return lax.ppermute(x, "row", perm)


def gather_blocks(x, steps, xchg):
    have = x[None]
    firsts = []
    for t in range(steps):
        have = jnp.concatenate([have, xchg(have, t)], axis=0)
        firsts.append(have)
    return have, firsts


def scatter_blocks(data, steps, xchg):
    for t in range(steps):
        data = data[1] + xchg(data[0], t)
    return data


def gather_pos(g, me, bits):
    pos = jnp.zeros_like(g)
    for t, b in enumerate(bits):
        pos = pos + ((((g ^ me) >> b) & 1) << t)
    return pos


def scatter_pos(g, me, bits):
    nb = len(bits)
    pos = jnp.zeros_like(g)
    for t, b in enumerate(bits):
        pos = pos + ((1 - (((g ^ me) >> b) & 1)) << (nb - 1 - t))
    return pos


def _chunk(slots):
    return 32 if slots % 32 == 0 else slots


def along_call(idx, cnt, values, group, nrb, dep):
    slots, side, _ = values.shape
    width = group.shape[-1]
    k = _chunk(slots)

    def kernel(idx_ref, cnt_ref, vals_ref, grp_ref, dep_ref, out_ref):
        i = pl.program_id(0)
        n = cnt_ref[0]

        @pl.when(i == 0)
        def _():
            out_ref[...] = jnp.zeros(out_ref.shape, out_ref.dtype)

        @pl.when(i * k < n)
        def _():
            for t in range(k):
                s = i * k + t
                tile = jnp.where(s < n, vals_ref[t], jnp.zeros((side, side), vals_ref.dtype))
                r = idx_ref[s]
                c = idx_ref[slots + s]
                out_ref[r] += jnp.dot(tile, grp_ref[c], preferred_element_type=jnp.float32)

    def vals_map(i, idx_ref, cnt_ref):
        last = jnp.maximum(cnt_ref[0] - 1, 0) // k
        return (jnp.minimum(i, last), 0, 0)

    spec = pltpu.PrefetchScalarGridSpec(
        num_scalar_prefetch=2,
        grid=(slots // k,),
        in_specs=[
            pl.BlockSpec((k, side, side), vals_map),
            pl.BlockSpec(group.shape, lambda i, *_: (0, 0, 0)),
            pl.BlockSpec(memory_space=pl.ANY),
        ],
        out_specs=pl.BlockSpec((nrb, side, width), lambda i, *_: (0, 0, 0)),
    )
    return pl.pallas_call(
        kernel,
        grid_spec=spec,
        out_shape=jax.ShapeDtypeStruct((nrb, side, width), jnp.float32),
    )(idx, cnt, values, group, dep)


def against_call(idx, cnt, values, stripe_t, ncb):
    slots, side, _ = values.shape
    width = stripe_t.shape[1]
    k = _chunk(slots)

    def kernel(idx_ref, cnt_ref, vals_ref, st_ref, out_ref):
        i = pl.program_id(0)
        n = cnt_ref[0]

        @pl.when(i == 0)
        def _():
            out_ref[...] = jnp.zeros(out_ref.shape, out_ref.dtype)

        @pl.when(i * k < n)
        def _():
            for t in range(k):
                s = i * k + t
                tile = jnp.where(s < n, vals_ref[t], jnp.zeros((side, side), vals_ref.dtype))
                r = idx_ref[2 * slots + s]
                c = idx_ref[3 * slots + s]
                out_ref[c] += jnp.dot(st_ref[r], tile, preferred_element_type=jnp.float32)

    def vals_map(i, idx_ref, cnt_ref):
        last = jnp.maximum(cnt_ref[0] - 1, 0) // k
        return (jnp.minimum(i, last), 0, 0)

    spec = pltpu.PrefetchScalarGridSpec(
        num_scalar_prefetch=2,
        grid=(slots // k,),
        in_specs=[
            pl.BlockSpec((k, side, side), vals_map),
            pl.BlockSpec(stripe_t.shape, lambda i, *_: (0, 0, 0)),
        ],
        out_specs=pl.BlockSpec((ncb, width, side), lambda i, *_: (0, 0, 0)),
    )
    return pl.pallas_call(
        kernel,
        grid_spec=spec,
        out_shape=jax.ShapeDtypeStruct((ncb, width, side), jnp.float32),
    )(idx, cnt, values, stripe_t)


def local(features, tile_vals, tile_rows, tile_cols, tile_count, w_fwd, w_bwd):
    row_size = lax.axis_size("row")
    col_size = lax.axis_size("col")
    values = tile_vals[0, 0]
    slots = values.shape[0]
    side = values.shape[1]
    nodes_here = features.shape[0]
    nbc = nodes_here // side
    width = features.shape[1]
    nrb = col_size * nbc
    ncb = row_size * nbc
    me_r = lax.axis_index("row")
    me_c = lax.axis_index("col")
    parity = me_r % 2

    rowblk = jnp.clip(tile_rows[0, 0], 0, nrb - 1)
    colblk = jnp.clip(tile_cols[0, 0], 0, ncb - 1)
    cnt = jnp.clip(tile_count[0, 0], 0, slots).reshape(1).astype(jnp.int32)

    nb_c = _nbits(col_size)
    nb_r = _nbits(row_size)
    assert nb_c is not None and nb_r is not None
    rs_order, ag_order = _orders(nb_c)
    row_bits = tuple(range(nb_r))

    dest = rowblk // nbc
    sub = rowblk % nbc
    src = colblk // nbc
    csub = colblk % nbc
    rs_bits = [_pick(parity, rs_order, t) for t in range(nb_c)]
    ag_bits = [_pick(parity, ag_order, t) for t in range(nb_c)]
    rows_fwd = scatter_pos(dest, me_c, rs_bits) * nbc + sub
    rows_bwd = gather_pos(dest, me_c, ag_bits) * nbc + sub
    cols_fwd = gather_pos(src, me_r, row_bits) * nbc + csub
    cols_bwd = scatter_pos(src, me_r, row_bits) * nbc + csub
    idx = jnp.stack([rows_fwd, cols_fwd, rows_bwd, cols_bwd]).reshape(-1)

    def col_x(order):
        return lambda x, t: _swap_col(x, row_size, col_size, (order[0][t], order[1][t]))

    def row_x(x, t):
        return _swap_row(x, row_size, row_bits[t])

    group = gather_blocks(features, nb_r, row_x)[0].reshape(ncb, side, width)
    mine_t = jnp.transpose(features.reshape(nbc, side, width), (0, 2, 1))
    stripe_t, stages = gather_blocks(mine_t, nb_c, col_x(ag_order))
    stripe_t = stripe_t.reshape(nrb, width, side)
    fwd_parts = along_call(idx, cnt, values, group, nrb, stages[0])
    along = scatter_blocks(fwd_parts.reshape((2,) * nb_c + (nbc, side, width)), nb_c, col_x(rs_order))

    bwd_t = against_call(idx, cnt, values, stripe_t, ncb)
    against_t = scatter_blocks(bwd_t.reshape((2,) * nb_r + (nbc, width, side)), nb_r, row_x)
    against = jnp.transpose(against_t, (0, 2, 1))

    along = along.reshape(-1, width)
    against = against.reshape(-1, width)
    result = jnp.dot(along, w_fwd.astype(jnp.float32), precision=lax.Precision.HIGHEST)
    result = result + jnp.dot(against, w_bwd.astype(jnp.float32), precision=lax.Precision.HIGHEST)
    return result.astype(jnp.bfloat16)


def solution(mesh):
    in_specs = (
        P(("row", "col"), None),
        P("row", "col", None, None, None),
        P("row", "col", None),
        P("row", "col", None),
        P("row", "col"),
        P(),
        P(),
    )
    out_specs = P(("row", "col"), None)
    return jax.shard_map(local, mesh=mesh, in_specs=in_specs, out_specs=out_specs, check_vma=False)
```

```python
import jax
import jax.numpy as jnp
from jax import lax
from jax.experimental import pallas as pl
from jax.experimental.pallas import tpu as pltpu
from jax.sharding import PartitionSpec as P


def _nbits(n):
    bits = n.bit_length() - 1
    return bits if (1 << bits) == n else None


def _orders(nb):
    if nb == 4:
        return ((0, 1, 2, 3), (2, 0, 1, 3)), ((3, 1, 2, 0), (3, 1, 0, 2))
    rs = tuple(range(nb))
    return (rs, rs), (rs[::-1], rs[::-1])


def _pick(parity, pair, t):
    return jnp.where(parity == 0, pair[0][t], pair[1][t])


def _swap_col(x, row_size, col_size, bits):
    perm = []
    for r in range(row_size):
        b = bits[r % 2]
        for c in range(col_size):
            perm.append((r * col_size + c, r * col_size + (c ^ (1 << b))))
    return lax.ppermute(x, ("row", "col"), perm)


def _swap_row(x, row_size, bit):
    perm = [(i, i ^ (1 << bit)) for i in range(row_size)]
    return lax.ppermute(x, "row", perm)


def gather_blocks(x, steps, xchg):
    have = x[None]
    firsts = []
    for t in range(steps):
        have = jnp.concatenate([have, xchg(have, t)], axis=0)
        firsts.append(have)
    return have, firsts


def scatter_blocks(data, steps, xchg):
    for t in range(steps):
        data = data[1] + xchg(data[0], t)
    return data


def gather_pos(g, me, bits):
    pos = jnp.zeros_like(g)
    for t, b in enumerate(bits):
        pos = pos + ((((g ^ me) >> b) & 1) << t)
    return pos


def scatter_pos(g, me, bits):
    nb = len(bits)
    pos = jnp.zeros_like(g)
    for t, b in enumerate(bits):
        pos = pos + ((1 - (((g ^ me) >> b) & 1)) << (nb - 1 - t))
    return pos


def _chunk(slots):
    return 32 if slots % 32 == 0 else slots


def along_call(idx, cnt, values, group, nrb, dep):
    slots, side, _ = values.shape
    width = group.shape[-1]
    k = _chunk(slots)

    def kernel(idx_ref, cnt_ref, vals_ref, grp_ref, dep_ref, out_ref):
        i = pl.program_id(0)
        n = cnt_ref[0]

        @pl.when(i == 0)
        def _():
            out_ref[...] = jnp.zeros(out_ref.shape, out_ref.dtype)

        @pl.when(i * k < n)
        def _():
            for t in range(k):
                s = i * k + t
                tile = jnp.where(s < n, vals_ref[t], jnp.zeros((side, side), vals_ref.dtype))
                r = idx_ref[s]
                c = idx_ref[slots + s]
                out_ref[r] += jnp.dot(tile, grp_ref[c], preferred_element_type=jnp.float32)

    def vals_map(i, idx_ref, cnt_ref):
        last = jnp.maximum(cnt_ref[0] - 1, 0) // k
        return (jnp.minimum(i, last), 0, 0)

    spec = pltpu.PrefetchScalarGridSpec(
        num_scalar_prefetch=2,
        grid=(slots // k,),
        in_specs=[
            pl.BlockSpec((k, side, side), vals_map),
            pl.BlockSpec(group.shape, lambda i, *_: (0, 0, 0)),
            pl.BlockSpec(memory_space=pl.ANY),
        ],
        out_specs=pl.BlockSpec((nrb, side, width), lambda i, *_: (0, 0, 0)),
    )
    return pl.pallas_call(
        kernel,
        grid_spec=spec,
        out_shape=jax.ShapeDtypeStruct((nrb, side, width), jnp.float32),
    )(idx, cnt, values, group, dep)


def against_call(idx, cnt, values, stripe_t, ncb):
    slots, side, _ = values.shape
    width = stripe_t.shape[1]
    k = _chunk(slots)

    def kernel(idx_ref, cnt_ref, vals_ref, st_ref, out_ref):
        i = pl.program_id(0)
        n = cnt_ref[0]

        @pl.when(i == 0)
        def _():
            out_ref[...] = jnp.zeros(out_ref.shape, out_ref.dtype)

        @pl.when(i * k < n)
        def _():
            for t in range(k):
                s = i * k + t
                tile = jnp.where(s < n, vals_ref[t], jnp.zeros((side, side), vals_ref.dtype))
                r = idx_ref[2 * slots + s]
                c = idx_ref[3 * slots + s]
                out_ref[c] += jnp.dot(st_ref[r], tile, preferred_element_type=jnp.float32)

    def vals_map(i, idx_ref, cnt_ref):
        last = jnp.maximum(cnt_ref[0] - 1, 0) // k
        return (jnp.minimum(i, last), 0, 0)

    spec = pltpu.PrefetchScalarGridSpec(
        num_scalar_prefetch=2,
        grid=(slots // k,),
        in_specs=[
            pl.BlockSpec((k, side, side), vals_map),
            pl.BlockSpec(stripe_t.shape, lambda i, *_: (0, 0, 0)),
        ],
        out_specs=pl.BlockSpec((ncb, width, side), lambda i, *_: (0, 0, 0)),
    )
    return pl.pallas_call(
        kernel,
        grid_spec=spec,
        out_shape=jax.ShapeDtypeStruct((ncb, width, side), jnp.float32),
    )(idx, cnt, values, stripe_t)


def local(features, tile_vals, tile_rows, tile_cols, tile_count, w_fwd, w_bwd):
    row_size = lax.axis_size("row")
    col_size = lax.axis_size("col")
    values = tile_vals[0, 0]
    slots = values.shape[0]
    side = values.shape[1]
    nodes_here = features.shape[0]
    nbc = nodes_here // side
    width = features.shape[1]
    nrb = col_size * nbc
    ncb = row_size * nbc
    me_r = lax.axis_index("row")
    me_c = lax.axis_index("col")
    parity = me_r % 2

    rowblk = jnp.clip(tile_rows[0, 0], 0, nrb - 1)
    colblk = jnp.clip(tile_cols[0, 0], 0, ncb - 1)
    cnt = jnp.clip(tile_count[0, 0], 0, slots).reshape(1).astype(jnp.int32)

    nb_c = _nbits(col_size)
    nb_r = _nbits(row_size)
    assert nb_c is not None and nb_r is not None
    rs_order, ag_order = _orders(nb_c)
    row_bits = tuple(range(nb_r))

    dest = rowblk // nbc
    sub = rowblk % nbc
    src = colblk // nbc
    csub = colblk % nbc
    rs_bits = [_pick(parity, rs_order, t) for t in range(nb_c)]
    ag_bits = [_pick(parity, ag_order, t) for t in range(nb_c)]
    rows_fwd = scatter_pos(dest, me_c, rs_bits) * nbc + sub
    rows_bwd = gather_pos(dest, me_c, ag_bits) * nbc + sub
    cols_fwd = gather_pos(src, me_r, row_bits) * nbc + csub
    cols_bwd = scatter_pos(src, me_r, row_bits) * nbc + csub
    idx = jnp.stack([rows_fwd, cols_fwd, rows_bwd, cols_bwd]).reshape(-1)

    def col_x(order):
        return lambda x, t: _swap_col(x, row_size, col_size, (order[0][t], order[1][t]))

    def row_x(x, t):
        return _swap_row(x, row_size, row_bits[t])

    group = gather_blocks(features, nb_r, row_x)[0].reshape(ncb, side, width)
    mine_t = jnp.transpose(features.reshape(nbc, side, width), (0, 2, 1))
    stripe_t, stages = gather_blocks(mine_t, nb_c, col_x(ag_order))
    stripe_t = stripe_t.reshape(nrb, width, side)
    fwd_parts = along_call(idx, cnt, values, group, nrb, stages[min(1, nb_c - 1)])
    along = scatter_blocks(fwd_parts.reshape((2,) * nb_c + (nbc, side, width)), nb_c, col_x(rs_order))

    bwd_t = against_call(idx, cnt, values, stripe_t, ncb)
    against_t = scatter_blocks(bwd_t.reshape((2,) * nb_r + (nbc, width, side)), nb_r, row_x)
    against = jnp.transpose(against_t, (0, 2, 1))

    along = along.reshape(-1, width)
    against = against.reshape(-1, width)
    result = jnp.dot(along, w_fwd.astype(jnp.float32), precision=lax.Precision.HIGHEST)
    result = result + jnp.dot(against, w_bwd.astype(jnp.float32), precision=lax.Precision.HIGHEST)
    return result.astype(jnp.bfloat16)


def solution(mesh):
    in_specs = (
        P(("row", "col"), None),
        P("row", "col", None, None, None),
        P("row", "col", None),
        P("row", "col", None),
        P("row", "col"),
        P(),
        P(),
    )
    out_specs = P(("row", "col"), None)
    return jax.shard_map(local, mesh=mesh, in_specs=in_specs, out_specs=out_specs, check_vma=False)
```

```python
import jax
import jax.numpy as jnp
from jax import lax
from jax.experimental import pallas as pl
from jax.experimental.pallas import tpu as pltpu
from jax.sharding import PartitionSpec as P


def _nbits(n):
    bits = n.bit_length() - 1
    return bits if (1 << bits) == n else None


def _orders(nb):
    if nb == 4:
        return ((0, 1, 2, 3), (2, 0, 1, 3)), ((3, 1, 2, 0), (3, 1, 0, 2))
    rs = tuple(range(nb))
    return (rs, rs), (rs[::-1], rs[::-1])


def _pick(parity, pair, t):
    return jnp.where(parity == 0, pair[0][t], pair[1][t])


def _swap_col(x, row_size, col_size, bits):
    perm = []
    for r in range(row_size):
        b = bits[r % 2]
        for c in range(col_size):
            perm.append((r * col_size + c, r * col_size + (c ^ (1 << b))))
    return lax.ppermute(x, ("row", "col"), perm)


def _swap_row(x, row_size, bit):
    perm = [(i, i ^ (1 << bit)) for i in range(row_size)]
    return lax.ppermute(x, "row", perm)


def gather_blocks(x, steps, xchg):
    have = x[None]
    firsts = []
    for t in range(steps):
        have = jnp.concatenate([have, xchg(have, t)], axis=0)
        firsts.append(have)
    return have, firsts


def scatter_blocks(data, steps, xchg):
    for t in range(steps):
        data = data[1] + xchg(data[0], t)
    return data


def gather_pos(g, me, bits):
    pos = jnp.zeros_like(g)
    for t, b in enumerate(bits):
        pos = pos + ((((g ^ me) >> b) & 1) << t)
    return pos


def scatter_pos(g, me, bits):
    nb = len(bits)
    pos = jnp.zeros_like(g)
    for t, b in enumerate(bits):
        pos = pos + ((1 - (((g ^ me) >> b) & 1)) << (nb - 1 - t))
    return pos


def _chunk(slots):
    return 32 if slots % 32 == 0 else slots


def along_call(idx, cnt, values, grp_a, grp_b, nrb, dep):
    slots, side, _ = values.shape
    width = grp_a.shape[-1]
    half = grp_a.shape[0]
    k = _chunk(slots)

    def kernel(idx_ref, cnt_ref, vals_ref, ga_ref, gb_ref, dep_ref, out_ref, grp_ref):
        i = pl.program_id(0)
        n = cnt_ref[0]

        @pl.when(i == 0)
        def _():
            out_ref[...] = jnp.zeros(out_ref.shape, out_ref.dtype)
            grp_ref[:half] = ga_ref[...]
            grp_ref[half:] = gb_ref[...]

        @pl.when(i * k < n)
        def _():
            for t in range(k):
                s = i * k + t
                tile = jnp.where(s < n, vals_ref[t], jnp.zeros((side, side), vals_ref.dtype))
                r = idx_ref[s]
                c = idx_ref[slots + s]
                out_ref[r] += jnp.dot(tile, grp_ref[c], preferred_element_type=jnp.float32)

    def vals_map(i, idx_ref, cnt_ref):
        last = jnp.maximum(cnt_ref[0] - 1, 0) // k
        return (jnp.minimum(i, last), 0, 0)

    spec = pltpu.PrefetchScalarGridSpec(
        num_scalar_prefetch=2,
        grid=(slots // k,),
        in_specs=[
            pl.BlockSpec((k, side, side), vals_map),
            pl.BlockSpec(grp_a.shape, lambda i, *_: (0, 0, 0)),
            pl.BlockSpec(grp_b.shape, lambda i, *_: (0, 0, 0)),
            pl.BlockSpec(memory_space=pl.ANY),
        ],
        out_specs=pl.BlockSpec((nrb, side, width), lambda i, *_: (0, 0, 0)),
        scratch_shapes=[pltpu.VMEM((2 * half, side, width), grp_a.dtype)],
    )
    return pl.pallas_call(
        kernel,
        grid_spec=spec,
        out_shape=jax.ShapeDtypeStruct((nrb, side, width), jnp.float32),
    )(idx, cnt, values, grp_a, grp_b, dep)


def against_call(idx, cnt, values, stripe_t, ncb, dep):
    slots, side, _ = values.shape
    width = stripe_t.shape[1]
    k = _chunk(slots)

    def kernel(idx_ref, cnt_ref, vals_ref, st_ref, dep_ref, out_ref):
        i = pl.program_id(0)
        n = cnt_ref[0]

        @pl.when(i == 0)
        def _():
            out_ref[...] = jnp.zeros(out_ref.shape, out_ref.dtype)

        @pl.when(i * k < n)
        def _():
            for t in range(k):
                s = i * k + t
                tile = jnp.where(s < n, vals_ref[t], jnp.zeros((side, side), vals_ref.dtype))
                r = idx_ref[2 * slots + s]
                c = idx_ref[3 * slots + s]
                out_ref[c] += jnp.dot(st_ref[r], tile, preferred_element_type=jnp.float32)

    def vals_map(i, idx_ref, cnt_ref):
        last = jnp.maximum(cnt_ref[0] - 1, 0) // k
        return (jnp.minimum(i, last), 0, 0)

    spec = pltpu.PrefetchScalarGridSpec(
        num_scalar_prefetch=2,
        grid=(slots // k,),
        in_specs=[
            pl.BlockSpec((k, side, side), vals_map),
            pl.BlockSpec(stripe_t.shape, lambda i, *_: (0, 0, 0)),
            pl.BlockSpec(memory_space=pl.ANY),
        ],
        out_specs=pl.BlockSpec((ncb, width, side), lambda i, *_: (0, 0, 0)),
    )
    return pl.pallas_call(
        kernel,
        grid_spec=spec,
        out_shape=jax.ShapeDtypeStruct((ncb, width, side), jnp.float32),
    )(idx, cnt, values, stripe_t, dep)


def local(features, tile_vals, tile_rows, tile_cols, tile_count, w_fwd, w_bwd):
    row_size = lax.axis_size("row")
    col_size = lax.axis_size("col")
    values = tile_vals[0, 0]
    slots = values.shape[0]
    side = values.shape[1]
    nodes_here = features.shape[0]
    nbc = nodes_here // side
    width = features.shape[1]
    nrb = col_size * nbc
    ncb = row_size * nbc
    me_r = lax.axis_index("row")
    me_c = lax.axis_index("col")
    parity = me_r % 2

    rowblk = jnp.clip(tile_rows[0, 0], 0, nrb - 1)
    colblk = jnp.clip(tile_cols[0, 0], 0, ncb - 1)
    cnt = jnp.clip(tile_count[0, 0], 0, slots).reshape(1).astype(jnp.int32)

    nb_c = _nbits(col_size)
    nb_r = _nbits(row_size)
    assert nb_c is not None and nb_r is not None
    rs_order, ag_order = _orders(nb_c)
    row_bits = tuple(range(nb_r))

    dest = rowblk // nbc
    sub = rowblk % nbc
    src = colblk // nbc
    csub = colblk % nbc
    rs_bits = [_pick(parity, rs_order, t) for t in range(nb_c)]
    ag_bits = [_pick(parity, ag_order, t) for t in range(nb_c)]
    which = lax.broadcasted_iota(jnp.int32, (4, slots), 0)
    dest = jnp.broadcast_to(dest, (4, slots))
    sub = jnp.broadcast_to(sub, (4, slots))
    src = jnp.broadcast_to(src, (4, slots))
    csub = jnp.broadcast_to(csub, (4, slots))
    rows_fwd = scatter_pos(dest, me_c, rs_bits) * nbc + sub
    rows_bwd = gather_pos(dest, me_c, ag_bits) * nbc + sub
    cols_fwd = gather_pos(src, me_r, row_bits) * nbc + csub
    cols_bwd = scatter_pos(src, me_r, row_bits) * nbc + csub
    idx = jnp.where(which == 0, rows_fwd, jnp.where(which == 1, cols_fwd, jnp.where(which == 2, rows_bwd, cols_bwd)))
    idx = idx.reshape(-1)

    def col_x(order):
        return lambda x, t: _swap_col(x, row_size, col_size, (order[0][t], order[1][t]))

    def row_x(x, t):
        return _swap_row(x, row_size, row_bits[t])

    grp_a, _ = gather_blocks(features, nb_r - 1, row_x)
    grp_b = row_x(grp_a, nb_r - 1)
    grp_a = grp_a.reshape(-1, side, width)
    grp_b = grp_b.reshape(-1, side, width)
    mine_t = jnp.transpose(features.reshape(nbc, side, width), (0, 2, 1))
    stripe_t, stages = gather_blocks(mine_t, nb_c, col_x(ag_order))
    stripe_t = stripe_t.reshape(nrb, width, side)
    fwd_parts = along_call(idx, cnt, values, grp_a, grp_b, nrb, stages[min(1, nb_c - 1)])
    along = scatter_blocks(fwd_parts.reshape((2,) * nb_c + (nbc, side, width)), nb_c, col_x(rs_order))

    bwd_t = against_call(idx, cnt, values, stripe_t, ncb, along)
    against_t = scatter_blocks(bwd_t.reshape((2,) * nb_r + (nbc, width, side)), nb_r, row_x)
    against = jnp.transpose(against_t, (0, 2, 1))

    along = along.reshape(-1, width)
    against = against.reshape(-1, width)
    result = jnp.dot(along, w_fwd.astype(jnp.float32), precision=lax.Precision.HIGHEST)
    result = result + jnp.dot(against, w_bwd.astype(jnp.float32), precision=lax.Precision.HIGHEST)
    return result.astype(jnp.bfloat16)


def solution(mesh):
    in_specs = (
        P(("row", "col"), None),
        P("row", "col", None, None, None),
        P("row", "col", None),
        P("row", "col", None),
        P("row", "col"),
        P(),
        P(),
    )
    out_specs = P(("row", "col"), None)
    return jax.shard_map(local, mesh=mesh, in_specs=in_specs, out_specs=out_specs, check_vma=False)
```

```python
import jax
import jax.numpy as jnp
from jax import lax
from jax.experimental import pallas as pl
from jax.experimental.pallas import tpu as pltpu
from jax.sharding import PartitionSpec as P


def _nbits(n):
    bits = n.bit_length() - 1
    return bits if (1 << bits) == n else None


def _orders(nb):
    if nb == 4:
        return ((0, 1, 2, 3), (2, 0, 1, 3)), ((3, 0, 2, 1), (3, 2, 0, 1))
    rs = tuple(range(nb))
    return (rs, rs), (rs[::-1], rs[::-1])


def _pick(parity, pair, t):
    return jnp.where(parity == 0, pair[0][t], pair[1][t])


def _swap_col(x, row_size, col_size, bits):
    perm = []
    for r in range(row_size):
        b = bits[r % 2]
        for c in range(col_size):
            perm.append((r * col_size + c, r * col_size + (c ^ (1 << b))))
    return lax.ppermute(x, ("row", "col"), perm)


def _swap_row(x, row_size, bit):
    perm = [(i, i ^ (1 << bit)) for i in range(row_size)]
    return lax.ppermute(x, "row", perm)


def gather_blocks(x, steps, xchg):
    have = x[None]
    firsts = []
    for t in range(steps):
        have = jnp.concatenate([have, xchg(have, t)], axis=0)
        firsts.append(have)
    return have, firsts


def scatter_blocks(data, steps, xchg):
    for t in range(steps):
        data = data[1] + xchg(data[0], t)
    return data


def gather_pos(g, me, bits):
    pos = jnp.zeros_like(g)
    for t, b in enumerate(bits):
        pos = pos + ((((g ^ me) >> b) & 1) << t)
    return pos


def scatter_pos(g, me, bits):
    nb = len(bits)
    pos = jnp.zeros_like(g)
    for t, b in enumerate(bits):
        pos = pos + ((1 - (((g ^ me) >> b) & 1)) << (nb - 1 - t))
    return pos


def _chunk(slots):
    return 32 if slots % 32 == 0 else slots


def along_call(idx, cnt, values, group, nrb, dep):
    slots, side, _ = values.shape
    width = group.shape[-1]
    k = _chunk(slots)

    def kernel(idx_ref, cnt_ref, vals_ref, grp_ref, dep_ref, out_ref):
        i = pl.program_id(0)
        n = cnt_ref[0]

        @pl.when(i == 0)
        def _():
            out_ref[...] = jnp.zeros(out_ref.shape, out_ref.dtype)

        @pl.when(i * k < n)
        def _():
            for t in range(k):
                s = i * k + t
                tile = jnp.where(s < n, vals_ref[t], jnp.zeros((side, side), vals_ref.dtype))
                r = idx_ref[s]
                c = idx_ref[slots + s]
                out_ref[r] += jnp.dot(tile, grp_ref[c], preferred_element_type=jnp.float32)

    def vals_map(i, idx_ref, cnt_ref):
        last = jnp.maximum(cnt_ref[0] - 1, 0) // k
        return (jnp.minimum(i, last), 0, 0)

    spec = pltpu.PrefetchScalarGridSpec(
        num_scalar_prefetch=2,
        grid=(slots // k,),
        in_specs=[
            pl.BlockSpec((k, side, side), vals_map),
            pl.BlockSpec(group.shape, lambda i, *_: (0, 0, 0)),
            pl.BlockSpec(memory_space=pl.ANY),
        ],
        out_specs=pl.BlockSpec((nrb, side, width), lambda i, *_: (0, 0, 0)),
    )
    return pl.pallas_call(
        kernel,
        grid_spec=spec,
        out_shape=jax.ShapeDtypeStruct((nrb, side, width), jnp.float32),
    )(idx, cnt, values, group, dep)


def against_call(idx, cnt, values, stripe_t, ncb):
    slots, side, _ = values.shape
    width = stripe_t.shape[1]
    k = _chunk(slots)

    def kernel(idx_ref, cnt_ref, vals_ref, st_ref, out_ref):
        i = pl.program_id(0)
        n = cnt_ref[0]

        @pl.when(i == 0)
        def _():
            out_ref[...] = jnp.zeros(out_ref.shape, out_ref.dtype)

        @pl.when(i * k < n)
        def _():
            for t in range(k):
                s = i * k + t
                tile = jnp.where(s < n, vals_ref[t], jnp.zeros((side, side), vals_ref.dtype))
                r = idx_ref[2 * slots + s]
                c = idx_ref[3 * slots + s]
                out_ref[c] += jnp.dot(st_ref[r], tile, preferred_element_type=jnp.float32)

    def vals_map(i, idx_ref, cnt_ref):
        last = jnp.maximum(cnt_ref[0] - 1, 0) // k
        return (jnp.minimum(i, last), 0, 0)

    spec = pltpu.PrefetchScalarGridSpec(
        num_scalar_prefetch=2,
        grid=(slots // k,),
        in_specs=[
            pl.BlockSpec((k, side, side), vals_map),
            pl.BlockSpec(stripe_t.shape, lambda i, *_: (0, 0, 0)),
        ],
        out_specs=pl.BlockSpec((ncb, width, side), lambda i, *_: (0, 0, 0)),
    )
    return pl.pallas_call(
        kernel,
        grid_spec=spec,
        out_shape=jax.ShapeDtypeStruct((ncb, width, side), jnp.float32),
    )(idx, cnt, values, stripe_t)


def local(features, tile_vals, tile_rows, tile_cols, tile_count, w_fwd, w_bwd):
    row_size = lax.axis_size("row")
    col_size = lax.axis_size("col")
    values = tile_vals[0, 0]
    slots = values.shape[0]
    side = values.shape[1]
    nodes_here = features.shape[0]
    nbc = nodes_here // side
    width = features.shape[1]
    nrb = col_size * nbc
    ncb = row_size * nbc
    me_r = lax.axis_index("row")
    me_c = lax.axis_index("col")
    parity = me_r % 2

    rowblk = jnp.clip(tile_rows[0, 0], 0, nrb - 1)
    colblk = jnp.clip(tile_cols[0, 0], 0, ncb - 1)
    cnt = jnp.clip(tile_count[0, 0], 0, slots).reshape(1).astype(jnp.int32)

    nb_c = _nbits(col_size)
    nb_r = _nbits(row_size)
    assert nb_c is not None and nb_r is not None
    rs_order, ag_order = _orders(nb_c)
    row_bits = tuple(range(nb_r))

    dest = rowblk // nbc
    sub = rowblk % nbc
    src = colblk // nbc
    csub = colblk % nbc
    rs_bits = [_pick(parity, rs_order, t) for t in range(nb_c)]
    ag_bits = [_pick(parity, ag_order, t) for t in range(nb_c)]
    rows_fwd = scatter_pos(dest, me_c, rs_bits) * nbc + sub
    rows_bwd = gather_pos(dest, me_c, ag_bits) * nbc + sub
    cols_fwd = gather_pos(src, me_r, row_bits) * nbc + csub
    cols_bwd = scatter_pos(src, me_r, row_bits) * nbc + csub
    idx = jnp.stack([rows_fwd, cols_fwd, rows_bwd, cols_bwd]).reshape(-1)

    def col_x(order):
        return lambda x, t: _swap_col(x, row_size, col_size, (order[0][t], order[1][t]))

    def row_x(x, t):
        return _swap_row(x, row_size, row_bits[t])

    group = gather_blocks(features, nb_r, row_x)[0].reshape(ncb, side, width)
    mine_t = jnp.transpose(features.reshape(nbc, side, width), (0, 2, 1))
    stripe_t, stages = gather_blocks(mine_t, nb_c, col_x(ag_order))
    stripe_t = stripe_t.reshape(nrb, width, side)
    fwd_parts = along_call(idx, cnt, values, group, nrb, stages[min(2, nb_c - 1)])
    along = scatter_blocks(fwd_parts.reshape((2,) * nb_c + (nbc, side, width)), nb_c, col_x(rs_order))

    bwd_t = against_call(idx, cnt, values, stripe_t, ncb)
    against_t = scatter_blocks(bwd_t.reshape((2,) * nb_r + (nbc, width, side)), nb_r, row_x)
    against = jnp.transpose(against_t, (0, 2, 1))

    along = along.reshape(-1, width)
    against = against.reshape(-1, width)
    result = jnp.dot(along, w_fwd.astype(jnp.float32), precision=lax.Precision.HIGHEST)
    result = result + jnp.dot(against, w_bwd.astype(jnp.float32), precision=lax.Precision.HIGHEST)
    return result.astype(jnp.bfloat16)


def solution(mesh):
    in_specs = (
        P(("row", "col"), None),
        P("row", "col", None, None, None),
        P("row", "col", None),
        P("row", "col", None),
        P("row", "col"),
        P(),
        P(),
    )
    out_specs = P(("row", "col"), None)
    return jax.shard_map(local, mesh=mesh, in_specs=in_specs, out_specs=out_specs, check_vma=False)
```

```python
import jax
import jax.numpy as jnp
from jax import lax
from jax.experimental import pallas as pl
from jax.experimental.pallas import tpu as pltpu
from jax.sharding import PartitionSpec as P


def _nbits(n):
    bits = n.bit_length() - 1
    return bits if (1 << bits) == n else None


def _orders(nb):
    if nb == 4:
        return ((0, 1, 2, 3), (2, 0, 1, 3)), ((3, 0, 1, 2), (3, 0, 1, 2))
    rs = tuple(range(nb))
    return (rs, rs), (rs[::-1], rs[::-1])


def _pick(parity, pair, t):
    return jnp.where(parity == 0, pair[0][t], pair[1][t])


def _swap_col(x, row_size, col_size, bits):
    perm = []
    for r in range(row_size):
        b = bits[r % 2]
        for c in range(col_size):
            perm.append((r * col_size + c, r * col_size + (c ^ (1 << b))))
    return lax.ppermute(x, ("row", "col"), perm)


def _swap(x, axis, size, bit):
    perm = [(i, i ^ (1 << bit)) for i in range(size)]
    return lax.ppermute(x, axis, perm)


def gather_row(x):
    size = lax.axis_size("row")
    nb = _nbits(size)
    if nb is None:
        return lax.all_gather(x, "row", axis=0, tiled=True)
    me = lax.axis_index("row")
    have = x[None]
    order = list(range(nb - 1, -1, -1))
    for bit in order:
        got = _swap(have, "row", size, bit)
        mine = (me >> bit) & 1
        lo = jnp.where(mine == 0, have, got)
        hi = jnp.where(mine == 0, got, have)
        have = jnp.stack([lo, hi], axis=0).reshape((-1,) + have.shape[1:])
    have = have.reshape((2,) * nb + x.shape)
    processed = order[::-1]
    perm = [processed.index(b) for b in range(nb - 1, -1, -1)]
    have = jnp.transpose(have, perm + list(range(nb, nb + x.ndim)))
    return have.reshape((size * x.shape[0],) + x.shape[1:])


def scatter_sum_row(x):
    size = lax.axis_size("row")
    nb = _nbits(size)
    if nb is None:
        return lax.psum_scatter(x, "row", scatter_dimension=0, tiled=True)
    me = lax.axis_index("row")
    data = x.reshape((2,) * nb + (x.shape[0] // size,) + x.shape[1:])
    axes_bits = list(range(nb - 1, -1, -1))
    for bit in range(nb):
        a = axes_bits.index(bit)
        mine = (me >> bit) & 1
        keep = lax.dynamic_index_in_dim(data, mine, axis=a, keepdims=False)
        other = lax.dynamic_index_in_dim(data, 1 - mine, axis=a, keepdims=False)
        data = keep + _swap(other, "row", size, bit)
        axes_bits.pop(a)
    return data


def gather_col(x, order):
    row_size = lax.axis_size("row")
    col_size = lax.axis_size("col")
    nb = len(order[0])
    me = lax.axis_index("col")
    parity = lax.axis_index("row") % 2
    have = x[None]
    for t in range(nb):
        got = _swap_col(have, row_size, col_size, (order[0][t], order[1][t]))
        mine = (me >> _pick(parity, order, t)) & 1
        lo = jnp.where(mine == 0, have, got)
        hi = jnp.where(mine == 0, got, have)
        have = jnp.stack([lo, hi], axis=0).reshape((-1,) + have.shape[1:])
    return have


def scatter_sum_col(data, order):
    row_size = lax.axis_size("row")
    col_size = lax.axis_size("col")
    nb = len(order[0])
    me = lax.axis_index("col")
    parity = lax.axis_index("row") % 2
    for t in range(nb):
        mine = (me >> _pick(parity, order, t)) & 1
        keep = lax.dynamic_index_in_dim(data, mine, axis=0, keepdims=False)
        other = lax.dynamic_index_in_dim(data, 1 - mine, axis=0, keepdims=False)
        data = keep + _swap_col(other, row_size, col_size, (order[0][t], order[1][t]))
    return data


def _chunk(slots):
    return 32 if slots % 32 == 0 else slots


def along_call(rows, cols, cnt, values, group, nrb):
    slots, side, _ = values.shape
    width = group.shape[-1]
    k = _chunk(slots)

    def kernel(rows_ref, cols_ref, cnt_ref, vals_ref, grp_ref, out_ref):
        i = pl.program_id(0)
        n = cnt_ref[0]

        @pl.when(i == 0)
        def _():
            out_ref[...] = jnp.zeros(out_ref.shape, out_ref.dtype)

        @pl.when(i * k < n)
        def _():
            for t in range(k):
                s = i * k + t
                tile = jnp.where(s < n, vals_ref[t], jnp.zeros((side, side), vals_ref.dtype))
                r = rows_ref[s]
                c = cols_ref[s]
                out_ref[r] += jnp.dot(tile, grp_ref[c], preferred_element_type=jnp.float32)

    def vals_map(i, rows_ref, cols_ref, cnt_ref):
        last = jnp.maximum(cnt_ref[0] - 1, 0) // k
        return (jnp.minimum(i, last), 0, 0)

    spec = pltpu.PrefetchScalarGridSpec(
        num_scalar_prefetch=3,
        grid=(slots // k,),
        in_specs=[
            pl.BlockSpec((k, side, side), vals_map),
            pl.BlockSpec(group.shape, lambda i, *_: (0, 0, 0)),
        ],
        out_specs=pl.BlockSpec((nrb, side, width), lambda i, *_: (0, 0, 0)),
    )
    return pl.pallas_call(
        kernel,
        grid_spec=spec,
        out_shape=jax.ShapeDtypeStruct((nrb, side, width), jnp.float32),
    )(rows, cols, cnt, values, group)


def against_call(rows, cols, cnt, values, stripe_t, ncb):
    slots, side, _ = values.shape
    width = stripe_t.shape[1]
    k = _chunk(slots)

    def kernel(rows_ref, cols_ref, cnt_ref, vals_ref, st_ref, out_ref):
        i = pl.program_id(0)
        n = cnt_ref[0]

        @pl.when(i == 0)
        def _():
            out_ref[...] = jnp.zeros(out_ref.shape, out_ref.dtype)

        @pl.when(i * k < n)
        def _():
            for t in range(k):
                s = i * k + t
                tile = jnp.where(s < n, vals_ref[t], jnp.zeros((side, side), vals_ref.dtype))
                r = rows_ref[s]
                c = cols_ref[s]
                out_ref[c] += jnp.dot(st_ref[r], tile, preferred_element_type=jnp.float32)

    def vals_map(i, rows_ref, cols_ref, cnt_ref):
        last = jnp.maximum(cnt_ref[0] - 1, 0) // k
        return (jnp.minimum(i, last), 0, 0)

    spec = pltpu.PrefetchScalarGridSpec(
        num_scalar_prefetch=3,
        grid=(slots // k,),
        in_specs=[
            pl.BlockSpec((k, side, side), vals_map),
            pl.BlockSpec(stripe_t.shape, lambda i, *_: (0, 0, 0)),
        ],
        out_specs=pl.BlockSpec((ncb, width, side), lambda i, *_: (0, 0, 0)),
    )
    return pl.pallas_call(
        kernel,
        grid_spec=spec,
        out_shape=jax.ShapeDtypeStruct((ncb, width, side), jnp.float32),
    )(rows, cols, cnt, values, stripe_t)


def local(features, tile_vals, tile_rows, tile_cols, tile_count, w_fwd, w_bwd):
    row_size = lax.axis_size("row")
    col_size = lax.axis_size("col")
    values = tile_vals[0, 0]
    slots = values.shape[0]
    side = values.shape[1]
    nodes_here = features.shape[0]
    nbc = nodes_here // side
    width = features.shape[1]
    nrb = col_size * nbc
    ncb = row_size * nbc
    parity = lax.axis_index("row") % 2

    rowblk = jnp.clip(tile_rows[0, 0], 0, nrb - 1)
    colblk = jnp.clip(tile_cols[0, 0], 0, ncb - 1)
    cnt = jnp.clip(tile_count[0, 0], 0, slots).reshape(1).astype(jnp.int32)

    nb = _nbits(col_size)
    if nb is not None:
        rs_order, ag_order = _orders(nb)
        dest = rowblk // nbc
        sub = rowblk % nbc
        rs_pos = jnp.zeros_like(dest)
        ag_pos = jnp.zeros_like(dest)
        for t in range(nb):
            rs_pos = rs_pos + (((dest >> _pick(parity, rs_order, t)) & 1) << (nb - 1 - t))
            ag_pos = ag_pos + (((dest >> _pick(parity, ag_order, t)) & 1) << t)
        rows_fwd = rs_pos * nbc + sub
        rows_bwd = ag_pos * nbc + sub
    else:
        rows_fwd = rowblk
        rows_bwd = rowblk

    group = gather_row(features).reshape(ncb, side, width)
    fwd_parts = along_call(rows_fwd, colblk, cnt, values, group, nrb)

    mine_t = jnp.transpose(features.reshape(nbc, side, width), (0, 2, 1))
    if nb is not None:
        stripe_t = gather_col(mine_t, ag_order).reshape(nrb, width, side)
        along = scatter_sum_col(fwd_parts.reshape((2,) * nb + (nbc, side, width)), rs_order)
    else:
        stripe_t = lax.all_gather(mine_t, "col", axis=0, tiled=True)
        along = lax.psum_scatter(fwd_parts, "col", scatter_dimension=0, tiled=True)

    bwd_t = against_call(rows_bwd, colblk, cnt, values, stripe_t, ncb)
    against_t = scatter_sum_row(bwd_t)
    against = jnp.transpose(against_t, (0, 2, 1))

    along = along.reshape(-1, width)
    against = against.reshape(-1, width)
    result = jnp.dot(along, w_fwd.astype(jnp.float32), precision=lax.Precision.HIGHEST)
    result = result + jnp.dot(against, w_bwd.astype(jnp.float32), precision=lax.Precision.HIGHEST)
    return result.astype(jnp.bfloat16)


def solution(mesh):
    in_specs = (
        P(("row", "col"), None),
        P("row", "col", None, None, None),
        P("row", "col", None),
        P("row", "col", None),
        P("row", "col"),
        P(),
        P(),
    )
    out_specs = P(("row", "col"), None)
    return jax.shard_map(local, mesh=mesh, in_specs=in_specs, out_specs=out_specs, check_vma=False)
```

```python
import jax
import jax.numpy as jnp
from jax import lax
from jax.experimental import pallas as pl
from jax.experimental.pallas import tpu as pltpu
from jax.sharding import PartitionSpec as P


def _nbits(n):
    bits = n.bit_length() - 1
    return bits if (1 << bits) == n else None


def _orders(nb):
    if nb == 4:
        return ((0, 1, 2, 3), (2, 0, 1, 3)), ((3, 0, 1, 2), (3, 2, 0, 1))
    rs = tuple(range(nb))
    return (rs, rs), (rs[::-1], rs[::-1])


def _pick(parity, pair, t):
    return jnp.where(parity == 0, pair[0][t], pair[1][t])


def _swap_col(x, row_size, col_size, bits):
    perm = []
    for r in range(row_size):
        b = bits[r % 2]
        for c in range(col_size):
            perm.append((r * col_size + c, r * col_size + (c ^ (1 << b))))
    return lax.ppermute(x, ("row", "col"), perm)


def _swap(x, axis, size, bit):
    perm = [(i, i ^ (1 << bit)) for i in range(size)]
    return lax.ppermute(x, axis, perm)


def gather_row(x):
    size = lax.axis_size("row")
    nb = _nbits(size)
    if nb is None:
        return lax.all_gather(x, "row", axis=0, tiled=True)
    me = lax.axis_index("row")
    have = x[None]
    order = list(range(nb - 1, -1, -1))
    for bit in order:
        got = _swap(have, "row", size, bit)
        mine = (me >> bit) & 1
        lo = jnp.where(mine == 0, have, got)
        hi = jnp.where(mine == 0, got, have)
        have = jnp.stack([lo, hi], axis=0).reshape((-1,) + have.shape[1:])
    have = have.reshape((2,) * nb + x.shape)
    processed = order[::-1]
    perm = [processed.index(b) for b in range(nb - 1, -1, -1)]
    have = jnp.transpose(have, perm + list(range(nb, nb + x.ndim)))
    return have.reshape((size * x.shape[0],) + x.shape[1:])


def scatter_sum_row(x):
    size = lax.axis_size("row")
    nb = _nbits(size)
    if nb is None:
        return lax.psum_scatter(x, "row", scatter_dimension=0, tiled=True)
    me = lax.axis_index("row")
    data = x.reshape((2,) * nb + (x.shape[0] // size,) + x.shape[1:])
    axes_bits = list(range(nb - 1, -1, -1))
    for bit in range(nb):
        a = axes_bits.index(bit)
        mine = (me >> bit) & 1
        keep = lax.dynamic_index_in_dim(data, mine, axis=a, keepdims=False)
        other = lax.dynamic_index_in_dim(data, 1 - mine, axis=a, keepdims=False)
        data = keep + _swap(other, "row", size, bit)
        axes_bits.pop(a)
    return data


def gather_col(x, order):
    row_size = lax.axis_size("row")
    col_size = lax.axis_size("col")
    nb = len(order[0])
    me = lax.axis_index("col")
    parity = lax.axis_index("row") % 2
    have = x[None]
    for t in range(nb):
        got = _swap_col(have, row_size, col_size, (order[0][t], order[1][t]))
        mine = (me >> _pick(parity, order, t)) & 1
        lo = jnp.where(mine == 0, have, got)
        hi = jnp.where(mine == 0, got, have)
        have = jnp.stack([lo, hi], axis=0).reshape((-1,) + have.shape[1:])
    return have


def scatter_sum_col(data, order):
    row_size = lax.axis_size("row")
    col_size = lax.axis_size("col")
    nb = len(order[0])
    me = lax.axis_index("col")
    parity = lax.axis_index("row") % 2
    for t in range(nb):
        mine = (me >> _pick(parity, order, t)) & 1
        keep = lax.dynamic_index_in_dim(data, mine, axis=0, keepdims=False)
        other = lax.dynamic_index_in_dim(data, 1 - mine, axis=0, keepdims=False)
        data = keep + _swap_col(other, row_size, col_size, (order[0][t], order[1][t]))
    return data


def _chunk(slots):
    return 32 if slots % 32 == 0 else slots


def along_call(rows, cols, cnt, values, group, nrb, fwd_index):
    slots, side, _ = values.shape
    width = group.shape[-1]
    k = _chunk(slots)

    def kernel(rows_ref, cols_ref, cnt_ref, vals_ref, grp_ref, out_ref):
        i = pl.program_id(0)
        n = jnp.clip(cnt_ref[0], 0, slots)

        @pl.when(i == 0)
        def _():
            out_ref[...] = jnp.zeros(out_ref.shape, out_ref.dtype)

        @pl.when(i * k < n)
        def _():
            for t in range(k):
                s = i * k + t
                tile = jnp.where(s < n, vals_ref[t], jnp.zeros((side, side), vals_ref.dtype))
                r, c = fwd_index(rows_ref[s], cols_ref[s])
                out_ref[r] += jnp.dot(tile, grp_ref[c], preferred_element_type=jnp.float32)

    def vals_map(i, rows_ref, cols_ref, cnt_ref):
        last = jnp.clip(cnt_ref[0] - 1, 0, slots - 1) // k
        return (jnp.minimum(i, last), 0, 0)

    spec = pltpu.PrefetchScalarGridSpec(
        num_scalar_prefetch=3,
        grid=(slots // k,),
        in_specs=[
            pl.BlockSpec((k, side, side), vals_map),
            pl.BlockSpec(group.shape, lambda i, *_: (0, 0, 0)),
        ],
        out_specs=pl.BlockSpec((nrb, side, width), lambda i, *_: (0, 0, 0)),
    )
    return pl.pallas_call(
        kernel,
        grid_spec=spec,
        out_shape=jax.ShapeDtypeStruct((nrb, side, width), jnp.float32),
    )(rows, cols, cnt, values, group)


def against_call(rows, cols, cnt, values, stripe_t, ncb, bwd_index):
    slots, side, _ = values.shape
    width = stripe_t.shape[1]
    k = _chunk(slots)

    def kernel(rows_ref, cols_ref, cnt_ref, vals_ref, st_ref, out_ref):
        i = pl.program_id(0)
        n = jnp.clip(cnt_ref[0], 0, slots)

        @pl.when(i == 0)
        def _():
            out_ref[...] = jnp.zeros(out_ref.shape, out_ref.dtype)

        @pl.when(i * k < n)
        def _():
            for t in range(k):
                s = i * k + t
                tile = jnp.where(s < n, vals_ref[t], jnp.zeros((side, side), vals_ref.dtype))
                r, c = bwd_index(rows_ref[s], cols_ref[s])
                out_ref[c] += jnp.dot(st_ref[r], tile, preferred_element_type=jnp.float32)

    def vals_map(i, rows_ref, cols_ref, cnt_ref):
        last = jnp.clip(cnt_ref[0] - 1, 0, slots - 1) // k
        return (jnp.minimum(i, last), 0, 0)

    spec = pltpu.PrefetchScalarGridSpec(
        num_scalar_prefetch=3,
        grid=(slots // k,),
        in_specs=[
            pl.BlockSpec((k, side, side), vals_map),
            pl.BlockSpec(stripe_t.shape, lambda i, *_: (0, 0, 0)),
        ],
        out_specs=pl.BlockSpec((ncb, width, side), lambda i, *_: (0, 0, 0)),
    )
    return pl.pallas_call(
        kernel,
        grid_spec=spec,
        out_shape=jax.ShapeDtypeStruct((ncb, width, side), jnp.float32),
    )(rows, cols, cnt, values, stripe_t)


def local(features, tile_vals, tile_rows, tile_cols, tile_count, w_fwd, w_bwd):
    row_size = lax.axis_size("row")
    col_size = lax.axis_size("col")
    values = tile_vals[0, 0]
    slots = values.shape[0]
    side = values.shape[1]
    nodes_here = features.shape[0]
    nbc = nodes_here // side
    width = features.shape[1]
    nrb = col_size * nbc
    ncb = row_size * nbc
    parity = lax.axis_index("row") % 2

    rows = tile_rows.reshape(slots)
    cols = tile_cols.reshape(slots)
    cnt = tile_count.reshape(1)

    nb = _nbits(col_size)
    if nb is not None:
        rs_order, ag_order = _orders(nb)

    def block_pos(rowblk, order, msb_first):
        if nb is None:
            return rowblk
        par = lax.axis_index("row") % 2
        dest = rowblk // nbc
        pos = 0
        for t in range(nb):
            bit = (dest >> _pick(par, order, t)) & 1
            pos = pos + (bit << ((nb - 1 - t) if msb_first else t))
        return pos * nbc + rowblk % nbc

    def fwd_index(r, c):
        r = jnp.clip(r, 0, nrb - 1)
        c = jnp.clip(c, 0, ncb - 1)
        return block_pos(r, rs_order if nb is not None else None, True), c

    def bwd_index(r, c):
        r = jnp.clip(r, 0, nrb - 1)
        c = jnp.clip(c, 0, ncb - 1)
        return block_pos(r, ag_order if nb is not None else None, False), c

    group = gather_row(features).reshape(ncb, side, width)
    fwd_parts = along_call(rows, cols, cnt, values, group, nrb, fwd_index)

    mine_t = jnp.transpose(features.reshape(nbc, side, width), (0, 2, 1))
    if nb is not None:
        stripe_t = gather_col(mine_t, ag_order).reshape(nrb, width, side)
        along = scatter_sum_col(fwd_parts.reshape((2,) * nb + (nbc, side, width)), rs_order)
    else:
        stripe_t = lax.all_gather(mine_t, "col", axis=0, tiled=True)
        along = lax.psum_scatter(fwd_parts, "col", scatter_dimension=0, tiled=True)

    bwd_t = against_call(rows, cols, cnt, values, stripe_t, ncb, bwd_index)
    against_t = scatter_sum_row(bwd_t)
    against = jnp.transpose(against_t, (0, 2, 1))

    along = along.reshape(-1, width)
    against = against.reshape(-1, width)
    result = jnp.dot(along, w_fwd.astype(jnp.float32), precision=lax.Precision.HIGHEST)
    result = result + jnp.dot(against, w_bwd.astype(jnp.float32), precision=lax.Precision.HIGHEST)
    return result.astype(jnp.bfloat16)


def solution(mesh):
    in_specs = (
        P(("row", "col"), None),
        P("row", "col", None, None, None),
        P("row", "col", None),
        P("row", "col", None),
        P("row", "col"),
        P(),
        P(),
    )
    out_specs = P(("row", "col"), None)
    return jax.shard_map(local, mesh=mesh, in_specs=in_specs, out_specs=out_specs, check_vma=False)
```

```python
import jax
import jax.numpy as jnp
from jax import lax
from jax.experimental import pallas as pl
from jax.experimental.pallas import tpu as pltpu
from jax.sharding import PartitionSpec as P


def _nbits(n):
    bits = n.bit_length() - 1
    return bits if (1 << bits) == n else None


def _orders(nb):
    if nb == 4:
        return ((0, 1, 2, 3), (2, 0, 1, 3)), ((3, 0, 1, 2), (3, 2, 0, 1))
    rs = tuple(range(nb))
    return (rs, rs), (rs[::-1], rs[::-1])


def _pick(parity, pair, t):
    return jnp.where(parity == 0, pair[0][t], pair[1][t])


def _swap_col(x, row_size, col_size, bits):
    perm = []
    for r in range(row_size):
        b = bits[r % 2]
        for c in range(col_size):
            perm.append((r * col_size + c, r * col_size + (c ^ (1 << b))))
    return lax.ppermute(x, ("row", "col"), perm)


def _swap(x, axis, size, bit):
    perm = [(i, i ^ (1 << bit)) for i in range(size)]
    return lax.ppermute(x, axis, perm)


def gather_row(x):
    size = lax.axis_size("row")
    nb = _nbits(size)
    if nb is None:
        return lax.all_gather(x, "row", axis=0, tiled=True)
    me = lax.axis_index("row")
    have = x[None]
    order = list(range(nb - 1, -1, -1))
    for bit in order:
        got = _swap(have, "row", size, bit)
        mine = (me >> bit) & 1
        lo = jnp.where(mine == 0, have, got)
        hi = jnp.where(mine == 0, got, have)
        have = jnp.stack([lo, hi], axis=0).reshape((-1,) + have.shape[1:])
    have = have.reshape((2,) * nb + x.shape)
    processed = order[::-1]
    perm = [processed.index(b) for b in range(nb - 1, -1, -1)]
    have = jnp.transpose(have, perm + list(range(nb, nb + x.ndim)))
    return have.reshape((size * x.shape[0],) + x.shape[1:])


def scatter_sum_row(x):
    size = lax.axis_size("row")
    nb = _nbits(size)
    if nb is None:
        return lax.psum_scatter(x, "row", scatter_dimension=0, tiled=True)
    me = lax.axis_index("row")
    data = x.reshape((2,) * nb + (x.shape[0] // size,) + x.shape[1:])
    axes_bits = list(range(nb - 1, -1, -1))
    for bit in range(nb):
        a = axes_bits.index(bit)
        mine = (me >> bit) & 1
        keep = lax.dynamic_index_in_dim(data, mine, axis=a, keepdims=False)
        other = lax.dynamic_index_in_dim(data, 1 - mine, axis=a, keepdims=False)
        data = keep + _swap(other, "row", size, bit)
        axes_bits.pop(a)
    return data


def gather_col(x, order):
    row_size = lax.axis_size("row")
    col_size = lax.axis_size("col")
    nb = len(order[0])
    me = lax.axis_index("col")
    parity = lax.axis_index("row") % 2
    have = x[None]
    for t in range(nb):
        got = _swap_col(have, row_size, col_size, (order[0][t], order[1][t]))
        mine = (me >> _pick(parity, order, t)) & 1
        lo = jnp.where(mine == 0, have, got)
        hi = jnp.where(mine == 0, got, have)
        have = jnp.stack([lo, hi], axis=0).reshape((-1,) + have.shape[1:])
    return have


def scatter_sum_col(data, order):
    row_size = lax.axis_size("row")
    col_size = lax.axis_size("col")
    nb = len(order[0])
    me = lax.axis_index("col")
    parity = lax.axis_index("row") % 2
    for t in range(nb):
        mine = (me >> _pick(parity, order, t)) & 1
        keep = lax.dynamic_index_in_dim(data, mine, axis=0, keepdims=False)
        other = lax.dynamic_index_in_dim(data, 1 - mine, axis=0, keepdims=False)
        data = keep + _swap_col(other, row_size, col_size, (order[0][t], order[1][t]))
    return data


def _chunk(slots):
    return 32 if slots % 32 == 0 else slots


def along_call(rows, cols, cnt, values, group, nrb, fwd_index):
    slots, side, _ = values.shape
    width = group.shape[-1]
    k = _chunk(slots)

    def kernel(rows_ref, cols_ref, cnt_ref, vals_ref, grp_ref, out_ref):
        i = pl.program_id(0)
        n = jnp.clip(cnt_ref[0], 0, slots)

        @pl.when(i == 0)
        def _():
            out_ref[...] = jnp.zeros(out_ref.shape, out_ref.dtype)

        @pl.when(i * k < n)
        def _():
            for t in range(k):
                s = i * k + t
                tile = jnp.where(s < n, vals_ref[t], jnp.zeros((side, side), vals_ref.dtype))
                r, c = fwd_index(rows_ref[s], cols_ref[s])
                out_ref[r] += jnp.dot(tile, grp_ref[c], preferred_element_type=jnp.float32)

    def vals_map(i, rows_ref, cols_ref, cnt_ref):
        last = jnp.clip(cnt_ref[0] - 1, 0, slots - 1) // k
        return (jnp.minimum(i, last), 0, 0)

    spec = pltpu.PrefetchScalarGridSpec(
        num_scalar_prefetch=3,
        grid=(slots // k,),
        in_specs=[
            pl.BlockSpec((k, side, side), vals_map),
            pl.BlockSpec(group.shape, lambda i, *_: (0, 0, 0)),
        ],
        out_specs=pl.BlockSpec((nrb, side, width), lambda i, *_: (0, 0, 0)),
    )
    return pl.pallas_call(
        kernel,
        grid_spec=spec,
        out_shape=jax.ShapeDtypeStruct((nrb, side, width), jnp.float32),
    )(rows, cols, cnt, values, group)


def against_call(rows, cols, cnt, values, stripe_t, ncb, bwd_index):
    slots, side, _ = values.shape
    width = stripe_t.shape[1]
    k = _chunk(slots)

    def kernel(rows_ref, cols_ref, cnt_ref, vals_ref, st_ref, out_ref):
        i = pl.program_id(0)
        n = jnp.clip(cnt_ref[0], 0, slots)

        @pl.when(i == 0)
        def _():
            out_ref[...] = jnp.zeros(out_ref.shape, out_ref.dtype)

        @pl.when(i * k < n)
        def _():
            for t in range(k):
                s = i * k + t
                tile = jnp.where(s < n, vals_ref[t], jnp.zeros((side, side), vals_ref.dtype))
                r, c = bwd_index(rows_ref[s], cols_ref[s])
                out_ref[c] += jnp.dot(st_ref[r], tile, preferred_element_type=jnp.float32)

    def vals_map(i, rows_ref, cols_ref, cnt_ref):
        last = jnp.clip(cnt_ref[0] - 1, 0, slots - 1) // k
        return (jnp.minimum(i, last), 0, 0)

    spec = pltpu.PrefetchScalarGridSpec(
        num_scalar_prefetch=3,
        grid=(slots // k,),
        in_specs=[
            pl.BlockSpec((k, side, side), vals_map),
            pl.BlockSpec(stripe_t.shape, lambda i, *_: (0, 0, 0)),
        ],
        out_specs=pl.BlockSpec((ncb, width, side), lambda i, *_: (0, 0, 0)),
    )
    return pl.pallas_call(
        kernel,
        grid_spec=spec,
        out_shape=jax.ShapeDtypeStruct((ncb, width, side), jnp.float32),
    )(rows, cols, cnt, values, stripe_t)


def local(features, tile_vals, tile_rows, tile_cols, tile_count, w_fwd, w_bwd):
    row_size = lax.axis_size("row")
    col_size = lax.axis_size("col")
    values = tile_vals[0, 0]
    slots = values.shape[0]
    side = values.shape[1]
    nodes_here = features.shape[0]
    nbc = nodes_here // side
    width = features.shape[1]
    nrb = col_size * nbc
    ncb = row_size * nbc
    parity = lax.axis_index("row") % 2

    rows = tile_rows.reshape(slots)
    cols = tile_cols.reshape(slots)
    cnt = tile_count.reshape(1)

    nb = _nbits(col_size)
    if nb is not None:
        rs_order, ag_order = _orders(nb)

    def block_pos(rowblk, order, msb_first):
        if nb is None:
            return rowblk
        par = lax.axis_index("row") % 2
        dest = rowblk // nbc
        pos = 0
        for t in range(nb):
            bit = (dest >> _pick(par, order, t)) & 1
            pos = pos + (bit << ((nb - 1 - t) if msb_first else t))
        return pos * nbc + rowblk % nbc

    def fwd_index(r, c):
        r = jnp.clip(r, 0, nrb - 1)
        c = jnp.clip(c, 0, ncb - 1)
        return block_pos(r, rs_order if nb is not None else None, True), c

    def bwd_index(r, c):
        r = jnp.clip(r, 0, nrb - 1)
        c = jnp.clip(c, 0, ncb - 1)
        return block_pos(r, ag_order if nb is not None else None, False), c

    group = gather_row(features).reshape(ncb, side, width)
    fwd_parts = along_call(rows, cols, cnt, values, group, nrb, fwd_index)

    mine_t = jnp.transpose(features.reshape(nbc, side, width), (0, 2, 1))
    mine_t, fwd_parts = lax.optimization_barrier((mine_t, fwd_parts))
    if nb is not None:
        stripe_t = gather_col(mine_t, ag_order).reshape(nrb, width, side)
        along = scatter_sum_col(fwd_parts.reshape((2,) * nb + (nbc, side, width)), rs_order)
    else:
        stripe_t = lax.all_gather(mine_t, "col", axis=0, tiled=True)
        along = lax.psum_scatter(fwd_parts, "col", scatter_dimension=0, tiled=True)

    bwd_t = against_call(rows, cols, cnt, values, stripe_t, ncb, bwd_index)
    against_t = scatter_sum_row(bwd_t)
    against = jnp.transpose(against_t, (0, 2, 1))

    along = along.reshape(-1, width)
    against = against.reshape(-1, width)
    result = jnp.dot(along, w_fwd.astype(jnp.float32), precision=lax.Precision.HIGHEST)
    result = result + jnp.dot(against, w_bwd.astype(jnp.float32), precision=lax.Precision.HIGHEST)
    return result.astype(jnp.bfloat16)


def solution(mesh):
    in_specs = (
        P(("row", "col"), None),
        P("row", "col", None, None, None),
        P("row", "col", None),
        P("row", "col", None),
        P("row", "col"),
        P(),
        P(),
    )
    out_specs = P(("row", "col"), None)
    return jax.shard_map(local, mesh=mesh, in_specs=in_specs, out_specs=out_specs, check_vma=False)
```

```python
import jax
import jax.numpy as jnp
from jax import lax
from jax.experimental import pallas as pl
from jax.experimental.pallas import tpu as pltpu
from jax.sharding import PartitionSpec as P


def _nbits(n):
    bits = n.bit_length() - 1
    return bits if (1 << bits) == n else None


def _orders(nb):
    if nb == 4:
        return ((0, 1, 2, 3), (2, 0, 1, 3)), ((3, 0, 1, 2), (3, 2, 0, 1))
    rs = tuple(range(nb))
    return (rs, rs), (rs[::-1], rs[::-1])


def _pick(parity, pair, t):
    return jnp.where(parity == 0, pair[0][t], pair[1][t])


def _swap_col(x, row_size, col_size, bits):
    perm = []
    for r in range(row_size):
        b = bits[r % 2]
        for c in range(col_size):
            perm.append((r * col_size + c, r * col_size + (c ^ (1 << b))))
    return lax.ppermute(x, ("row", "col"), perm)


def _swap(x, axis, size, bit):
    perm = [(i, i ^ (1 << bit)) for i in range(size)]
    return lax.ppermute(x, axis, perm)


def gather_row(x):
    size = lax.axis_size("row")
    nb = _nbits(size)
    if nb is None:
        return lax.all_gather(x, "row", axis=0, tiled=True)
    me = lax.axis_index("row")
    have = x[None]
    order = list(range(nb - 1, -1, -1))
    for bit in order:
        got = _swap(have, "row", size, bit)
        mine = (me >> bit) & 1
        lo = jnp.where(mine == 0, have, got)
        hi = jnp.where(mine == 0, got, have)
        have = jnp.stack([lo, hi], axis=0).reshape((-1,) + have.shape[1:])
    have = have.reshape((2,) * nb + x.shape)
    processed = order[::-1]
    perm = [processed.index(b) for b in range(nb - 1, -1, -1)]
    have = jnp.transpose(have, perm + list(range(nb, nb + x.ndim)))
    return have.reshape((size * x.shape[0],) + x.shape[1:])


def scatter_sum_row(x):
    size = lax.axis_size("row")
    nb = _nbits(size)
    if nb is None:
        return lax.psum_scatter(x, "row", scatter_dimension=0, tiled=True)
    me = lax.axis_index("row")
    data = x.reshape((2,) * nb + (x.shape[0] // size,) + x.shape[1:])
    axes_bits = list(range(nb - 1, -1, -1))
    for bit in range(nb):
        a = axes_bits.index(bit)
        mine = (me >> bit) & 1
        keep = lax.dynamic_index_in_dim(data, mine, axis=a, keepdims=False)
        other = lax.dynamic_index_in_dim(data, 1 - mine, axis=a, keepdims=False)
        data = keep + _swap(other, "row", size, bit)
        axes_bits.pop(a)
    return data


def gather_col(x, order):
    row_size = lax.axis_size("row")
    col_size = lax.axis_size("col")
    nb = len(order[0])
    me = lax.axis_index("col")
    parity = lax.axis_index("row") % 2
    have = x[None]
    for t in range(nb):
        got = _swap_col(have, row_size, col_size, (order[0][t], order[1][t]))
        mine = (me >> _pick(parity, order, t)) & 1
        lo = jnp.where(mine == 0, have, got)
        hi = jnp.where(mine == 0, got, have)
        have = jnp.stack([lo, hi], axis=0).reshape((-1,) + have.shape[1:])
    return have


def scatter_sum_col(data, order, first=0, stop=None):
    row_size = lax.axis_size("row")
    col_size = lax.axis_size("col")
    nb = len(order[0])
    me = lax.axis_index("col")
    parity = lax.axis_index("row") % 2
    for t in range(first, nb if stop is None else stop):
        mine = (me >> _pick(parity, order, t)) & 1
        keep = lax.dynamic_index_in_dim(data, mine, axis=0, keepdims=False)
        other = lax.dynamic_index_in_dim(data, 1 - mine, axis=0, keepdims=False)
        data = keep + _swap_col(other, row_size, col_size, (order[0][t], order[1][t]))
    return data


def _chunk(slots):
    return 32 if slots % 32 == 0 else slots


def along_call(rows, cols, cnt, values, group, nrb, fwd_index):
    slots, side, _ = values.shape
    width = group.shape[-1]
    k = _chunk(slots)

    def kernel(rows_ref, cols_ref, cnt_ref, vals_ref, grp_ref, out_ref):
        i = pl.program_id(0)
        n = jnp.clip(cnt_ref[0], 0, slots)

        @pl.when(i == 0)
        def _():
            out_ref[...] = jnp.zeros(out_ref.shape, out_ref.dtype)

        @pl.when(i * k < n)
        def _():
            for t in range(k):
                s = i * k + t
                tile = jnp.where(s < n, vals_ref[t], jnp.zeros((side, side), vals_ref.dtype))
                r, c = fwd_index(rows_ref[s], cols_ref[s])
                out_ref[r] += jnp.dot(tile, grp_ref[c], preferred_element_type=jnp.float32)

    def vals_map(i, rows_ref, cols_ref, cnt_ref):
        last = jnp.clip(cnt_ref[0] - 1, 0, slots - 1) // k
        return (jnp.minimum(i, last), 0, 0)

    spec = pltpu.PrefetchScalarGridSpec(
        num_scalar_prefetch=3,
        grid=(slots // k,),
        in_specs=[
            pl.BlockSpec((k, side, side), vals_map),
            pl.BlockSpec(group.shape, lambda i, *_: (0, 0, 0)),
        ],
        out_specs=pl.BlockSpec((nrb, side, width), lambda i, *_: (0, 0, 0)),
    )
    return pl.pallas_call(
        kernel,
        grid_spec=spec,
        out_shape=jax.ShapeDtypeStruct((nrb, side, width), jnp.float32),
    )(rows, cols, cnt, values, group)


def against_call(rows, cols, cnt, values, stripe_t, ncb, bwd_index):
    slots, side, _ = values.shape
    width = stripe_t.shape[1]
    k = _chunk(slots)

    def kernel(rows_ref, cols_ref, cnt_ref, vals_ref, st_ref, out_ref):
        i = pl.program_id(0)
        n = jnp.clip(cnt_ref[0], 0, slots)

        @pl.when(i == 0)
        def _():
            out_ref[...] = jnp.zeros(out_ref.shape, out_ref.dtype)

        @pl.when(i * k < n)
        def _():
            for t in range(k):
                s = i * k + t
                tile = jnp.where(s < n, vals_ref[t], jnp.zeros((side, side), vals_ref.dtype))
                r, c = bwd_index(rows_ref[s], cols_ref[s])
                out_ref[c] += jnp.dot(st_ref[r], tile, preferred_element_type=jnp.float32)

    def vals_map(i, rows_ref, cols_ref, cnt_ref):
        last = jnp.clip(cnt_ref[0] - 1, 0, slots - 1) // k
        return (jnp.minimum(i, last), 0, 0)

    spec = pltpu.PrefetchScalarGridSpec(
        num_scalar_prefetch=3,
        grid=(slots // k,),
        in_specs=[
            pl.BlockSpec((k, side, side), vals_map),
            pl.BlockSpec(stripe_t.shape, lambda i, *_: (0, 0, 0)),
        ],
        out_specs=pl.BlockSpec((ncb, width, side), lambda i, *_: (0, 0, 0)),
    )
    return pl.pallas_call(
        kernel,
        grid_spec=spec,
        out_shape=jax.ShapeDtypeStruct((ncb, width, side), jnp.float32),
    )(rows, cols, cnt, values, stripe_t)


def local(features, tile_vals, tile_rows, tile_cols, tile_count, w_fwd, w_bwd):
    row_size = lax.axis_size("row")
    col_size = lax.axis_size("col")
    values = tile_vals[0, 0]
    slots = values.shape[0]
    side = values.shape[1]
    nodes_here = features.shape[0]
    nbc = nodes_here // side
    width = features.shape[1]
    nrb = col_size * nbc
    ncb = row_size * nbc
    parity = lax.axis_index("row") % 2

    rows = tile_rows.reshape(slots)
    cols = tile_cols.reshape(slots)
    cnt = tile_count.reshape(1)

    nb = _nbits(col_size)
    if nb is not None:
        rs_order, ag_order = _orders(nb)

    def block_pos(rowblk, order, msb_first):
        if nb is None:
            return rowblk
        par = lax.axis_index("row") % 2
        dest = rowblk // nbc
        pos = 0
        for t in range(nb):
            bit = (dest >> _pick(par, order, t)) & 1
            pos = pos + (bit << ((nb - 1 - t) if msb_first else t))
        return pos * nbc + rowblk % nbc

    def fwd_index(r, c):
        r = jnp.clip(r, 0, nrb - 1)
        c = jnp.clip(c, 0, ncb - 1)
        return block_pos(r, rs_order if nb is not None else None, True), c

    def bwd_index(r, c):
        r = jnp.clip(r, 0, nrb - 1)
        c = jnp.clip(c, 0, ncb - 1)
        return block_pos(r, ag_order if nb is not None else None, False), c

    group = gather_row(features).reshape(ncb, side, width)
    fwd_parts = along_call(rows, cols, cnt, values, group, nrb, fwd_index)

    mine_t = jnp.transpose(features.reshape(nbc, side, width), (0, 2, 1))
    if nb is not None:
        along = scatter_sum_col(fwd_parts.reshape((2,) * nb + (nbc, side, width)), rs_order, 0, 1)
        mine_t, along = lax.optimization_barrier((mine_t, along))
        stripe_t = gather_col(mine_t, ag_order).reshape(nrb, width, side)
        along = scatter_sum_col(along, rs_order, 1)
    else:
        stripe_t = lax.all_gather(mine_t, "col", axis=0, tiled=True)
        along = lax.psum_scatter(fwd_parts, "col", scatter_dimension=0, tiled=True)

    bwd_t = against_call(rows, cols, cnt, values, stripe_t, ncb, bwd_index)
    against_t = scatter_sum_row(bwd_t)
    against = jnp.transpose(against_t, (0, 2, 1))

    along = along.reshape(-1, width)
    against = against.reshape(-1, width)
    result = jnp.dot(along, w_fwd.astype(jnp.float32), precision=lax.Precision.HIGHEST)
    result = result + jnp.dot(against, w_bwd.astype(jnp.float32), precision=lax.Precision.HIGHEST)
    return result.astype(jnp.bfloat16)


def solution(mesh):
    in_specs = (
        P(("row", "col"), None),
        P("row", "col", None, None, None),
        P("row", "col", None),
        P("row", "col", None),
        P("row", "col"),
        P(),
        P(),
    )
    out_specs = P(("row", "col"), None)
    return jax.shard_map(local, mesh=mesh, in_specs=in_specs, out_specs=out_specs, check_vma=False)
```

```python
import jax
import jax.numpy as jnp
from jax import lax
from jax.experimental import pallas as pl
from jax.experimental.pallas import tpu as pltpu
from jax.sharding import PartitionSpec as P


def _nbits(n):
    bits = n.bit_length() - 1
    return bits if (1 << bits) == n else None


def _orders(nb):
    if nb == 4:
        return ((0, 1, 2, 3), (2, 0, 1, 3)), ((3, 0, 1, 2), (3, 2, 0, 1))
    rs = tuple(range(nb))
    return (rs, rs), (rs[::-1], rs[::-1])


def _pick(parity, pair, t):
    return jnp.where(parity == 0, pair[0][t], pair[1][t])


def _swap_col(x, row_size, col_size, bits):
    perm = []
    for r in range(row_size):
        b = bits[r % 2]
        for c in range(col_size):
            perm.append((r * col_size + c, r * col_size + (c ^ (1 << b))))
    return lax.ppermute(x, ("row", "col"), perm)


def _swap(x, axis, size, bit):
    perm = [(i, i ^ (1 << bit)) for i in range(size)]
    return lax.ppermute(x, axis, perm)


def gather_row(x):
    size = lax.axis_size("row")
    nb = _nbits(size)
    if nb is None:
        return lax.all_gather(x, "row", axis=0, tiled=True)
    me = lax.axis_index("row")
    have = x[None]
    order = list(range(nb - 1, -1, -1))
    for bit in order:
        got = _swap(have, "row", size, bit)
        mine = (me >> bit) & 1
        lo = jnp.where(mine == 0, have, got)
        hi = jnp.where(mine == 0, got, have)
        have = jnp.stack([lo, hi], axis=0).reshape((-1,) + have.shape[1:])
    have = have.reshape((2,) * nb + x.shape)
    processed = order[::-1]
    perm = [processed.index(b) for b in range(nb - 1, -1, -1)]
    have = jnp.transpose(have, perm + list(range(nb, nb + x.ndim)))
    return have.reshape((size * x.shape[0],) + x.shape[1:])


def scatter_sum_row(x):
    size = lax.axis_size("row")
    nb = _nbits(size)
    if nb is None:
        return lax.psum_scatter(x, "row", scatter_dimension=0, tiled=True)
    me = lax.axis_index("row")
    data = x.reshape((2,) * nb + (x.shape[0] // size,) + x.shape[1:])
    axes_bits = list(range(nb - 1, -1, -1))
    for bit in range(nb):
        a = axes_bits.index(bit)
        mine = (me >> bit) & 1
        keep = lax.dynamic_index_in_dim(data, mine, axis=a, keepdims=False)
        other = lax.dynamic_index_in_dim(data, 1 - mine, axis=a, keepdims=False)
        data = keep + _swap(other, "row", size, bit)
        axes_bits.pop(a)
    return data


def gather_col(x, order):
    row_size = lax.axis_size("row")
    col_size = lax.axis_size("col")
    nb = len(order[0])
    me = lax.axis_index("col")
    parity = lax.axis_index("row") % 2
    have = x[None]
    for t in range(nb):
        got = _swap_col(have, row_size, col_size, (order[0][t], order[1][t]))
        mine = (me >> _pick(parity, order, t)) & 1
        lo = jnp.where(mine == 0, have, got)
        hi = jnp.where(mine == 0, got, have)
        have = jnp.stack([lo, hi], axis=0).reshape((-1,) + have.shape[1:])
    return have


def scatter_sum_col(data, order):
    row_size = lax.axis_size("row")
    col_size = lax.axis_size("col")
    nb = len(order[0])
    me = lax.axis_index("col")
    parity = lax.axis_index("row") % 2
    for t in range(nb):
        mine = (me >> _pick(parity, order, t)) & 1
        keep = lax.dynamic_index_in_dim(data, mine, axis=0, keepdims=False)
        other = lax.dynamic_index_in_dim(data, 1 - mine, axis=0, keepdims=False)
        bits = (order[0][t], order[1][t])
        if other.shape[0] % 2 == 0:
            half = other.shape[0] // 2
            got = jnp.concatenate(
                [_swap_col(other[:half], row_size, col_size, bits),
                 _swap_col(other[half:], row_size, col_size, bits)], axis=0)
        else:
            got = _swap_col(other, row_size, col_size, bits)
        data = keep + got
    return data


def _chunk(slots):
    return 32 if slots % 32 == 0 else slots


def along_call(rows, cols, cnt, values, group, nrb):
    slots, side, _ = values.shape
    width = group.shape[-1]
    k = _chunk(slots)

    def kernel(rows_ref, cols_ref, cnt_ref, vals_ref, grp_ref, out_ref):
        i = pl.program_id(0)
        n = cnt_ref[0]

        @pl.when(i == 0)
        def _():
            out_ref[...] = jnp.zeros(out_ref.shape, out_ref.dtype)

        @pl.when(i * k < n)
        def _():
            for t in range(k):
                s = i * k + t
                tile = jnp.where(s < n, vals_ref[t], jnp.zeros((side, side), vals_ref.dtype))
                r = rows_ref[s]
                c = cols_ref[s]
                out_ref[r] += jnp.dot(tile, grp_ref[c], preferred_element_type=jnp.float32)

    def vals_map(i, rows_ref, cols_ref, cnt_ref):
        last = jnp.maximum(cnt_ref[0] - 1, 0) // k
        return (jnp.minimum(i, last), 0, 0)

    spec = pltpu.PrefetchScalarGridSpec(
        num_scalar_prefetch=3,
        grid=(slots // k,),
        in_specs=[
            pl.BlockSpec((k, side, side), vals_map),
            pl.BlockSpec(group.shape, lambda i, *_: (0, 0, 0)),
        ],
        out_specs=pl.BlockSpec((nrb, side, width), lambda i, *_: (0, 0, 0)),
    )
    return pl.pallas_call(
        kernel,
        grid_spec=spec,
        out_shape=jax.ShapeDtypeStruct((nrb, side, width), jnp.float32),
    )(rows, cols, cnt, values, group)


def against_call(rows, cols, cnt, values, stripe_t, ncb):
    slots, side, _ = values.shape
    width = stripe_t.shape[1]
    k = _chunk(slots)

    def kernel(rows_ref, cols_ref, cnt_ref, vals_ref, st_ref, out_ref):
        i = pl.program_id(0)
        n = cnt_ref[0]

        @pl.when(i == 0)
        def _():
            out_ref[...] = jnp.zeros(out_ref.shape, out_ref.dtype)

        @pl.when(i * k < n)
        def _():
            for t in range(k):
                s = i * k + t
                tile = jnp.where(s < n, vals_ref[t], jnp.zeros((side, side), vals_ref.dtype))
                r = rows_ref[s]
                c = cols_ref[s]
                out_ref[c] += jnp.dot(st_ref[r], tile, preferred_element_type=jnp.float32)

    def vals_map(i, rows_ref, cols_ref, cnt_ref):
        last = jnp.maximum(cnt_ref[0] - 1, 0) // k
        return (jnp.minimum(i, last), 0, 0)

    spec = pltpu.PrefetchScalarGridSpec(
        num_scalar_prefetch=3,
        grid=(slots // k,),
        in_specs=[
            pl.BlockSpec((k, side, side), vals_map),
            pl.BlockSpec(stripe_t.shape, lambda i, *_: (0, 0, 0)),
        ],
        out_specs=pl.BlockSpec((ncb, width, side), lambda i, *_: (0, 0, 0)),
    )
    return pl.pallas_call(
        kernel,
        grid_spec=spec,
        out_shape=jax.ShapeDtypeStruct((ncb, width, side), jnp.float32),
    )(rows, cols, cnt, values, stripe_t)


def local(features, tile_vals, tile_rows, tile_cols, tile_count, w_fwd, w_bwd):
    row_size = lax.axis_size("row")
    col_size = lax.axis_size("col")
    values = tile_vals[0, 0]
    slots = values.shape[0]
    side = values.shape[1]
    nodes_here = features.shape[0]
    nbc = nodes_here // side
    width = features.shape[1]
    nrb = col_size * nbc
    ncb = row_size * nbc
    parity = lax.axis_index("row") % 2

    rowblk = jnp.clip(tile_rows[0, 0], 0, nrb - 1)
    colblk = jnp.clip(tile_cols[0, 0], 0, ncb - 1)
    cnt = jnp.clip(tile_count[0, 0], 0, slots).reshape(1).astype(jnp.int32)

    nb = _nbits(col_size)
    if nb is not None:
        rs_order, ag_order = _orders(nb)
        dest = rowblk // nbc
        sub = rowblk % nbc
        rs_pos = jnp.zeros_like(dest)
        ag_pos = jnp.zeros_like(dest)
        for t in range(nb):
            rs_pos = rs_pos + (((dest >> _pick(parity, rs_order, t)) & 1) << (nb - 1 - t))
            ag_pos = ag_pos + (((dest >> _pick(parity, ag_order, t)) & 1) << t)
        rows_fwd = rs_pos * nbc + sub
        rows_bwd = ag_pos * nbc + sub
    else:
        rows_fwd = rowblk
        rows_bwd = rowblk

    group = gather_row(features).reshape(ncb, side, width)
    fwd_parts = along_call(rows_fwd, colblk, cnt, values, group, nrb)

    mine_t = jnp.transpose(features.reshape(nbc, side, width), (0, 2, 1))
    if nb is not None:
        stripe_t = gather_col(mine_t, ag_order).reshape(nrb, width, side)
        along = scatter_sum_col(fwd_parts.reshape((2,) * nb + (nbc, side, width)), rs_order)
    else:
        stripe_t = lax.all_gather(mine_t, "col", axis=0, tiled=True)
        along = lax.psum_scatter(fwd_parts, "col", scatter_dimension=0, tiled=True)

    bwd_t = against_call(rows_bwd, colblk, cnt, values, stripe_t, ncb)
    against_t = scatter_sum_row(bwd_t)
    against = jnp.transpose(against_t, (0, 2, 1))

    along = along.reshape(-1, width)
    against = against.reshape(-1, width)
    result = jnp.dot(along, w_fwd.astype(jnp.float32), precision=lax.Precision.HIGHEST)
    result = result + jnp.dot(against, w_bwd.astype(jnp.float32), precision=lax.Precision.HIGHEST)
    return result.astype(jnp.bfloat16)


def solution(mesh):
    in_specs = (
        P(("row", "col"), None),
        P("row", "col", None, None, None),
        P("row", "col", None),
        P("row", "col", None),
        P("row", "col"),
        P(),
        P(),
    )
    out_specs = P(("row", "col"), None)
    return jax.shard_map(local, mesh=mesh, in_specs=in_specs, out_specs=out_specs, check_vma=False)
```

```python
import jax
import jax.numpy as jnp
from jax import lax
from jax.experimental import pallas as pl
from jax.experimental.pallas import tpu as pltpu
from jax.sharding import PartitionSpec as P


def _nbits(n):
    bits = n.bit_length() - 1
    return bits if (1 << bits) == n else None


def _orders(nb):
    if nb == 4:
        return ((0, 1, 2, 3), (2, 0, 1, 3)), ((3, 0, 1, 2), (3, 2, 0, 1))
    rs = tuple(range(nb))
    return (rs, rs), (rs[::-1], rs[::-1])


def _pick(parity, pair, t):
    return jnp.where(parity == 0, pair[0][t], pair[1][t])


def _swap_col(x, row_size, col_size, bits):
    perm = []
    for r in range(row_size):
        b = bits[r % 2]
        for c in range(col_size):
            perm.append((r * col_size + c, r * col_size + (c ^ (1 << b))))
    return lax.ppermute(x, ("row", "col"), perm)


def _swap(x, axis, size, bit):
    perm = [(i, i ^ (1 << bit)) for i in range(size)]
    return lax.ppermute(x, axis, perm)


def gather_row(x):
    size = lax.axis_size("row")
    nb = _nbits(size)
    if nb is None:
        return lax.all_gather(x, "row", axis=0, tiled=True)
    me = lax.axis_index("row")
    have = x[None]
    order = list(range(nb - 1, -1, -1))
    for bit in order:
        got = _swap(have, "row", size, bit)
        mine = (me >> bit) & 1
        lo = jnp.where(mine == 0, have, got)
        hi = jnp.where(mine == 0, got, have)
        have = jnp.stack([lo, hi], axis=0).reshape((-1,) + have.shape[1:])
    have = have.reshape((2,) * nb + x.shape)
    processed = order[::-1]
    perm = [processed.index(b) for b in range(nb - 1, -1, -1)]
    have = jnp.transpose(have, perm + list(range(nb, nb + x.ndim)))
    return have.reshape((size * x.shape[0],) + x.shape[1:])


def scatter_sum_row(x):
    size = lax.axis_size("row")
    nb = _nbits(size)
    if nb is None:
        return lax.psum_scatter(x, "row", scatter_dimension=0, tiled=True)
    me = lax.axis_index("row")
    data = x.reshape((2,) * nb + (x.shape[0] // size,) + x.shape[1:])
    axes_bits = list(range(nb - 1, -1, -1))
    for bit in range(nb):
        a = axes_bits.index(bit)
        mine = (me >> bit) & 1
        keep = lax.dynamic_index_in_dim(data, mine, axis=a, keepdims=False)
        other = lax.dynamic_index_in_dim(data, 1 - mine, axis=a, keepdims=False)
        data = keep + _swap(other, "row", size, bit)
        axes_bits.pop(a)
    return data


def gather_col(x, order):
    row_size = lax.axis_size("row")
    col_size = lax.axis_size("col")
    nb = len(order[0])
    me = lax.axis_index("col")
    parity = lax.axis_index("row") % 2
    have = x[None]
    for t in range(nb):
        got = _swap_col(have, row_size, col_size, (order[0][t], order[1][t]))
        mine = (me >> _pick(parity, order, t)) & 1
        lo = jnp.where(mine == 0, have, got)
        hi = jnp.where(mine == 0, got, have)
        have = jnp.stack([lo, hi], axis=0).reshape((-1,) + have.shape[1:])
    return have


def scatter_sum_col(data, order):
    row_size = lax.axis_size("row")
    col_size = lax.axis_size("col")
    nb = len(order[0])
    me = lax.axis_index("col")
    parity = lax.axis_index("row") % 2
    for t in range(nb):
        mine = (me >> _pick(parity, order, t)) & 1
        keep = lax.dynamic_index_in_dim(data, mine, axis=0, keepdims=False)
        other = lax.dynamic_index_in_dim(data, 1 - mine, axis=0, keepdims=False)
        data = keep + _swap_col(other, row_size, col_size, (order[0][t], order[1][t]))
    return data


def _chunk(slots):
    return 32 if slots % 32 == 0 else slots


def along_call(rows, cols, cnt, values, group, nrb):
    slots, side, _ = values.shape
    width = group.shape[-1]
    k = _chunk(slots)

    def kernel(rows_ref, cols_ref, cnt_ref, vals_ref, grp_ref, out_ref):
        i = pl.program_id(0)
        n = cnt_ref[0]

        @pl.when(i == 0)
        def _():
            out_ref[...] = jnp.zeros(out_ref.shape, out_ref.dtype)

        @pl.when(i * k < n)
        def _():
            for t in range(k):
                s = i * k + t
                tile = jnp.where(s < n, vals_ref[t], jnp.zeros((side, side), vals_ref.dtype))
                r = rows_ref[s]
                c = cols_ref[s]
                out_ref[r] += jnp.dot(tile, grp_ref[c], preferred_element_type=jnp.float32)

    def vals_map(i, rows_ref, cols_ref, cnt_ref):
        last = jnp.maximum(cnt_ref[0] - 1, 0) // k
        return (jnp.minimum(i, last), 0, 0)

    spec = pltpu.PrefetchScalarGridSpec(
        num_scalar_prefetch=3,
        grid=(slots // k,),
        in_specs=[
            pl.BlockSpec((k, side, side), vals_map),
            pl.BlockSpec(group.shape, lambda i, *_: (0, 0, 0)),
        ],
        out_specs=pl.BlockSpec((nrb, side, width), lambda i, *_: (0, 0, 0)),
    )
    return pl.pallas_call(
        kernel,
        grid_spec=spec,
        out_shape=jax.ShapeDtypeStruct((nrb, side, width), jnp.float32),
    )(rows, cols, cnt, values, group)


def against_call(rows, cols, cnt, values, stripe_t, ncb):
    slots, side, _ = values.shape
    width = stripe_t.shape[1]
    k = _chunk(slots)

    def kernel(rows_ref, cols_ref, cnt_ref, vals_ref, st_ref, out_ref):
        i = pl.program_id(0)
        n = cnt_ref[0]

        @pl.when(i == 0)
        def _():
            out_ref[...] = jnp.zeros(out_ref.shape, out_ref.dtype)

        @pl.when(i * k < n)
        def _():
            for t in range(k):
                s = i * k + t
                tile = jnp.where(s < n, vals_ref[t], jnp.zeros((side, side), vals_ref.dtype))
                r = rows_ref[s]
                c = cols_ref[s]
                out_ref[c] += jnp.dot(st_ref[r], tile, preferred_element_type=jnp.float32)

    def vals_map(i, rows_ref, cols_ref, cnt_ref):
        last = jnp.maximum(cnt_ref[0] - 1, 0) // k
        return (jnp.minimum(i, last), 0, 0)

    spec = pltpu.PrefetchScalarGridSpec(
        num_scalar_prefetch=3,
        grid=(slots // k,),
        in_specs=[
            pl.BlockSpec((k, side, side), vals_map),
            pl.BlockSpec(stripe_t.shape, lambda i, *_: (0, 0, 0)),
        ],
        out_specs=pl.BlockSpec((ncb, width, side), lambda i, *_: (0, 0, 0)),
    )
    return pl.pallas_call(
        kernel,
        grid_spec=spec,
        out_shape=jax.ShapeDtypeStruct((ncb, width, side), jnp.float32),
    )(rows, cols, cnt, values, stripe_t)


def local(features, tile_vals, tile_rows, tile_cols, tile_count, w_fwd, w_bwd):
    row_size = lax.axis_size("row")
    col_size = lax.axis_size("col")
    values = tile_vals[0, 0]
    slots = values.shape[0]
    side = values.shape[1]
    nodes_here = features.shape[0]
    nbc = nodes_here // side
    width = features.shape[1]
    nrb = col_size * nbc
    ncb = row_size * nbc
    parity = lax.axis_index("row") % 2

    rowblk = jnp.clip(tile_rows[0, 0], 0, nrb - 1)
    colblk = jnp.clip(tile_cols[0, 0], 0, ncb - 1)
    cnt = jnp.clip(tile_count[0, 0], 0, slots).reshape(1).astype(jnp.int32)

    nb = _nbits(col_size)
    if nb is not None:
        rs_order, ag_order = _orders(nb)
        dest = rowblk // nbc
        sub = rowblk % nbc
        rs_pos = jnp.zeros_like(dest)
        ag_pos = jnp.zeros_like(dest)
        for t in range(nb):
            rs_pos = rs_pos + (((dest >> _pick(parity, rs_order, t)) & 1) << (nb - 1 - t))
            ag_pos = ag_pos + (((dest >> _pick(parity, ag_order, t)) & 1) << t)
        rows_fwd = rs_pos * nbc + sub
        rows_bwd = ag_pos * nbc + sub
    else:
        rows_fwd = rowblk
        rows_bwd = rowblk

    group = gather_row(features).reshape(ncb, side, width)
    fwd_parts = along_call(rows_fwd, colblk, cnt, values, group, nrb)

    mine_t = jnp.transpose(features.reshape(nbc, side, width), (0, 2, 1))
    if nb is not None:
        stripe_t = gather_col(mine_t, ag_order).reshape(nrb, width, side)
        cut = side // 4
        parts = fwd_parts.reshape((2,) * nb + (nbc, side, width))
        quarter = parts[..., :cut, :]
        canon = []
        for p in range(2):
            order = rs_order[p]
            perm = [order.index(b) for b in range(nb - 1, -1, -1)]
            canon.append(jnp.transpose(quarter, perm + list(range(nb, nb + 3))))
        quarter = jnp.where(parity == 0, canon[0], canon[1]).reshape(-1, width)
        sc_part = lax.psum_scatter(quarter, "col", scatter_dimension=0, tiled=True)
        rest = scatter_sum_col(parts[..., cut:, :], rs_order)
        along = jnp.concatenate([sc_part.reshape(nbc, cut, width), rest], axis=1)
    else:
        stripe_t = lax.all_gather(mine_t, "col", axis=0, tiled=True)
        along = lax.psum_scatter(fwd_parts, "col", scatter_dimension=0, tiled=True)

    bwd_t = against_call(rows_bwd, colblk, cnt, values, stripe_t, ncb)
    against_t = scatter_sum_row(bwd_t)
    against = jnp.transpose(against_t, (0, 2, 1))

    along = along.reshape(-1, width)
    against = against.reshape(-1, width)
    result = jnp.dot(along, w_fwd.astype(jnp.float32), precision=lax.Precision.HIGHEST)
    result = result + jnp.dot(against, w_bwd.astype(jnp.float32), precision=lax.Precision.HIGHEST)
    return result.astype(jnp.bfloat16)


def solution(mesh):
    in_specs = (
        P(("row", "col"), None),
        P("row", "col", None, None, None),
        P("row", "col", None),
        P("row", "col", None),
        P("row", "col"),
        P(),
        P(),
    )
    out_specs = P(("row", "col"), None)
    return jax.shard_map(local, mesh=mesh, in_specs=in_specs, out_specs=out_specs, check_vma=False)
```

```python
import jax
import jax.numpy as jnp
from jax import lax
from jax.experimental import pallas as pl
from jax.experimental.pallas import tpu as pltpu
from jax.sharding import PartitionSpec as P


def _nbits(n):
    bits = n.bit_length() - 1
    return bits if (1 << bits) == n else None


def _orders(nb):
    if nb == 4:
        return ((0, 1, 2, 3), (2, 0, 1, 3)), ((3, 0, 1, 2), (3, 2, 0, 1))
    rs = tuple(range(nb))
    return (rs, rs), (rs[::-1], rs[::-1])


def _pick(parity, pair, t):
    return jnp.where(parity == 0, pair[0][t], pair[1][t])


def _swap_col(x, row_size, col_size, bits):
    perm = []
    for r in range(row_size):
        b = bits[r % 2]
        for c in range(col_size):
            perm.append((r * col_size + c, r * col_size + (c ^ (1 << b))))
    return lax.ppermute(x, ("row", "col"), perm)


def _swap(x, axis, size, bit):
    perm = [(i, i ^ (1 << bit)) for i in range(size)]
    return lax.ppermute(x, axis, perm)


def gather_row(x):
    size = lax.axis_size("row")
    nb = _nbits(size)
    if nb is None:
        return lax.all_gather(x, "row", axis=0, tiled=True)
    me = lax.axis_index("row")
    have = x[None]
    order = list(range(nb - 1, -1, -1))
    for bit in order:
        got = _swap(have, "row", size, bit)
        mine = (me >> bit) & 1
        lo = jnp.where(mine == 0, have, got)
        hi = jnp.where(mine == 0, got, have)
        have = jnp.stack([lo, hi], axis=0).reshape((-1,) + have.shape[1:])
    have = have.reshape((2,) * nb + x.shape)
    processed = order[::-1]
    perm = [processed.index(b) for b in range(nb - 1, -1, -1)]
    have = jnp.transpose(have, perm + list(range(nb, nb + x.ndim)))
    return have.reshape((size * x.shape[0],) + x.shape[1:])


def scatter_sum_row(x):
    size = lax.axis_size("row")
    nb = _nbits(size)
    if nb is None:
        return lax.psum_scatter(x, "row", scatter_dimension=0, tiled=True)
    me = lax.axis_index("row")
    data = x.reshape((2,) * nb + (x.shape[0] // size,) + x.shape[1:])
    axes_bits = list(range(nb - 1, -1, -1))
    for bit in range(nb):
        a = axes_bits.index(bit)
        mine = (me >> bit) & 1
        keep = lax.dynamic_index_in_dim(data, mine, axis=a, keepdims=False)
        other = lax.dynamic_index_in_dim(data, 1 - mine, axis=a, keepdims=False)
        data = keep + _swap(other, "row", size, bit)
        axes_bits.pop(a)
    return data


def gather_col(x, order):
    row_size = lax.axis_size("row")
    col_size = lax.axis_size("col")
    nb = len(order[0])
    me = lax.axis_index("col")
    parity = lax.axis_index("row") % 2
    have = x[None]
    for t in range(nb):
        got = _swap_col(have, row_size, col_size, (order[0][t], order[1][t]))
        mine = (me >> _pick(parity, order, t)) & 1
        lo = jnp.where(mine == 0, have, got)
        hi = jnp.where(mine == 0, got, have)
        have = jnp.stack([lo, hi], axis=0).reshape((-1,) + have.shape[1:])
    return have


def scatter_sum_col(data, order):
    row_size = lax.axis_size("row")
    col_size = lax.axis_size("col")
    nb = len(order[0])
    me = lax.axis_index("col")
    parity = lax.axis_index("row") % 2
    for t in range(nb):
        mine = (me >> _pick(parity, order, t)) & 1
        keep = lax.dynamic_index_in_dim(data, mine, axis=0, keepdims=False)
        other = lax.dynamic_index_in_dim(data, 1 - mine, axis=0, keepdims=False)
        data = keep + _swap_col(other, row_size, col_size, (order[0][t], order[1][t]))
    return data


def _chunk(slots):
    return 64 if slots % 64 == 0 else slots


def along_call(rows, cols, cnt, values, group, nrb):
    slots, side, _ = values.shape
    width = group.shape[-1]
    k = _chunk(slots)

    def kernel(rows_ref, cols_ref, cnt_ref, vals_ref, grp_ref, out_ref):
        i = pl.program_id(0)
        n = cnt_ref[0]

        @pl.when(i == 0)
        def _():
            out_ref[...] = jnp.zeros(out_ref.shape, out_ref.dtype)

        @pl.when(i * k < n)
        def _():
            for t in range(k):
                s = i * k + t
                tile = jnp.where(s < n, vals_ref[t], jnp.zeros((side, side), vals_ref.dtype))
                r = rows_ref[s]
                c = cols_ref[s]
                out_ref[r] += jnp.dot(tile, grp_ref[c], preferred_element_type=jnp.float32)

    def vals_map(i, rows_ref, cols_ref, cnt_ref):
        last = jnp.maximum(cnt_ref[0] - 1, 0) // k
        return (jnp.minimum(i, last), 0, 0)

    spec = pltpu.PrefetchScalarGridSpec(
        num_scalar_prefetch=3,
        grid=(slots // k,),
        in_specs=[
            pl.BlockSpec((k, side, side), vals_map),
            pl.BlockSpec(group.shape, lambda i, *_: (0, 0, 0)),
        ],
        out_specs=pl.BlockSpec((nrb, side, width), lambda i, *_: (0, 0, 0)),
    )
    return pl.pallas_call(
        kernel,
        grid_spec=spec,
        out_shape=jax.ShapeDtypeStruct((nrb, side, width), jnp.float32),
    )(rows, cols, cnt, values, group)


def against_call(rows, cols, cnt, values, stripe_t, ncb):
    slots, side, _ = values.shape
    width = stripe_t.shape[1]
    k = _chunk(slots)

    def kernel(rows_ref, cols_ref, cnt_ref, vals_ref, st_ref, out_ref):
        i = pl.program_id(0)
        n = cnt_ref[0]

        @pl.when(i == 0)
        def _():
            out_ref[...] = jnp.zeros(out_ref.shape, out_ref.dtype)

        @pl.when(i * k < n)
        def _():
            for t in range(k):
                s = i * k + t
                tile = jnp.where(s < n, vals_ref[t], jnp.zeros((side, side), vals_ref.dtype))
                r = rows_ref[s]
                c = cols_ref[s]
                out_ref[c] += jnp.dot(st_ref[r], tile, preferred_element_type=jnp.float32)

    def vals_map(i, rows_ref, cols_ref, cnt_ref):
        last = jnp.maximum(cnt_ref[0] - 1, 0) // k
        return (jnp.minimum(i, last), 0, 0)

    spec = pltpu.PrefetchScalarGridSpec(
        num_scalar_prefetch=3,
        grid=(slots // k,),
        in_specs=[
            pl.BlockSpec((k, side, side), vals_map),
            pl.BlockSpec(stripe_t.shape, lambda i, *_: (0, 0, 0)),
        ],
        out_specs=pl.BlockSpec((ncb, width, side), lambda i, *_: (0, 0, 0)),
    )
    return pl.pallas_call(
        kernel,
        grid_spec=spec,
        out_shape=jax.ShapeDtypeStruct((ncb, width, side), jnp.float32),
    )(rows, cols, cnt, values, stripe_t)


def local(features, tile_vals, tile_rows, tile_cols, tile_count, w_fwd, w_bwd):
    row_size = lax.axis_size("row")
    col_size = lax.axis_size("col")
    values = tile_vals[0, 0]
    slots = values.shape[0]
    side = values.shape[1]
    nodes_here = features.shape[0]
    nbc = nodes_here // side
    width = features.shape[1]
    nrb = col_size * nbc
    ncb = row_size * nbc
    parity = lax.axis_index("row") % 2

    rowblk = jnp.clip(tile_rows[0, 0], 0, nrb - 1)
    colblk = jnp.clip(tile_cols[0, 0], 0, ncb - 1)
    cnt = jnp.clip(tile_count[0, 0], 0, slots).reshape(1).astype(jnp.int32)

    nb = _nbits(col_size)
    if nb is not None:
        rs_order, ag_order = _orders(nb)
        dest = rowblk // nbc
        sub = rowblk % nbc
        rs_pos = jnp.zeros_like(dest)
        ag_pos = jnp.zeros_like(dest)
        for t in range(nb):
            rs_pos = rs_pos + (((dest >> _pick(parity, rs_order, t)) & 1) << (nb - 1 - t))
            ag_pos = ag_pos + (((dest >> _pick(parity, ag_order, t)) & 1) << t)
        rows_fwd = rs_pos * nbc + sub
        rows_bwd = ag_pos * nbc + sub
    else:
        rows_fwd = rowblk
        rows_bwd = rowblk

    group = gather_row(features).reshape(ncb, side, width)
    fwd_parts = along_call(rows_fwd, colblk, cnt, values, group, nrb)

    mine_t = jnp.transpose(features.reshape(nbc, side, width), (0, 2, 1))
    if nb is not None:
        stripe_t = gather_col(mine_t, ag_order).reshape(nrb, width, side)
        along = scatter_sum_col(fwd_parts.reshape((2,) * nb + (nbc, side, width)), rs_order)
    else:
        stripe_t = lax.all_gather(mine_t, "col", axis=0, tiled=True)
        along = lax.psum_scatter(fwd_parts, "col", scatter_dimension=0, tiled=True)

    bwd_t = against_call(rows_bwd, colblk, cnt, values, stripe_t, ncb)
    against_t = scatter_sum_row(bwd_t)
    against = jnp.transpose(against_t, (0, 2, 1))

    along = along.reshape(-1, width)
    against = against.reshape(-1, width)
    result = jnp.dot(along, w_fwd.astype(jnp.float32), precision=lax.Precision.HIGHEST)
    result = result + jnp.dot(against, w_bwd.astype(jnp.float32), precision=lax.Precision.HIGHEST)
    return result.astype(jnp.bfloat16)


def solution(mesh):
    in_specs = (
        P(("row", "col"), None),
        P("row", "col", None, None, None),
        P("row", "col", None),
        P("row", "col", None),
        P("row", "col"),
        P(),
        P(),
    )
    out_specs = P(("row", "col"), None)
    return jax.shard_map(local, mesh=mesh, in_specs=in_specs, out_specs=out_specs, check_vma=False)
```

```python
import jax
import jax.numpy as jnp
from jax import lax
from jax.experimental import pallas as pl
from jax.experimental.pallas import tpu as pltpu
from jax.sharding import PartitionSpec as P


def _nbits(n):
    bits = n.bit_length() - 1
    return bits if (1 << bits) == n else None


def _orders(nb):
    if nb == 4:
        return ((0, 1, 2, 3), (2, 0, 1, 3)), ((3, 0, 1, 2), (3, 2, 0, 1))
    rs = tuple(range(nb))
    return (rs, rs), (rs[::-1], rs[::-1])


def _pick(parity, pair, t):
    return jnp.where(parity == 0, pair[0][t], pair[1][t])


def _swap_col(x, row_size, col_size, bits):
    perm = []
    for r in range(row_size):
        b = bits[r % 2]
        for c in range(col_size):
            perm.append((r * col_size + c, r * col_size + (c ^ (1 << b))))
    return lax.ppermute(x, ("row", "col"), perm)


def _swap(x, axis, size, bit):
    perm = [(i, i ^ (1 << bit)) for i in range(size)]
    return lax.ppermute(x, axis, perm)


def gather_row(x):
    size = lax.axis_size("row")
    nb = _nbits(size)
    if nb is None:
        return lax.all_gather(x, "row", axis=0, tiled=True)
    me = lax.axis_index("row")
    have = x[None]
    order = list(range(nb - 1, -1, -1))
    for bit in order:
        got = _swap(have, "row", size, bit)
        mine = (me >> bit) & 1
        lo = jnp.where(mine == 0, have, got)
        hi = jnp.where(mine == 0, got, have)
        have = jnp.stack([lo, hi], axis=0).reshape((-1,) + have.shape[1:])
    have = have.reshape((2,) * nb + x.shape)
    processed = order[::-1]
    perm = [processed.index(b) for b in range(nb - 1, -1, -1)]
    have = jnp.transpose(have, perm + list(range(nb, nb + x.ndim)))
    return have.reshape((size * x.shape[0],) + x.shape[1:])


def scatter_sum_row(x):
    size = lax.axis_size("row")
    nb = _nbits(size)
    if nb is None:
        return lax.psum_scatter(x, "row", scatter_dimension=0, tiled=True)
    me = lax.axis_index("row")
    data = x.reshape((2,) * nb + (x.shape[0] // size,) + x.shape[1:])
    axes_bits = list(range(nb - 1, -1, -1))
    for bit in range(nb):
        a = axes_bits.index(bit)
        mine = (me >> bit) & 1
        keep = lax.dynamic_index_in_dim(data, mine, axis=a, keepdims=False)
        other = lax.dynamic_index_in_dim(data, 1 - mine, axis=a, keepdims=False)
        data = keep + _swap(other, "row", size, bit)
        axes_bits.pop(a)
    return data


def gather_col(x, order):
    row_size = lax.axis_size("row")
    col_size = lax.axis_size("col")
    nb = len(order[0])
    me = lax.axis_index("col")
    parity = lax.axis_index("row") % 2
    have = x[None]
    for t in range(nb):
        got = _swap_col(have, row_size, col_size, (order[0][t], order[1][t]))
        mine = (me >> _pick(parity, order, t)) & 1
        lo = jnp.where(mine == 0, have, got)
        hi = jnp.where(mine == 0, got, have)
        have = jnp.stack([lo, hi], axis=0).reshape((-1,) + have.shape[1:])
    return have


def scatter_sum_col(data, order, first=0, stop=None):
    row_size = lax.axis_size("row")
    col_size = lax.axis_size("col")
    nb = len(order[0])
    me = lax.axis_index("col")
    parity = lax.axis_index("row") % 2
    for t in range(first, nb if stop is None else stop):
        mine = (me >> _pick(parity, order, t)) & 1
        keep = lax.dynamic_index_in_dim(data, mine, axis=0, keepdims=False)
        other = lax.dynamic_index_in_dim(data, 1 - mine, axis=0, keepdims=False)
        data = keep + _swap_col(other, row_size, col_size, (order[0][t], order[1][t]))
    return data


def _chunk(slots):
    return 32 if slots % 32 == 0 else slots


def along_call(rows, cols, cnt, values, group, nrb, fwd_index):
    slots, side, _ = values.shape
    width = group.shape[-1]
    k = _chunk(slots)

    def kernel(rows_ref, cols_ref, cnt_ref, vals_ref, grp_ref, out_ref):
        i = pl.program_id(0)
        n = jnp.clip(cnt_ref[0], 0, slots)

        @pl.when(i == 0)
        def _():
            out_ref[...] = jnp.zeros(out_ref.shape, out_ref.dtype)

        @pl.when(i * k < n)
        def _():
            for t in range(k):
                s = i * k + t
                tile = jnp.where(s < n, vals_ref[t], jnp.zeros((side, side), vals_ref.dtype))
                r, c = fwd_index(rows_ref[s], cols_ref[s])
                out_ref[r] += jnp.dot(tile, grp_ref[c], preferred_element_type=jnp.float32)

    def vals_map(i, rows_ref, cols_ref, cnt_ref):
        last = jnp.clip(cnt_ref[0] - 1, 0, slots - 1) // k
        return (jnp.minimum(i, last), 0, 0)

    spec = pltpu.PrefetchScalarGridSpec(
        num_scalar_prefetch=3,
        grid=(slots // k,),
        in_specs=[
            pl.BlockSpec((k, side, side), vals_map),
            pl.BlockSpec(group.shape, lambda i, *_: (0, 0, 0)),
        ],
        out_specs=pl.BlockSpec((nrb, side, width), lambda i, *_: (0, 0, 0)),
    )
    return pl.pallas_call(
        kernel,
        grid_spec=spec,
        out_shape=jax.ShapeDtypeStruct((nrb, side, width), jnp.float32),
    )(rows, cols, cnt, values, group)


def against_call(rows, cols, cnt, values, stripe_t, ncb, bwd_index):
    slots, side, _ = values.shape
    width = stripe_t.shape[1]
    k = _chunk(slots)

    def kernel(rows_ref, cols_ref, cnt_ref, vals_ref, st_ref, out_ref):
        i = pl.program_id(0)
        n = jnp.clip(cnt_ref[0], 0, slots)

        @pl.when(i == 0)
        def _():
            out_ref[...] = jnp.zeros(out_ref.shape, out_ref.dtype)

        @pl.when(i * k < n)
        def _():
            for t in range(k):
                s = i * k + t
                tile = jnp.where(s < n, vals_ref[t], jnp.zeros((side, side), vals_ref.dtype))
                r, c = bwd_index(rows_ref[s], cols_ref[s])
                out_ref[c] += jnp.dot(st_ref[r], tile, preferred_element_type=jnp.float32)

    def vals_map(i, rows_ref, cols_ref, cnt_ref):
        last = jnp.clip(cnt_ref[0] - 1, 0, slots - 1) // k
        return (jnp.minimum(i, last), 0, 0)

    spec = pltpu.PrefetchScalarGridSpec(
        num_scalar_prefetch=3,
        grid=(slots // k,),
        in_specs=[
            pl.BlockSpec((k, side, side), vals_map),
            pl.BlockSpec(stripe_t.shape, lambda i, *_: (0, 0, 0)),
        ],
        out_specs=pl.BlockSpec((ncb, width, side), lambda i, *_: (0, 0, 0)),
    )
    return pl.pallas_call(
        kernel,
        grid_spec=spec,
        out_shape=jax.ShapeDtypeStruct((ncb, width, side), jnp.float32),
    )(rows, cols, cnt, values, stripe_t)


def local(features, tile_vals, tile_rows, tile_cols, tile_count, w_fwd, w_bwd):
    row_size = lax.axis_size("row")
    col_size = lax.axis_size("col")
    values = tile_vals[0, 0]
    slots = values.shape[0]
    side = values.shape[1]
    nodes_here = features.shape[0]
    nbc = nodes_here // side
    width = features.shape[1]
    nrb = col_size * nbc
    ncb = row_size * nbc
    parity = lax.axis_index("row") % 2

    rows = tile_rows.reshape(slots)
    cols = tile_cols.reshape(slots)
    cnt = tile_count.reshape(1)

    nb = _nbits(col_size)
    if nb is not None:
        rs_order, ag_order = _orders(nb)

    def block_pos(rowblk, order, msb_first):
        if nb is None:
            return rowblk
        par = lax.axis_index("row") % 2
        dest = rowblk // nbc
        pos = 0
        for t in range(nb):
            bit = (dest >> _pick(par, order, t)) & 1
            pos = pos + (bit << ((nb - 1 - t) if msb_first else t))
        return pos * nbc + rowblk % nbc

    def fwd_index(r, c):
        r = jnp.clip(r, 0, nrb - 1)
        c = jnp.clip(c, 0, ncb - 1)
        return block_pos(r, rs_order if nb is not None else None, True), c

    def bwd_index(r, c):
        r = jnp.clip(r, 0, nrb - 1)
        c = jnp.clip(c, 0, ncb - 1)
        return block_pos(r, ag_order if nb is not None else None, False), c

    group = gather_row(features).reshape(ncb, side, width)
    fwd_parts = along_call(rows, cols, cnt, values, group, nrb, fwd_index)

    mine_t = jnp.transpose(features.reshape(nbc, side, width), (0, 2, 1))
    if nb is not None:
        parts = fwd_parts.reshape((2,) * nb + (nbc, side, width))
        par = lax.axis_index("row") % 2
        mine0 = (lax.axis_index("col") >> _pick(par, rs_order, 0)) & 1
        keep0 = lax.dynamic_index_in_dim(parts, mine0, axis=0, keepdims=False)
        send0 = lax.dynamic_index_in_dim(parts, 1 - mine0, axis=0, keepdims=False)
        mine_t, send0 = lax.optimization_barrier((mine_t, send0))
        got0 = _swap_col(send0, row_size, col_size, (rs_order[0][0], rs_order[1][0]))
        stripe_t = gather_col(mine_t, ag_order).reshape(nrb, width, side)
        along = scatter_sum_col(keep0 + got0, rs_order, 1)
    else:
        stripe_t = lax.all_gather(mine_t, "col", axis=0, tiled=True)
        along = lax.psum_scatter(fwd_parts, "col", scatter_dimension=0, tiled=True)

    bwd_t = against_call(rows, cols, cnt, values, stripe_t, ncb, bwd_index)
    against_t = scatter_sum_row(bwd_t)
    against = jnp.transpose(against_t, (0, 2, 1))

    along = along.reshape(-1, width)
    against = against.reshape(-1, width)
    result = jnp.dot(along, w_fwd.astype(jnp.float32), precision=lax.Precision.HIGHEST)
    result = result + jnp.dot(against, w_bwd.astype(jnp.float32), precision=lax.Precision.HIGHEST)
    return result.astype(jnp.bfloat16)


def solution(mesh):
    in_specs = (
        P(("row", "col"), None),
        P("row", "col", None, None, None),
        P("row", "col", None),
        P("row", "col", None),
        P("row", "col"),
        P(),
        P(),
    )
    out_specs = P(("row", "col"), None)
    return jax.shard_map(local, mesh=mesh, in_specs=in_specs, out_specs=out_specs, check_vma=False)
```

```python
import jax
import jax.numpy as jnp
from jax import lax
from jax.experimental import pallas as pl
from jax.experimental.pallas import tpu as pltpu
from jax.sharding import PartitionSpec as P


def _nbits(n):
    bits = n.bit_length() - 1
    return bits if (1 << bits) == n else None


def _orders(nb):
    if nb == 4:
        return ((0, 1, 2, 3), (2, 0, 1, 3)), ((3, 2, 0, 1), (3, 0, 1, 2))
    rs = tuple(range(nb))
    return (rs, rs), (rs[::-1], rs[::-1])


def _pick(parity, pair, t):
    return jnp.where(parity == 0, pair[0][t], pair[1][t])


def _swap_col(x, row_size, col_size, bits):
    perm = []
    for r in range(row_size):
        b = bits[r % 2]
        for c in range(col_size):
            perm.append((r * col_size + c, r * col_size + (c ^ (1 << b))))
    return lax.ppermute(x, ("row", "col"), perm)


def _swap(x, axis, size, bit):
    perm = [(i, i ^ (1 << bit)) for i in range(size)]
    return lax.ppermute(x, axis, perm)


def gather_row(x):
    size = lax.axis_size("row")
    nb = _nbits(size)
    if nb is None:
        return lax.all_gather(x, "row", axis=0, tiled=True)
    me = lax.axis_index("row")
    have = x[None]
    order = list(range(nb - 1, -1, -1))
    for bit in order:
        got = _swap(have, "row", size, bit)
        mine = (me >> bit) & 1
        lo = jnp.where(mine == 0, have, got)
        hi = jnp.where(mine == 0, got, have)
        have = jnp.stack([lo, hi], axis=0).reshape((-1,) + have.shape[1:])
    have = have.reshape((2,) * nb + x.shape)
    processed = order[::-1]
    perm = [processed.index(b) for b in range(nb - 1, -1, -1)]
    have = jnp.transpose(have, perm + list(range(nb, nb + x.ndim)))
    return have.reshape((size * x.shape[0],) + x.shape[1:])


def scatter_sum_row(x):
    size = lax.axis_size("row")
    nb = _nbits(size)
    if nb is None:
        return lax.psum_scatter(x, "row", scatter_dimension=0, tiled=True)
    me = lax.axis_index("row")
    data = x.reshape((2,) * nb + (x.shape[0] // size,) + x.shape[1:])
    axes_bits = list(range(nb - 1, -1, -1))
    for bit in range(nb):
        a = axes_bits.index(bit)
        mine = (me >> bit) & 1
        keep = lax.dynamic_index_in_dim(data, mine, axis=a, keepdims=False)
        other = lax.dynamic_index_in_dim(data, 1 - mine, axis=a, keepdims=False)
        data = keep + _swap(other, "row", size, bit)
        axes_bits.pop(a)
    return data


def gather_col(x, order):
    row_size = lax.axis_size("row")
    col_size = lax.axis_size("col")
    nb = len(order[0])
    me = lax.axis_index("col")
    parity = lax.axis_index("row") % 2
    have = x[None]
    for t in range(nb):
        got = _swap_col(have, row_size, col_size, (order[0][t], order[1][t]))
        mine = (me >> _pick(parity, order, t)) & 1
        lo = jnp.where(mine == 0, have, got)
        hi = jnp.where(mine == 0, got, have)
        have = jnp.stack([lo, hi], axis=0).reshape((-1,) + have.shape[1:])
    return have


def scatter_sum_col(data, order):
    row_size = lax.axis_size("row")
    col_size = lax.axis_size("col")
    nb = len(order[0])
    me = lax.axis_index("col")
    parity = lax.axis_index("row") % 2
    for t in range(nb):
        mine = (me >> _pick(parity, order, t)) & 1
        keep = lax.dynamic_index_in_dim(data, mine, axis=0, keepdims=False)
        other = lax.dynamic_index_in_dim(data, 1 - mine, axis=0, keepdims=False)
        data = keep + _swap_col(other, row_size, col_size, (order[0][t], order[1][t]))
    return data


def _chunk(slots):
    return 32 if slots % 32 == 0 else slots


def along_call(rows, cols, cnt, values, group, nrb):
    slots, side, _ = values.shape
    width = group.shape[-1]
    k = _chunk(slots)

    def kernel(rows_ref, cols_ref, cnt_ref, vals_ref, grp_ref, out_ref):
        i = pl.program_id(0)
        n = cnt_ref[0]

        @pl.when(i == 0)
        def _():
            out_ref[...] = jnp.zeros(out_ref.shape, out_ref.dtype)

        @pl.when(i * k < n)
        def _():
            for t in range(k):
                s = i * k + t
                tile = jnp.where(s < n, vals_ref[t], jnp.zeros((side, side), vals_ref.dtype))
                r = rows_ref[s]
                c = cols_ref[s]
                out_ref[r] += jnp.dot(tile, grp_ref[c], preferred_element_type=jnp.float32)

    def vals_map(i, rows_ref, cols_ref, cnt_ref):
        last = jnp.maximum(cnt_ref[0] - 1, 0) // k
        return (jnp.minimum(i, last), 0, 0)

    spec = pltpu.PrefetchScalarGridSpec(
        num_scalar_prefetch=3,
        grid=(slots // k,),
        in_specs=[
            pl.BlockSpec((k, side, side), vals_map),
            pl.BlockSpec(group.shape, lambda i, *_: (0, 0, 0)),
        ],
        out_specs=pl.BlockSpec((nrb, side, width), lambda i, *_: (0, 0, 0)),
    )
    return pl.pallas_call(
        kernel,
        grid_spec=spec,
        out_shape=jax.ShapeDtypeStruct((nrb, side, width), jnp.float32),
    )(rows, cols, cnt, values, group)


def against_call(rows, cols, cnt, values, stripe_t, ncb):
    slots, side, _ = values.shape
    width = stripe_t.shape[1]
    k = _chunk(slots)

    def kernel(rows_ref, cols_ref, cnt_ref, vals_ref, st_ref, out_ref):
        i = pl.program_id(0)
        n = cnt_ref[0]

        @pl.when(i == 0)
        def _():
            out_ref[...] = jnp.zeros(out_ref.shape, out_ref.dtype)

        @pl.when(i * k < n)
        def _():
            for t in range(k):
                s = i * k + t
                tile = jnp.where(s < n, vals_ref[t], jnp.zeros((side, side), vals_ref.dtype))
                r = rows_ref[s]
                c = cols_ref[s]
                out_ref[c] += jnp.dot(st_ref[r], tile, preferred_element_type=jnp.float32)

    def vals_map(i, rows_ref, cols_ref, cnt_ref):
        last = jnp.maximum(cnt_ref[0] - 1, 0) // k
        return (jnp.minimum(i, last), 0, 0)

    spec = pltpu.PrefetchScalarGridSpec(
        num_scalar_prefetch=3,
        grid=(slots // k,),
        in_specs=[
            pl.BlockSpec((k, side, side), vals_map),
            pl.BlockSpec(stripe_t.shape, lambda i, *_: (0, 0, 0)),
        ],
        out_specs=pl.BlockSpec((ncb, width, side), lambda i, *_: (0, 0, 0)),
    )
    return pl.pallas_call(
        kernel,
        grid_spec=spec,
        out_shape=jax.ShapeDtypeStruct((ncb, width, side), jnp.float32),
    )(rows, cols, cnt, values, stripe_t)


def local(features, tile_vals, tile_rows, tile_cols, tile_count, w_fwd, w_bwd):
    row_size = lax.axis_size("row")
    col_size = lax.axis_size("col")
    values = tile_vals[0, 0]
    slots = values.shape[0]
    side = values.shape[1]
    nodes_here = features.shape[0]
    nbc = nodes_here // side
    width = features.shape[1]
    nrb = col_size * nbc
    ncb = row_size * nbc
    parity = lax.axis_index("row") % 2

    rowblk = jnp.clip(tile_rows[0, 0], 0, nrb - 1)
    colblk = jnp.clip(tile_cols[0, 0], 0, ncb - 1)
    cnt = jnp.clip(tile_count[0, 0], 0, slots).reshape(1).astype(jnp.int32)

    nb = _nbits(col_size)
    if nb is not None:
        rs_order, ag_order = _orders(nb)
        dest = rowblk // nbc
        sub = rowblk % nbc
        rs_pos = jnp.zeros_like(dest)
        ag_pos = jnp.zeros_like(dest)
        for t in range(nb):
            rs_pos = rs_pos + (((dest >> _pick(parity, rs_order, t)) & 1) << (nb - 1 - t))
            ag_pos = ag_pos + (((dest >> _pick(parity, ag_order, t)) & 1) << t)
        rows_fwd = rs_pos * nbc + sub
        rows_bwd = ag_pos * nbc + sub
    else:
        rows_fwd = rowblk
        rows_bwd = rowblk

    group = gather_row(features).reshape(ncb, side, width)
    fwd_parts = along_call(rows_fwd, colblk, cnt, values, group, nrb)

    mine_t = jnp.transpose(features.reshape(nbc, side, width), (0, 2, 1))
    if nb is not None:
        stripe_t = gather_col(mine_t, ag_order).reshape(nrb, width, side)
        along = scatter_sum_col(fwd_parts.reshape((2,) * nb + (nbc, side, width)), rs_order)
    else:
        stripe_t = lax.all_gather(mine_t, "col", axis=0, tiled=True)
        along = lax.psum_scatter(fwd_parts, "col", scatter_dimension=0, tiled=True)

    bwd_t = against_call(rows_bwd, colblk, cnt, values, stripe_t, ncb)
    against_t = scatter_sum_row(bwd_t)
    against = jnp.transpose(against_t, (0, 2, 1))

    along = along.reshape(-1, width)
    against = against.reshape(-1, width)
    result = jnp.dot(along, w_fwd.astype(jnp.float32), precision=lax.Precision.HIGHEST)
    result = result + jnp.dot(against, w_bwd.astype(jnp.float32), precision=lax.Precision.HIGHEST)
    return result.astype(jnp.bfloat16)


def solution(mesh):
    in_specs = (
        P(("row", "col"), None),
        P("row", "col", None, None, None),
        P("row", "col", None),
        P("row", "col", None),
        P("row", "col"),
        P(),
        P(),
    )
    out_specs = P(("row", "col"), None)
    return jax.shard_map(local, mesh=mesh, in_specs=in_specs, out_specs=out_specs, check_vma=False)
```

```python
import jax
import jax.numpy as jnp
from jax import lax
from jax.experimental import pallas as pl
from jax.experimental.pallas import tpu as pltpu
from jax.sharding import PartitionSpec as P


def _nbits(n):
    bits = n.bit_length() - 1
    return bits if (1 << bits) == n else None


def _orders(nb):
    if nb == 4:
        return ((2, 0, 1, 3), (0, 1, 2, 3)), ((3, 0, 1, 2), (3, 2, 0, 1))
    rs = tuple(range(nb))
    return (rs, rs), (rs[::-1], rs[::-1])


def _pick(parity, pair, t):
    return jnp.where(parity == 0, pair[0][t], pair[1][t])


def _swap_col(x, row_size, col_size, bits):
    perm = []
    for r in range(row_size):
        b = bits[r % 2]
        for c in range(col_size):
            perm.append((r * col_size + c, r * col_size + (c ^ (1 << b))))
    return lax.ppermute(x, ("row", "col"), perm)


def _swap(x, axis, size, bit):
    perm = [(i, i ^ (1 << bit)) for i in range(size)]
    return lax.ppermute(x, axis, perm)


def gather_row(x):
    size = lax.axis_size("row")
    nb = _nbits(size)
    if nb is None:
        return lax.all_gather(x, "row", axis=0, tiled=True)
    me = lax.axis_index("row")
    have = x[None]
    order = list(range(nb - 1, -1, -1))
    for bit in order:
        got = _swap(have, "row", size, bit)
        mine = (me >> bit) & 1
        lo = jnp.where(mine == 0, have, got)
        hi = jnp.where(mine == 0, got, have)
        have = jnp.stack([lo, hi], axis=0).reshape((-1,) + have.shape[1:])
    have = have.reshape((2,) * nb + x.shape)
    processed = order[::-1]
    perm = [processed.index(b) for b in range(nb - 1, -1, -1)]
    have = jnp.transpose(have, perm + list(range(nb, nb + x.ndim)))
    return have.reshape((size * x.shape[0],) + x.shape[1:])


def scatter_sum_row(x):
    size = lax.axis_size("row")
    nb = _nbits(size)
    if nb is None:
        return lax.psum_scatter(x, "row", scatter_dimension=0, tiled=True)
    me = lax.axis_index("row")
    data = x.reshape((2,) * nb + (x.shape[0] // size,) + x.shape[1:])
    axes_bits = list(range(nb - 1, -1, -1))
    for bit in range(nb):
        a = axes_bits.index(bit)
        mine = (me >> bit) & 1
        keep = lax.dynamic_index_in_dim(data, mine, axis=a, keepdims=False)
        other = lax.dynamic_index_in_dim(data, 1 - mine, axis=a, keepdims=False)
        data = keep + _swap(other, "row", size, bit)
        axes_bits.pop(a)
    return data


def gather_col(x, order):
    row_size = lax.axis_size("row")
    col_size = lax.axis_size("col")
    nb = len(order[0])
    me = lax.axis_index("col")
    parity = lax.axis_index("row") % 2
    have = x[None]
    for t in range(nb):
        got = _swap_col(have, row_size, col_size, (order[0][t], order[1][t]))
        mine = (me >> _pick(parity, order, t)) & 1
        lo = jnp.where(mine == 0, have, got)
        hi = jnp.where(mine == 0, got, have)
        have = jnp.stack([lo, hi], axis=0).reshape((-1,) + have.shape[1:])
    return have


def scatter_sum_col(data, order):
    row_size = lax.axis_size("row")
    col_size = lax.axis_size("col")
    nb = len(order[0])
    me = lax.axis_index("col")
    parity = lax.axis_index("row") % 2
    for t in range(nb):
        mine = (me >> _pick(parity, order, t)) & 1
        keep = lax.dynamic_index_in_dim(data, mine, axis=0, keepdims=False)
        other = lax.dynamic_index_in_dim(data, 1 - mine, axis=0, keepdims=False)
        data = keep + _swap_col(other, row_size, col_size, (order[0][t], order[1][t]))
    return data


def _chunk(slots):
    return 32 if slots % 32 == 0 else slots


def along_call(rows, cols, cnt, values, group, nrb):
    slots, side, _ = values.shape
    width = group.shape[-1]
    k = _chunk(slots)

    def kernel(rows_ref, cols_ref, cnt_ref, vals_ref, grp_ref, out_ref):
        i = pl.program_id(0)
        n = cnt_ref[0]

        @pl.when(i == 0)
        def _():
            out_ref[...] = jnp.zeros(out_ref.shape, out_ref.dtype)

        @pl.when(i * k < n)
        def _():
            for t in range(k):
                s = i * k + t
                tile = jnp.where(s < n, vals_ref[t], jnp.zeros((side, side), vals_ref.dtype))
                r = rows_ref[s]
                c = cols_ref[s]
                out_ref[r] += jnp.dot(tile, grp_ref[c], preferred_element_type=jnp.float32)

    def vals_map(i, rows_ref, cols_ref, cnt_ref):
        last = jnp.maximum(cnt_ref[0] - 1, 0) // k
        return (jnp.minimum(i, last), 0, 0)

    spec = pltpu.PrefetchScalarGridSpec(
        num_scalar_prefetch=3,
        grid=(slots // k,),
        in_specs=[
            pl.BlockSpec((k, side, side), vals_map),
            pl.BlockSpec(group.shape, lambda i, *_: (0, 0, 0)),
        ],
        out_specs=pl.BlockSpec((nrb, side, width), lambda i, *_: (0, 0, 0)),
    )
    return pl.pallas_call(
        kernel,
        grid_spec=spec,
        out_shape=jax.ShapeDtypeStruct((nrb, side, width), jnp.float32),
    )(rows, cols, cnt, values, group)


def against_call(rows, cols, cnt, values, stripe_t, ncb):
    slots, side, _ = values.shape
    width = stripe_t.shape[1]
    k = _chunk(slots)

    def kernel(rows_ref, cols_ref, cnt_ref, vals_ref, st_ref, out_ref):
        i = pl.program_id(0)
        n = cnt_ref[0]

        @pl.when(i == 0)
        def _():
            out_ref[...] = jnp.zeros(out_ref.shape, out_ref.dtype)

        @pl.when(i * k < n)
        def _():
            for t in range(k):
                s = i * k + t
                tile = jnp.where(s < n, vals_ref[t], jnp.zeros((side, side), vals_ref.dtype))
                r = rows_ref[s]
                c = cols_ref[s]
                out_ref[c] += jnp.dot(st_ref[r], tile, preferred_element_type=jnp.float32)

    def vals_map(i, rows_ref, cols_ref, cnt_ref):
        last = jnp.maximum(cnt_ref[0] - 1, 0) // k
        return (jnp.minimum(i, last), 0, 0)

    spec = pltpu.PrefetchScalarGridSpec(
        num_scalar_prefetch=3,
        grid=(slots // k,),
        in_specs=[
            pl.BlockSpec((k, side, side), vals_map),
            pl.BlockSpec(stripe_t.shape, lambda i, *_: (0, 0, 0)),
        ],
        out_specs=pl.BlockSpec((ncb, width, side), lambda i, *_: (0, 0, 0)),
    )
    return pl.pallas_call(
        kernel,
        grid_spec=spec,
        out_shape=jax.ShapeDtypeStruct((ncb, width, side), jnp.float32),
    )(rows, cols, cnt, values, stripe_t)


def local(features, tile_vals, tile_rows, tile_cols, tile_count, w_fwd, w_bwd):
    row_size = lax.axis_size("row")
    col_size = lax.axis_size("col")
    values = tile_vals[0, 0]
    slots = values.shape[0]
    side = values.shape[1]
    nodes_here = features.shape[0]
    nbc = nodes_here // side
    width = features.shape[1]
    nrb = col_size * nbc
    ncb = row_size * nbc
    parity = lax.axis_index("row") % 2

    rowblk = jnp.clip(tile_rows[0, 0], 0, nrb - 1)
    colblk = jnp.clip(tile_cols[0, 0], 0, ncb - 1)
    cnt = jnp.clip(tile_count[0, 0], 0, slots).reshape(1).astype(jnp.int32)

    nb = _nbits(col_size)
    if nb is not None:
        rs_order, ag_order = _orders(nb)
        dest = rowblk // nbc
        sub = rowblk % nbc
        rs_pos = jnp.zeros_like(dest)
        ag_pos = jnp.zeros_like(dest)
        for t in range(nb):
            rs_pos = rs_pos + (((dest >> _pick(parity, rs_order, t)) & 1) << (nb - 1 - t))
            ag_pos = ag_pos + (((dest >> _pick(parity, ag_order, t)) & 1) << t)
        rows_fwd = rs_pos * nbc + sub
        rows_bwd = ag_pos * nbc + sub
    else:
        rows_fwd = rowblk
        rows_bwd = rowblk

    group = gather_row(features).reshape(ncb, side, width)
    fwd_parts = along_call(rows_fwd, colblk, cnt, values, group, nrb)

    mine_t = jnp.transpose(features.reshape(nbc, side, width), (0, 2, 1))
    if nb is not None:
        stripe_t = gather_col(mine_t, ag_order).reshape(nrb, width, side)
        along = scatter_sum_col(fwd_parts.reshape((2,) * nb + (nbc, side, width)), rs_order)
    else:
        stripe_t = lax.all_gather(mine_t, "col", axis=0, tiled=True)
        along = lax.psum_scatter(fwd_parts, "col", scatter_dimension=0, tiled=True)

    bwd_t = against_call(rows_bwd, colblk, cnt, values, stripe_t, ncb)
    against_t = scatter_sum_row(bwd_t)
    against = jnp.transpose(against_t, (0, 2, 1))

    along = along.reshape(-1, width)
    against = against.reshape(-1, width)
    result = jnp.dot(along, w_fwd.astype(jnp.float32), precision=lax.Precision.HIGHEST)
    result = result + jnp.dot(against, w_bwd.astype(jnp.float32), precision=lax.Precision.HIGHEST)
    return result.astype(jnp.bfloat16)


def solution(mesh):
    in_specs = (
        P(("row", "col"), None),
        P("row", "col", None, None, None),
        P("row", "col", None),
        P("row", "col", None),
        P("row", "col"),
        P(),
        P(),
    )
    out_specs = P(("row", "col"), None)
    return jax.shard_map(local, mesh=mesh, in_specs=in_specs, out_specs=out_specs, check_vma=False)
```

```python
import jax
import jax.numpy as jnp
from jax import lax
from jax.experimental import pallas as pl
from jax.experimental.pallas import tpu as pltpu
from jax.sharding import PartitionSpec as P


def _nbits(n):
    bits = n.bit_length() - 1
    return bits if (1 << bits) == n else None


def _orders(nb):
    if nb == 4:
        return ((0, 1, 2, 3), (2, 0, 1, 3)), ((3, 0, 1, 2), (3, 2, 0, 1))
    rs = tuple(range(nb))
    return (rs, rs), (rs[::-1], rs[::-1])


def _pick(parity, pair, t):
    return jnp.where(parity == 0, pair[0][t], pair[1][t])


def _swap_col(x, row_size, col_size, bits):
    perm = []
    for r in range(row_size):
        b = bits[r % 2]
        for c in range(col_size):
            perm.append((r * col_size + c, r * col_size + (c ^ (1 << b))))
    return lax.ppermute(x, ("row", "col"), perm)


def _swap(x, axis, size, bit):
    perm = [(i, i ^ (1 << bit)) for i in range(size)]
    return lax.ppermute(x, axis, perm)


def gather_row(x):
    size = lax.axis_size("row")
    nb = _nbits(size)
    if nb is None:
        return lax.all_gather(x, "row", axis=0, tiled=True)
    me = lax.axis_index("row")
    have = x[None]
    order = list(range(nb - 1, -1, -1))
    for bit in order:
        got = _swap(have, "row", size, bit)
        mine = (me >> bit) & 1
        lo = jnp.where(mine == 0, have, got)
        hi = jnp.where(mine == 0, got, have)
        have = jnp.stack([lo, hi], axis=0).reshape((-1,) + have.shape[1:])
    have = have.reshape((2,) * nb + x.shape)
    processed = order[::-1]
    perm = [processed.index(b) for b in range(nb - 1, -1, -1)]
    have = jnp.transpose(have, perm + list(range(nb, nb + x.ndim)))
    return have.reshape((size * x.shape[0],) + x.shape[1:])


def scatter_sum_row(x):
    size = lax.axis_size("row")
    nb = _nbits(size)
    if nb is None:
        return lax.psum_scatter(x, "row", scatter_dimension=0, tiled=True)
    me = lax.axis_index("row")
    data = x.reshape((2,) * nb + (x.shape[0] // size,) + x.shape[1:])
    axes_bits = list(range(nb - 1, -1, -1))
    for bit in range(nb):
        a = axes_bits.index(bit)
        mine = (me >> bit) & 1
        keep = lax.dynamic_index_in_dim(data, mine, axis=a, keepdims=False)
        other = lax.dynamic_index_in_dim(data, 1 - mine, axis=a, keepdims=False)
        data = keep + _swap(other, "row", size, bit)
        axes_bits.pop(a)
    return data


def gather_col(x, order):
    row_size = lax.axis_size("row")
    col_size = lax.axis_size("col")
    nb = len(order[0])
    me = lax.axis_index("col")
    parity = lax.axis_index("row") % 2
    have = x[None]
    for t in range(nb):
        got = _swap_col(have, row_size, col_size, (order[0][t], order[1][t]))
        mine = (me >> _pick(parity, order, t)) & 1
        lo = jnp.where(mine == 0, have, got)
        hi = jnp.where(mine == 0, got, have)
        have = jnp.stack([lo, hi], axis=0).reshape((-1,) + have.shape[1:])
    return have


def scatter_sum_col(data, order):
    row_size = lax.axis_size("row")
    col_size = lax.axis_size("col")
    nb = len(order[0])
    me = lax.axis_index("col")
    parity = lax.axis_index("row") % 2
    for t in range(nb):
        if t == 0:
            keep, other = data[1], data[0]
        else:
            mine = (me >> _pick(parity, order, t)) & 1
            keep = lax.dynamic_index_in_dim(data, mine, axis=0, keepdims=False)
            other = lax.dynamic_index_in_dim(data, 1 - mine, axis=0, keepdims=False)
        data = keep + _swap_col(other, row_size, col_size, (order[0][t], order[1][t]))
    return data


def _chunk(slots):
    return 32 if slots % 32 == 0 else slots


def along_call(rows, cols, cnt, values, group, nrb):
    slots, side, _ = values.shape
    width = group.shape[-1]
    k = _chunk(slots)

    def kernel(rows_ref, cols_ref, cnt_ref, vals_ref, grp_ref, out_ref):
        i = pl.program_id(0)
        n = cnt_ref[0]

        @pl.when(i == 0)
        def _():
            out_ref[...] = jnp.zeros(out_ref.shape, out_ref.dtype)

        @pl.when(i * k < n)
        def _():
            for t in range(k):
                s = i * k + t
                tile = jnp.where(s < n, vals_ref[t], jnp.zeros((side, side), vals_ref.dtype))
                r = rows_ref[s]
                c = cols_ref[s]
                out_ref[r] += jnp.dot(tile, grp_ref[c], preferred_element_type=jnp.float32)

    def vals_map(i, rows_ref, cols_ref, cnt_ref):
        last = jnp.maximum(cnt_ref[0] - 1, 0) // k
        return (jnp.minimum(i, last), 0, 0)

    spec = pltpu.PrefetchScalarGridSpec(
        num_scalar_prefetch=3,
        grid=(slots // k,),
        in_specs=[
            pl.BlockSpec((k, side, side), vals_map),
            pl.BlockSpec(group.shape, lambda i, *_: (0, 0, 0)),
        ],
        out_specs=pl.BlockSpec((nrb, side, width), lambda i, *_: (0, 0, 0)),
    )
    return pl.pallas_call(
        kernel,
        grid_spec=spec,
        out_shape=jax.ShapeDtypeStruct((nrb, side, width), jnp.float32),
    )(rows, cols, cnt, values, group)


def against_call(rows, cols, cnt, values, stripe_t, ncb):
    slots, side, _ = values.shape
    width = stripe_t.shape[1]
    k = _chunk(slots)

    def kernel(rows_ref, cols_ref, cnt_ref, vals_ref, st_ref, out_ref):
        i = pl.program_id(0)
        n = cnt_ref[0]

        @pl.when(i == 0)
        def _():
            out_ref[...] = jnp.zeros(out_ref.shape, out_ref.dtype)

        @pl.when(i * k < n)
        def _():
            for t in range(k):
                s = i * k + t
                tile = jnp.where(s < n, vals_ref[t], jnp.zeros((side, side), vals_ref.dtype))
                r = rows_ref[s]
                c = cols_ref[s]
                out_ref[c] += jnp.dot(st_ref[r], tile, preferred_element_type=jnp.float32)

    def vals_map(i, rows_ref, cols_ref, cnt_ref):
        last = jnp.maximum(cnt_ref[0] - 1, 0) // k
        return (jnp.minimum(i, last), 0, 0)

    spec = pltpu.PrefetchScalarGridSpec(
        num_scalar_prefetch=3,
        grid=(slots // k,),
        in_specs=[
            pl.BlockSpec((k, side, side), vals_map),
            pl.BlockSpec(stripe_t.shape, lambda i, *_: (0, 0, 0)),
        ],
        out_specs=pl.BlockSpec((ncb, width, side), lambda i, *_: (0, 0, 0)),
    )
    return pl.pallas_call(
        kernel,
        grid_spec=spec,
        out_shape=jax.ShapeDtypeStruct((ncb, width, side), jnp.float32),
    )(rows, cols, cnt, values, stripe_t)


def local(features, tile_vals, tile_rows, tile_cols, tile_count, w_fwd, w_bwd):
    row_size = lax.axis_size("row")
    col_size = lax.axis_size("col")
    values = tile_vals[0, 0]
    slots = values.shape[0]
    side = values.shape[1]
    nodes_here = features.shape[0]
    nbc = nodes_here // side
    width = features.shape[1]
    nrb = col_size * nbc
    ncb = row_size * nbc
    parity = lax.axis_index("row") % 2

    rowblk = jnp.clip(tile_rows[0, 0], 0, nrb - 1)
    colblk = jnp.clip(tile_cols[0, 0], 0, ncb - 1)
    cnt = jnp.clip(tile_count[0, 0], 0, slots).reshape(1).astype(jnp.int32)

    nb = _nbits(col_size)
    if nb is not None:
        rs_order, ag_order = _orders(nb)
        dest = rowblk // nbc
        sub = rowblk % nbc
        rs_pos = jnp.zeros_like(dest)
        ag_pos = jnp.zeros_like(dest)
        for t in range(nb):
            bit = (dest >> _pick(parity, rs_order, t)) & 1
            if t == 0:
                bit = 1 - (bit ^ ((lax.axis_index("col") >> _pick(parity, rs_order, 0)) & 1))
            rs_pos = rs_pos + (bit << (nb - 1 - t))
            ag_pos = ag_pos + (((dest >> _pick(parity, ag_order, t)) & 1) << t)
        rows_fwd = rs_pos * nbc + sub
        rows_bwd = ag_pos * nbc + sub
    else:
        rows_fwd = rowblk
        rows_bwd = rowblk

    group = gather_row(features).reshape(ncb, side, width)
    fwd_parts = along_call(rows_fwd, colblk, cnt, values, group, nrb)

    mine_t = jnp.transpose(features.reshape(nbc, side, width), (0, 2, 1))
    if nb is not None:
        stripe_t = gather_col(mine_t, ag_order).reshape(nrb, width, side)
        along = scatter_sum_col(fwd_parts.reshape((2,) * nb + (nbc, side, width)), rs_order)
    else:
        stripe_t = lax.all_gather(mine_t, "col", axis=0, tiled=True)
        along = lax.psum_scatter(fwd_parts, "col", scatter_dimension=0, tiled=True)

    bwd_t = against_call(rows_bwd, colblk, cnt, values, stripe_t, ncb)
    against_t = scatter_sum_row(bwd_t)
    against = jnp.transpose(against_t, (0, 2, 1))

    along = along.reshape(-1, width)
    against = against.reshape(-1, width)
    result = jnp.dot(along, w_fwd.astype(jnp.float32), precision=lax.Precision.HIGHEST)
    result = result + jnp.dot(against, w_bwd.astype(jnp.float32), precision=lax.Precision.HIGHEST)
    return result.astype(jnp.bfloat16)


def solution(mesh):
    in_specs = (
        P(("row", "col"), None),
        P("row", "col", None, None, None),
        P("row", "col", None),
        P("row", "col", None),
        P("row", "col"),
        P(),
        P(),
    )
    out_specs = P(("row", "col"), None)
    return jax.shard_map(local, mesh=mesh, in_specs=in_specs, out_specs=out_specs, check_vma=False)
```

```python
import jax
import jax.numpy as jnp
from jax import lax
from jax.experimental import pallas as pl
from jax.experimental.pallas import tpu as pltpu
from jax.sharding import PartitionSpec as P


def _nbits(n):
    bits = n.bit_length() - 1
    return bits if (1 << bits) == n else None


def _orders(nb):
    if nb == 4:
        return ((0, 1, 2, 3), (2, 0, 1, 3)), ((3, 0, 1, 2), (3, 2, 0, 1))
    rs = tuple(range(nb))
    return (rs, rs), (rs[::-1], rs[::-1])


def _pick(parity, pair, t):
    return jnp.where(parity == 0, pair[0][t], pair[1][t])


def _swap_col(x, row_size, col_size, bits):
    perm = []
    for r in range(row_size):
        b = bits[r % 2]
        for c in range(col_size):
            perm.append((r * col_size + c, r * col_size + (c ^ (1 << b))))
    return lax.ppermute(x, ("row", "col"), perm)


def _swap(x, axis, size, bit):
    perm = [(i, i ^ (1 << bit)) for i in range(size)]
    return lax.ppermute(x, axis, perm)


def gather_row(x):
    size = lax.axis_size("row")
    nb = _nbits(size)
    if nb is None:
        return lax.all_gather(x, "row", axis=0, tiled=True)
    me = lax.axis_index("row")
    have = x[None]
    order = list(range(nb - 1, -1, -1))
    for bit in order:
        got = _swap(have, "row", size, bit)
        mine = (me >> bit) & 1
        lo = jnp.where(mine == 0, have, got)
        hi = jnp.where(mine == 0, got, have)
        have = jnp.stack([lo, hi], axis=0).reshape((-1,) + have.shape[1:])
    have = have.reshape((2,) * nb + x.shape)
    processed = order[::-1]
    perm = [processed.index(b) for b in range(nb - 1, -1, -1)]
    have = jnp.transpose(have, perm + list(range(nb, nb + x.ndim)))
    return have.reshape((size * x.shape[0],) + x.shape[1:])


def scatter_sum_row(x):
    size = lax.axis_size("row")
    nb = _nbits(size)
    if nb is None:
        return lax.psum_scatter(x, "row", scatter_dimension=0, tiled=True)
    me = lax.axis_index("row")
    data = x.reshape((2,) * nb + (x.shape[0] // size,) + x.shape[1:])
    axes_bits = list(range(nb - 1, -1, -1))
    for bit in range(nb):
        a = axes_bits.index(bit)
        mine = (me >> bit) & 1
        keep = lax.dynamic_index_in_dim(data, mine, axis=a, keepdims=False)
        other = lax.dynamic_index_in_dim(data, 1 - mine, axis=a, keepdims=False)
        data = keep + _swap(other, "row", size, bit)
        axes_bits.pop(a)
    return data


def gather_col(x, order):
    row_size = lax.axis_size("row")
    col_size = lax.axis_size("col")
    nb = len(order[0])
    me = lax.axis_index("col")
    parity = lax.axis_index("row") % 2
    have = x[None]
    for t in range(nb):
        got = _swap_col(have, row_size, col_size, (order[0][t], order[1][t]))
        mine = (me >> _pick(parity, order, t)) & 1
        lo = jnp.where(mine == 0, have, got)
        hi = jnp.where(mine == 0, got, have)
        have = jnp.stack([lo, hi], axis=0).reshape((-1,) + have.shape[1:])
    return have


def scatter_sum_col(data, order):
    row_size = lax.axis_size("row")
    col_size = lax.axis_size("col")
    nb = len(order[0])
    me = lax.axis_index("col")
    parity = lax.axis_index("row") % 2
    for t in range(nb):
        mine = (me >> _pick(parity, order, t)) & 1
        keep = lax.dynamic_index_in_dim(data, mine, axis=0, keepdims=False)
        other = lax.dynamic_index_in_dim(data, 1 - mine, axis=0, keepdims=False)
        data = keep + _swap_col(other, row_size, col_size, (order[0][t], order[1][t]))
    return data


def _chunk(slots):
    return 32 if slots % 32 == 0 else slots


def along_call(rows, cols, cnt, values, group, nrb):
    slots, side, _ = values.shape
    width = group.shape[-1]
    k = _chunk(slots)

    def kernel(rows_ref, cols_ref, cnt_ref, vals_ref, grp_ref, out_ref):
        i = pl.program_id(0)
        n = cnt_ref[0]

        @pl.when(i == 0)
        def _():
            out_ref[...] = jnp.zeros(out_ref.shape, out_ref.dtype)

        @pl.when(i * k < n)
        def _():
            for t in range(k):
                s = i * k + t
                tile = jnp.where(s < n, vals_ref[t], jnp.zeros((side, side), vals_ref.dtype))
                r = rows_ref[s]
                c = cols_ref[s]
                out_ref[r] += jnp.dot(tile, grp_ref[c], preferred_element_type=jnp.float32)

    def vals_map(i, rows_ref, cols_ref, cnt_ref):
        last = jnp.maximum(cnt_ref[0] - 1, 0) // k
        return (jnp.minimum(i, last), 0, 0)

    spec = pltpu.PrefetchScalarGridSpec(
        num_scalar_prefetch=3,
        grid=(slots // k,),
        in_specs=[
            pl.BlockSpec((k, side, side), vals_map),
            pl.BlockSpec(group.shape, lambda i, *_: (0, 0, 0)),
        ],
        out_specs=pl.BlockSpec((nrb, side, width), lambda i, *_: (0, 0, 0)),
    )
    return pl.pallas_call(
        kernel,
        grid_spec=spec,
        out_shape=jax.ShapeDtypeStruct((nrb, side, width), jnp.float32),
    )(rows, cols, cnt, values, group)


def against_call(rows, cols, cnt, values, stripe_t, ncb):
    slots, side, _ = values.shape
    width = stripe_t.shape[1]
    k = _chunk(slots)

    def kernel(rows_ref, cols_ref, cnt_ref, vals_ref, st_ref, out_ref):
        i = pl.program_id(0)
        n = cnt_ref[0]

        @pl.when(i == 0)
        def _():
            out_ref[...] = jnp.zeros(out_ref.shape, out_ref.dtype)

        @pl.when(i * k < n)
        def _():
            for t in range(k):
                s = i * k + t
                tile = jnp.where(s < n, vals_ref[t], jnp.zeros((side, side), vals_ref.dtype))
                r = rows_ref[s]
                c = cols_ref[s]
                out_ref[c] += jnp.dot(st_ref[r], tile, preferred_element_type=jnp.float32)

    def vals_map(i, rows_ref, cols_ref, cnt_ref):
        last = jnp.maximum(cnt_ref[0] - 1, 0) // k
        return (jnp.minimum(i, last), 0, 0)

    spec = pltpu.PrefetchScalarGridSpec(
        num_scalar_prefetch=3,
        grid=(slots // k,),
        in_specs=[
            pl.BlockSpec((k, side, side), vals_map),
            pl.BlockSpec(stripe_t.shape, lambda i, *_: (0, 0, 0)),
        ],
        out_specs=pl.BlockSpec((ncb, width, side), lambda i, *_: (0, 0, 0)),
    )
    return pl.pallas_call(
        kernel,
        grid_spec=spec,
        out_shape=jax.ShapeDtypeStruct((ncb, width, side), jnp.float32),
    )(rows, cols, cnt, values, stripe_t)


def local(features, tile_vals, tile_rows, tile_cols, tile_count, w_fwd, w_bwd):
    row_size = lax.axis_size("row")
    col_size = lax.axis_size("col")
    values = tile_vals[0, 0]
    slots = values.shape[0]
    side = values.shape[1]
    nodes_here = features.shape[0]
    nbc = nodes_here // side
    width = features.shape[1]
    nrb = col_size * nbc
    ncb = row_size * nbc
    parity = lax.axis_index("row") % 2

    rowblk = jnp.clip(tile_rows[0, 0], 0, nrb - 1)
    colblk = jnp.clip(tile_cols[0, 0], 0, ncb - 1)
    cnt = jnp.clip(tile_count[0, 0], 0, slots).reshape(1).astype(jnp.int32)

    nb = _nbits(col_size)
    if nb is not None:
        rs_order, ag_order = _orders(nb)
        dest = rowblk // nbc
        sub = rowblk % nbc
        rs_pos = jnp.zeros_like(dest)
        ag_pos = jnp.zeros_like(dest)
        for t in range(nb):
            rs_pos = rs_pos + (((dest >> _pick(parity, rs_order, t)) & 1) << (nb - 1 - t))
            ag_pos = ag_pos + (((dest >> _pick(parity, ag_order, t)) & 1) << t)
        rows_fwd = rs_pos * nbc + sub
        rows_bwd = ag_pos * nbc + sub
    else:
        rows_fwd = rowblk
        rows_bwd = rowblk

    nb_r = _nbits(row_size)
    if nb_r is not None:
        me_r = lax.axis_index("row")
        have = features[None]
        src = colblk // nbc
        pos = jnp.zeros_like(src)
        for t, bit in enumerate(range(nb_r - 1, -1, -1)):
            have = jnp.concatenate([have, _swap(have, "row", row_size, bit)], axis=0)
            pos = pos + ((((src ^ me_r) >> bit) & 1) << t)
        group = have.reshape(ncb, side, width)
        cols_fwd = pos * nbc + colblk % nbc
    else:
        group = gather_row(features).reshape(ncb, side, width)
        cols_fwd = colblk
    fwd_parts = along_call(rows_fwd, cols_fwd, cnt, values, group, nrb)

    mine_t = jnp.transpose(features.reshape(nbc, side, width), (0, 2, 1))
    if nb is not None:
        stripe_t = gather_col(mine_t, ag_order).reshape(nrb, width, side)
        along = scatter_sum_col(fwd_parts.reshape((2,) * nb + (nbc, side, width)), rs_order)
    else:
        stripe_t = lax.all_gather(mine_t, "col", axis=0, tiled=True)
        along = lax.psum_scatter(fwd_parts, "col", scatter_dimension=0, tiled=True)

    bwd_t = against_call(rows_bwd, colblk, cnt, values, stripe_t, ncb)
    against_t = scatter_sum_row(bwd_t)
    against = jnp.transpose(against_t, (0, 2, 1))

    along = along.reshape(-1, width)
    against = against.reshape(-1, width)
    result = jnp.dot(along, w_fwd.astype(jnp.float32), precision=lax.Precision.HIGHEST)
    result = result + jnp.dot(against, w_bwd.astype(jnp.float32), precision=lax.Precision.HIGHEST)
    return result.astype(jnp.bfloat16)


def solution(mesh):
    in_specs = (
        P(("row", "col"), None),
        P("row", "col", None, None, None),
        P("row", "col", None),
        P("row", "col", None),
        P("row", "col"),
        P(),
        P(),
    )
    out_specs = P(("row", "col"), None)
    return jax.shard_map(local, mesh=mesh, in_specs=in_specs, out_specs=out_specs, check_vma=False)
```

```python
import jax
import jax.numpy as jnp
from jax import lax
from jax.experimental import pallas as pl
from jax.experimental.pallas import tpu as pltpu
from jax.sharding import PartitionSpec as P


def _nbits(n):
    bits = n.bit_length() - 1
    return bits if (1 << bits) == n else None


def _orders(nb):
    if nb == 4:
        return ((0, 1, 2, 3), (2, 0, 1, 3)), ((3, 0, 1, 2), (3, 2, 0, 1))
    rs = tuple(range(nb))
    return (rs, rs), (rs[::-1], rs[::-1])


def _pick(parity, pair, t):
    return jnp.where(parity == 0, pair[0][t], pair[1][t])


def _swap_col(x, row_size, col_size, bits):
    perm = []
    for r in range(row_size):
        b = bits[r % 2]
        for c in range(col_size):
            perm.append((r * col_size + c, r * col_size + (c ^ (1 << b))))
    return lax.ppermute(x, ("row", "col"), perm)


def _swap(x, axis, size, bit):
    perm = [(i, i ^ (1 << bit)) for i in range(size)]
    return lax.ppermute(x, axis, perm)


def gather_row(x):
    size = lax.axis_size("row")
    nb = _nbits(size)
    if nb is None:
        return lax.all_gather(x, "row", axis=0, tiled=True)
    me = lax.axis_index("row")
    have = x[None]
    order = list(range(nb - 1, -1, -1))
    for bit in order:
        got = _swap(have, "row", size, bit)
        mine = (me >> bit) & 1
        lo = jnp.where(mine == 0, have, got)
        hi = jnp.where(mine == 0, got, have)
        have = jnp.stack([lo, hi], axis=0).reshape((-1,) + have.shape[1:])
    have = have.reshape((2,) * nb + x.shape)
    processed = order[::-1]
    perm = [processed.index(b) for b in range(nb - 1, -1, -1)]
    have = jnp.transpose(have, perm + list(range(nb, nb + x.ndim)))
    return have.reshape((size * x.shape[0],) + x.shape[1:])


def scatter_sum_row(x):
    size = lax.axis_size("row")
    nb = _nbits(size)
    if nb is None:
        return lax.psum_scatter(x, "row", scatter_dimension=0, tiled=True)
    me = lax.axis_index("row")
    data = x.reshape((2,) * nb + (x.shape[0] // size,) + x.shape[1:])
    axes_bits = list(range(nb - 1, -1, -1))
    for bit in range(nb):
        a = axes_bits.index(bit)
        mine = (me >> bit) & 1
        keep = lax.dynamic_index_in_dim(data, mine, axis=a, keepdims=False)
        other = lax.dynamic_index_in_dim(data, 1 - mine, axis=a, keepdims=False)
        data = keep + _swap(other, "row", size, bit)
        axes_bits.pop(a)
    return data


def gather_col(x, order):
    row_size = lax.axis_size("row")
    col_size = lax.axis_size("col")
    nb = len(order[0])
    me = lax.axis_index("col")
    parity = lax.axis_index("row") % 2
    have = x[None]
    for t in range(nb):
        got = _swap_col(have, row_size, col_size, (order[0][t], order[1][t]))
        mine = (me >> _pick(parity, order, t)) & 1
        lo = jnp.where(mine == 0, have, got)
        hi = jnp.where(mine == 0, got, have)
        have = jnp.stack([lo, hi], axis=0).reshape((-1,) + have.shape[1:])
    return have


def scatter_sum_col(data, order):
    row_size = lax.axis_size("row")
    col_size = lax.axis_size("col")
    nb = len(order[0])
    me = lax.axis_index("col")
    parity = lax.axis_index("row") % 2
    for t in range(nb):
        if t == 0:
            keep, other = data[1], data[0]
        else:
            mine = (me >> _pick(parity, order, t)) & 1
            keep = lax.dynamic_index_in_dim(data, mine, axis=0, keepdims=False)
            other = lax.dynamic_index_in_dim(data, 1 - mine, axis=0, keepdims=False)
        data = keep + _swap_col(other, row_size, col_size, (order[0][t], order[1][t]))
    return data


def _chunk(slots):
    return 32 if slots % 32 == 0 else slots


def along_call(rows, cols, cnt, values, group, nrb):
    slots, side, _ = values.shape
    width = group.shape[-1]
    k = _chunk(slots)

    def kernel(rows_ref, cols_ref, cnt_ref, vals_ref, grp_ref, out_ref):
        i = pl.program_id(0)
        n = cnt_ref[0]

        @pl.when(i == 0)
        def _():
            out_ref[...] = jnp.zeros(out_ref.shape, out_ref.dtype)

        @pl.when(i * k < n)
        def _():
            for t in range(k):
                s = i * k + t
                tile = jnp.where(s < n, vals_ref[t], jnp.zeros((side, side), vals_ref.dtype))
                r = rows_ref[s]
                c = cols_ref[s]
                out_ref[r] += jnp.dot(tile, grp_ref[c], preferred_element_type=jnp.float32)

    def vals_map(i, rows_ref, cols_ref, cnt_ref):
        last = jnp.maximum(cnt_ref[0] - 1, 0) // k
        return (jnp.minimum(i, last), 0, 0)

    spec = pltpu.PrefetchScalarGridSpec(
        num_scalar_prefetch=3,
        grid=(slots // k,),
        in_specs=[
            pl.BlockSpec((k, side, side), vals_map),
            pl.BlockSpec(group.shape, lambda i, *_: (0, 0, 0)),
        ],
        out_specs=pl.BlockSpec((nrb, side, width), lambda i, *_: (0, 0, 0)),
    )
    return pl.pallas_call(
        kernel,
        grid_spec=spec,
        out_shape=jax.ShapeDtypeStruct((nrb, side, width), jnp.float32),
    )(rows, cols, cnt, values, group)


def against_call(rows, cols, cnt, values, stripe_t, ncb):
    slots, side, _ = values.shape
    width = stripe_t.shape[1]
    k = _chunk(slots)

    def kernel(rows_ref, cols_ref, cnt_ref, vals_ref, st_ref, out_ref):
        i = pl.program_id(0)
        n = cnt_ref[0]

        @pl.when(i == 0)
        def _():
            out_ref[...] = jnp.zeros(out_ref.shape, out_ref.dtype)

        @pl.when(i * k < n)
        def _():
            for t in range(k):
                s = i * k + t
                tile = jnp.where(s < n, vals_ref[t], jnp.zeros((side, side), vals_ref.dtype))
                r = rows_ref[s]
                c = cols_ref[s]
                out_ref[c] += jnp.dot(st_ref[r], tile, preferred_element_type=jnp.float32)

    def vals_map(i, rows_ref, cols_ref, cnt_ref):
        last = jnp.maximum(cnt_ref[0] - 1, 0) // k
        return (jnp.minimum(i, last), 0, 0)

    spec = pltpu.PrefetchScalarGridSpec(
        num_scalar_prefetch=3,
        grid=(slots // k,),
        in_specs=[
            pl.BlockSpec((k, side, side), vals_map),
            pl.BlockSpec(stripe_t.shape, lambda i, *_: (0, 0, 0)),
        ],
        out_specs=pl.BlockSpec((ncb, width, side), lambda i, *_: (0, 0, 0)),
    )
    return pl.pallas_call(
        kernel,
        grid_spec=spec,
        out_shape=jax.ShapeDtypeStruct((ncb, width, side), jnp.float32),
    )(rows, cols, cnt, values, stripe_t)


def local(features, tile_vals, tile_rows, tile_cols, tile_count, w_fwd, w_bwd):
    row_size = lax.axis_size("row")
    col_size = lax.axis_size("col")
    values = tile_vals[0, 0]
    slots = values.shape[0]
    side = values.shape[1]
    nodes_here = features.shape[0]
    nbc = nodes_here // side
    width = features.shape[1]
    nrb = col_size * nbc
    ncb = row_size * nbc
    parity = lax.axis_index("row") % 2

    rowblk = jnp.clip(tile_rows[0, 0], 0, nrb - 1)
    colblk = jnp.clip(tile_cols[0, 0], 0, ncb - 1)
    cnt = jnp.clip(tile_count[0, 0], 0, slots).reshape(1).astype(jnp.int32)

    nb = _nbits(col_size)
    if nb is not None:
        rs_order, ag_order = _orders(nb)
        dest = rowblk // nbc
        sub = rowblk % nbc
        rs_pos = jnp.zeros_like(dest)
        ag_pos = jnp.zeros_like(dest)
        for t in range(nb):
            bit = (dest >> _pick(parity, rs_order, t)) & 1
            if t == 0:
                bit = 1 - (bit ^ ((lax.axis_index("col") >> _pick(parity, rs_order, 0)) & 1))
            rs_pos = rs_pos + (bit << (nb - 1 - t))
            ag_pos = ag_pos + (((dest >> _pick(parity, ag_order, t)) & 1) << t)
        rows_fwd = rs_pos * nbc + sub
        rows_bwd = ag_pos * nbc + sub
    else:
        rows_fwd = rowblk
        rows_bwd = rowblk

    nb_r = _nbits(row_size)
    if nb_r is not None:
        me_r = lax.axis_index("row")
        have = features[None]
        src = colblk // nbc
        pos = jnp.zeros_like(src)
        for t, bit in enumerate(range(nb_r - 1, -1, -1)):
            have = jnp.concatenate([have, _swap(have, "row", row_size, bit)], axis=0)
            pos = pos + ((((src ^ me_r) >> bit) & 1) << t)
        group = have.reshape(ncb, side, width)
        cols_fwd = pos * nbc + colblk % nbc
    else:
        group = gather_row(features).reshape(ncb, side, width)
        cols_fwd = colblk
    fwd_parts = along_call(rows_fwd, cols_fwd, cnt, values, group, nrb)

    mine_t = jnp.transpose(features.reshape(nbc, side, width), (0, 2, 1))
    if nb is not None:
        stripe_t = gather_col(mine_t, ag_order).reshape(nrb, width, side)
        along = scatter_sum_col(fwd_parts.reshape((2,) * nb + (nbc, side, width)), rs_order)
    else:
        stripe_t = lax.all_gather(mine_t, "col", axis=0, tiled=True)
        along = lax.psum_scatter(fwd_parts, "col", scatter_dimension=0, tiled=True)

    bwd_t = against_call(rows_bwd, colblk, cnt, values, stripe_t, ncb)
    against_t = scatter_sum_row(bwd_t)
    against = jnp.transpose(against_t, (0, 2, 1))

    along = along.reshape(-1, width)
    against = against.reshape(-1, width)
    result = jnp.dot(along, w_fwd.astype(jnp.float32), precision=lax.Precision.HIGHEST)
    result = result + jnp.dot(against, w_bwd.astype(jnp.float32), precision=lax.Precision.HIGHEST)
    return result.astype(jnp.bfloat16)


def solution(mesh):
    in_specs = (
        P(("row", "col"), None),
        P("row", "col", None, None, None),
        P("row", "col", None),
        P("row", "col", None),
        P("row", "col"),
        P(),
        P(),
    )
    out_specs = P(("row", "col"), None)
    return jax.shard_map(local, mesh=mesh, in_specs=in_specs, out_specs=out_specs, check_vma=False)
```

```python
import jax
import jax.numpy as jnp
from jax import lax
from jax.experimental import pallas as pl
from jax.experimental.pallas import tpu as pltpu
from jax.sharding import PartitionSpec as P


def _nbits(n):
    bits = n.bit_length() - 1
    return bits if (1 << bits) == n else None


def _orders(nb):
    if nb == 4:
        return ((0, 1, 2, 3), (2, 0, 1, 3)), ((3, 0, 1, 2), (3, 2, 0, 1))
    rs = tuple(range(nb))
    return (rs, rs), (rs[::-1], rs[::-1])


def _pick(parity, pair, t):
    return jnp.where(parity == 0, pair[0][t], pair[1][t])


def _swap_col(x, row_size, col_size, bits):
    perm = []
    for r in range(row_size):
        b = bits[r % 2]
        for c in range(col_size):
            perm.append((r * col_size + c, r * col_size + (c ^ (1 << b))))
    return lax.ppermute(x, ("row", "col"), perm)


def _swap(x, axis, size, bit):
    perm = [(i, i ^ (1 << bit)) for i in range(size)]
    return lax.ppermute(x, axis, perm)


def gather_row(x):
    size = lax.axis_size("row")
    nb = _nbits(size)
    if nb is None:
        return lax.all_gather(x, "row", axis=0, tiled=True)
    me = lax.axis_index("row")
    have = x[None]
    order = list(range(nb - 1, -1, -1))
    for bit in order:
        got = _swap(have, "row", size, bit)
        mine = (me >> bit) & 1
        lo = jnp.where(mine == 0, have, got)
        hi = jnp.where(mine == 0, got, have)
        have = jnp.stack([lo, hi], axis=0).reshape((-1,) + have.shape[1:])
    have = have.reshape((2,) * nb + x.shape)
    processed = order[::-1]
    perm = [processed.index(b) for b in range(nb - 1, -1, -1)]
    have = jnp.transpose(have, perm + list(range(nb, nb + x.ndim)))
    return have.reshape((size * x.shape[0],) + x.shape[1:])


def scatter_sum_row(x):
    size = lax.axis_size("row")
    nb = _nbits(size)
    if nb is None:
        return lax.psum_scatter(x, "row", scatter_dimension=0, tiled=True)
    me = lax.axis_index("row")
    data = x.reshape((2,) * nb + (x.shape[0] // size,) + x.shape[1:])
    axes_bits = list(range(nb - 1, -1, -1))
    for bit in range(nb):
        a = axes_bits.index(bit)
        mine = (me >> bit) & 1
        keep = lax.dynamic_index_in_dim(data, mine, axis=a, keepdims=False)
        other = lax.dynamic_index_in_dim(data, 1 - mine, axis=a, keepdims=False)
        data = keep + _swap(other, "row", size, bit)
        axes_bits.pop(a)
    return data


def gather_col(x, order):
    row_size = lax.axis_size("row")
    col_size = lax.axis_size("col")
    nb = len(order[0])
    me = lax.axis_index("col")
    parity = lax.axis_index("row") % 2
    have = x[None]
    for t in range(nb):
        got = _swap_col(have, row_size, col_size, (order[0][t], order[1][t]))
        mine = (me >> _pick(parity, order, t)) & 1
        lo = jnp.where(mine == 0, have, got)
        hi = jnp.where(mine == 0, got, have)
        have = jnp.stack([lo, hi], axis=0).reshape((-1,) + have.shape[1:])
    return have


def scatter_sum_col(data, order):
    row_size = lax.axis_size("row")
    col_size = lax.axis_size("col")
    nb = len(order[0])
    me = lax.axis_index("col")
    parity = lax.axis_index("row") % 2
    for t in range(nb):
        mine = (me >> _pick(parity, order, t)) & 1
        keep = lax.dynamic_index_in_dim(data, mine, axis=0, keepdims=False)
        other = lax.dynamic_index_in_dim(data, 1 - mine, axis=0, keepdims=False)
        data = keep + _swap_col(other, row_size, col_size, (order[0][t], order[1][t]))
    return data


def _chunk(slots):
    return 16 if slots % 16 == 0 else slots


def along_call(rows, cols, cnt, values, group, nrb):
    slots, side, _ = values.shape
    width = group.shape[-1]
    k = _chunk(slots)

    def kernel(rows_ref, cols_ref, cnt_ref, vals_ref, grp_ref, out_ref):
        i = pl.program_id(0)
        n = cnt_ref[0]

        @pl.when(i == 0)
        def _():
            out_ref[...] = jnp.zeros(out_ref.shape, out_ref.dtype)

        @pl.when(i * k < n)
        def _():
            for t in range(k):
                s = i * k + t
                tile = jnp.where(s < n, vals_ref[t], jnp.zeros((side, side), vals_ref.dtype))
                r = rows_ref[s]
                c = cols_ref[s]
                out_ref[r] += jnp.dot(tile, grp_ref[c], preferred_element_type=jnp.float32)

    def vals_map(i, rows_ref, cols_ref, cnt_ref):
        last = jnp.maximum(cnt_ref[0] - 1, 0) // k
        return (jnp.minimum(i, last), 0, 0)

    spec = pltpu.PrefetchScalarGridSpec(
        num_scalar_prefetch=3,
        grid=(slots // k,),
        in_specs=[
            pl.BlockSpec((k, side, side), vals_map),
            pl.BlockSpec(group.shape, lambda i, *_: (0, 0, 0)),
        ],
        out_specs=pl.BlockSpec((nrb, side, width), lambda i, *_: (0, 0, 0)),
    )
    return pl.pallas_call(
        kernel,
        grid_spec=spec,
        out_shape=jax.ShapeDtypeStruct((nrb, side, width), jnp.float32),
    )(rows, cols, cnt, values, group)


def against_call(rows, cols, cnt, values, stripe_t, ncb):
    slots, side, _ = values.shape
    width = stripe_t.shape[1]
    k = _chunk(slots)

    def kernel(rows_ref, cols_ref, cnt_ref, vals_ref, st_ref, out_ref):
        i = pl.program_id(0)
        n = cnt_ref[0]

        @pl.when(i == 0)
        def _():
            out_ref[...] = jnp.zeros(out_ref.shape, out_ref.dtype)

        @pl.when(i * k < n)
        def _():
            for t in range(k):
                s = i * k + t
                tile = jnp.where(s < n, vals_ref[t], jnp.zeros((side, side), vals_ref.dtype))
                r = rows_ref[s]
                c = cols_ref[s]
                out_ref[c] += jnp.dot(st_ref[r], tile, preferred_element_type=jnp.float32)

    def vals_map(i, rows_ref, cols_ref, cnt_ref):
        last = jnp.maximum(cnt_ref[0] - 1, 0) // k
        return (jnp.minimum(i, last), 0, 0)

    spec = pltpu.PrefetchScalarGridSpec(
        num_scalar_prefetch=3,
        grid=(slots // k,),
        in_specs=[
            pl.BlockSpec((k, side, side), vals_map),
            pl.BlockSpec(stripe_t.shape, lambda i, *_: (0, 0, 0)),
        ],
        out_specs=pl.BlockSpec((ncb, width, side), lambda i, *_: (0, 0, 0)),
    )
    return pl.pallas_call(
        kernel,
        grid_spec=spec,
        out_shape=jax.ShapeDtypeStruct((ncb, width, side), jnp.float32),
    )(rows, cols, cnt, values, stripe_t)


def local(features, tile_vals, tile_rows, tile_cols, tile_count, w_fwd, w_bwd):
    row_size = lax.axis_size("row")
    col_size = lax.axis_size("col")
    values = tile_vals[0, 0]
    slots = values.shape[0]
    side = values.shape[1]
    nodes_here = features.shape[0]
    nbc = nodes_here // side
    width = features.shape[1]
    nrb = col_size * nbc
    ncb = row_size * nbc
    parity = lax.axis_index("row") % 2

    rowblk = jnp.clip(tile_rows[0, 0], 0, nrb - 1)
    colblk = jnp.clip(tile_cols[0, 0], 0, ncb - 1)
    cnt = jnp.clip(tile_count[0, 0], 0, slots).reshape(1).astype(jnp.int32)

    nb = _nbits(col_size)
    if nb is not None:
        rs_order, ag_order = _orders(nb)
        dest = rowblk // nbc
        sub = rowblk % nbc
        rs_pos = jnp.zeros_like(dest)
        ag_pos = jnp.zeros_like(dest)
        for t in range(nb):
            rs_pos = rs_pos + (((dest >> _pick(parity, rs_order, t)) & 1) << (nb - 1 - t))
            ag_pos = ag_pos + (((dest >> _pick(parity, ag_order, t)) & 1) << t)
        rows_fwd = rs_pos * nbc + sub
        rows_bwd = ag_pos * nbc + sub
    else:
        rows_fwd = rowblk
        rows_bwd = rowblk

    group = gather_row(features).reshape(ncb, side, width)
    fwd_parts = along_call(rows_fwd, colblk, cnt, values, group, nrb)

    mine_t = jnp.transpose(features.reshape(nbc, side, width), (0, 2, 1))
    if nb is not None:
        stripe_t = gather_col(mine_t, ag_order).reshape(nrb, width, side)
        along = scatter_sum_col(fwd_parts.reshape((2,) * nb + (nbc, side, width)), rs_order)
    else:
        stripe_t = lax.all_gather(mine_t, "col", axis=0, tiled=True)
        along = lax.psum_scatter(fwd_parts, "col", scatter_dimension=0, tiled=True)

    bwd_t = against_call(rows_bwd, colblk, cnt, values, stripe_t, ncb)
    against_t = scatter_sum_row(bwd_t)
    against = jnp.transpose(against_t, (0, 2, 1))

    along = along.reshape(-1, width)
    against = against.reshape(-1, width)
    result = jnp.dot(along, w_fwd.astype(jnp.float32), precision=lax.Precision.HIGHEST)
    result = result + jnp.dot(against, w_bwd.astype(jnp.float32), precision=lax.Precision.HIGHEST)
    return result.astype(jnp.bfloat16)


def solution(mesh):
    in_specs = (
        P(("row", "col"), None),
        P("row", "col", None, None, None),
        P("row", "col", None),
        P("row", "col", None),
        P("row", "col"),
        P(),
        P(),
    )
    out_specs = P(("row", "col"), None)
    return jax.shard_map(local, mesh=mesh, in_specs=in_specs, out_specs=out_specs, check_vma=False)
```
